32 devices in a mesh: group: 4 (over z), member: 8 (over y, x, core).
Axes of the slice: x: 2, y: 2, z: 4, core: 2. Of those that a mesh axis runs over, the one named last changes fastest.
Arguments:
- object_field: bfloat16 [2, 2, 2048, 4096], P(None, None, 'group', 'member'), may hold values from -4 to 4
- probe_modes: float32 [4, 2, 2, 128, 128], P('group'), may hold values from -7.2 to 7.2
- prop_phase: float32 [128, 128], replicated, may hold values from -3.140625 to 3.140625
- amplitude: float32 [4, 128, 128, 128], P('group', 'member'), may hold values from 0.5 to 4
- tile_owner: int32 [4, 128, 1], P('group', 'member'), may hold values from 0 to 7; in each aligned block of 16 rows (0 to 15, 16 to 31, ..., all dimensions but the last counted through in order) at most 4 rows name the same one
- corner: int32 [4, 128, 2], P('group', 'member'), may hold values from 0 to 384
Outputs:
- object_grad: float32 [2, 2, 2048, 4096], P(None, None, 'group', 'member')
- probe_grad: float32 [4, 2, 2, 128, 128], P('group')
The draws below stay inside these ranges and needn't reach their ends.
Inputs may be any that keep to these rules, and one draw needn't show every extreme that they name: `tile_owner`: among the positions of one device at most 4 name the same tile column.
All inputs are finite; a program needn't handle non-finite values.
Results may differ from the reference program's by a relative error of at most 0.0003.
Values may be sent and summed in bfloat16 or wider, within the bound.
No kernel may reach another device: no remote copies, remote signals or barrier semaphores. Data moves between devices by JAX's collectives and lax.ppermute only.
A program may use at most 128 MiB of HBM per device.

```python
import math
import jax
import jax.numpy as jnp
import numpy as np
from jax import lax

P_SIZE = 128
MODES = 2
SLICES = 2
TILE = 512
POS_DEV = 16
GROUPS = 4
POSITIONS = 128
CAP = 4
ROWS = 2048
COLS = 4096
N_MEMBER = 8


def draw_probe_modes(key, part):
    array_shape = (GROUPS, MODES, 2, P_SIZE, P_SIZE)
    growth = jnp.arange(GROUPS, dtype=jnp.float32) / max(GROUPS - 1, 1)
    values = jnp.clip(jax.random.normal(key, array_shape, jnp.float32), -4.0, 4.0)
    spread = 0.6 + 1.2 * growth
    return values * spread[:, None, None, None, None]


def place_ends(array, own_key, least, high):
    extent = array.shape
    index_at = [jax.random.randint(jax.random.fold_in(own_key, axis), (), 0, extent[axis]) for axis in range(len(extent))]
    array = array.at[tuple(index_at)].set(least)
    longest = extent.index(max(extent))
    index_at[longest] = (index_at[longest] + 1) % extent[longest]
    return array.at[tuple(index_at)].set(high)


def steps_of(rng, shape, cuts, least, high):
    def one(axis_at, shards_of):
        heights = jax.random.uniform(jax.random.fold_in(jax.random.fold_in(rng, 6), axis_at), (shards_of,), jnp.float32, least / len(cuts), high / len(cuts))
        return jnp.repeat(jnp.exp(heights), shape[axis_at] // shards_of).reshape((-1,) + (1,) * (len(shape) - axis_at - 1))

    factor_of = one(*cuts[0])
    for cut in cuts[1:]:
        factor_of = factor_of * one(*cut)
    return factor_of


def routed_block(stream_key, own, number, rows, count, top, reach, lean):
    order = jax.random.permutation(stream_key, count)
    crowded, usual = portions_of(count, rows * top, reach, lean, True), portions_of(count, rows * top, reach, lean, False)
    places = jnp.arange(count)

    def named(lengths, offset_by):
        used = int((lengths > 0).sum())
        fixed = max(1, used // 4)
        shifted = fixed + (places - fixed + offset_by * (used - fixed)) % max(1, count - fixed)
        return jnp.zeros((count,), jnp.int32).at[order[jnp.where(places < fixed, places, shifted)]].set(jnp.asarray(lengths, jnp.int32))

    lengths = jnp.where(number % 4 == 0, named(crowded, number // 4), named(usual, number - number // 4 - 1))
    mixed = jax.random.permutation(jax.random.fold_in(own, 3), count)
    source_of, receiver = mixed[0:count // 2 * 2:2], mixed[1:count // 2 * 2:2]
    room = jnp.minimum(lengths[source_of] - 1, reach - lengths[receiver]) // 2
    room = jnp.where((source_of == order[0]) | (receiver == order[0]) | (lengths[receiver] == 0), 0, jnp.maximum(room, 0))
    shifted = jax.random.randint(jax.random.fold_in(own, 4), (count // 2,), 0, 1 << 20) % (room + 1)
    lengths = lengths.at[source_of].add(-shifted).at[receiver].add(shifted)
    items = jnp.searchsorted(jnp.cumsum(lengths), jnp.arange(rows * top), side="right").astype(jnp.int32)
    listing = items.reshape(top, rows).T
    listing = listing[jax.random.permutation(jax.random.fold_in(own, 1), rows)]
    offset_by = jax.random.randint(jax.random.fold_in(own, 2), (rows, 1), 0, top)
    return jnp.take_along_axis(listing, (jnp.arange(top)[None, :] + offset_by) % top, axis=1)


def portions_of(amount, total, reach, lean, full):
    weights = [(1 << 20) // math.isqrt(standing ** lean) + 1 for standing in range(1, amount + 1)]
    largest = reach if full else min(reach, max(-(-total // amount), total * weights[0] // sum(weights)))
    least = 1 if total - largest >= amount - 1 else 0
    given, rest = [largest] + [least] * (amount - 1), total - largest - least * (amount - 1)
    while rest > 0:
        candidates = [i for i in range(1, amount) if given[i] < largest] or [i for i in range(1, amount) if given[i] < reach]
        mass, left = sum([weights[i] for i in candidates]), rest
        for i in candidates:
            more = min(reach - given[i], max(1, left * weights[i] // mass), rest)
            given[i] = given[i] + more
            rest = rest - more
    return np.array(given)


def noise(stream_key, dims, width, most, cuts=(), kind=jnp.bfloat16):
    entries = width * jax.random.normal(stream_key, dims, jnp.float32)
    if cuts:
        entries = entries * steps_of(stream_key, dims, cuts, -0.22, 0.18)
    return jnp.clip(entries, -most, most).astype(kind)


def setup_inputs(seed: int = 0) -> dict:
    arg_keys = jax.random.split(jax.random.key(seed), 7)
    object_field = noise(arg_keys[0], (SLICES, 2, ROWS, COLS), 0.7, 4.0, ((2, 4), (3, 8)))
    probe_modes = draw_probe_modes(jax.random.fold_in(arg_keys[6], 71), 0)
    prop_phase = jnp.clip(jax.random.uniform(arg_keys[2], (P_SIZE, P_SIZE), jnp.float32, -3.140625, 3.140625), -3.140625, 3.140625)
    amplitude = jnp.clip(0.5 + 3.5 * jax.random.uniform(arg_keys[3], (GROUPS, POSITIONS, P_SIZE, P_SIZE), jnp.float32) ** steps_of(arg_keys[3], (GROUPS, POSITIONS, P_SIZE, P_SIZE), ((0, 4), (1, 8)), -0.2, 0.2), 0.5, 4.0)
    tile_owner_keys = jax.random.split(jax.random.fold_in(arg_keys[4], 1), GROUPS * POSITIONS // POS_DEV)
    tile_owner_turns = jax.random.permutation(jax.random.fold_in(arg_keys[4], 3), GROUPS * POSITIONS // POS_DEV)
    tile_owner = jax.vmap(lambda own, number: routed_block(jax.random.fold_in(arg_keys[4], 2), own, number, POS_DEV, N_MEMBER, 1, CAP, 2))(tile_owner_keys, tile_owner_turns).reshape((GROUPS, POSITIONS, 1))
    corner = place_ends(jax.random.randint(arg_keys[5], (GROUPS, POSITIONS, 2), 0, TILE - P_SIZE + 1), jax.random.fold_in(arg_keys[5], 1), 0, TILE - P_SIZE).astype(jnp.int32)
    return {"object_field": object_field, "probe_modes": probe_modes, "prop_phase": prop_phase, "amplitude": amplitude, "tile_owner": tile_owner, "corner": corner}


def complex_of(pair):
    return lax.complex(pair[..., 0, :, :], pair[..., 1, :, :])

def pair_of(value):
    return jnp.stack([jnp.real(value), jnp.imag(value)], axis=-3)

def forward_transform(value):
    return jnp.fft.fft2(value, norm='ortho')

def inverse_transform(value):
    return jnp.fft.ifft2(value, norm='ortho')

def reference(object_field, probe_modes, prop_phase, amplitude, tile_owner, corner):
    kernel = lax.complex(jnp.cos(prop_phase), jnp.sin(prop_phase))
    power = lax.optimization_barrier(jnp.sum(probe_modes * probe_modes, axis=(1, 2)))
    peak_power = jnp.max(power) + 1e-06
    group_ids = jnp.repeat(jnp.arange(GROUPS, dtype=jnp.int32), POSITIONS)
    owners_all = tile_owner.reshape(GROUPS * POSITIONS).astype(jnp.int32)
    corners_all = corner.reshape(GROUPS * POSITIONS, 2).astype(jnp.int32)
    measured_all = amplitude.reshape(GROUPS * POSITIONS, P_SIZE, P_SIZE)
    anchor = jnp.zeros((), jnp.int32)

    def visit(carry, inputs):
        object_grad, probe_grad = carry
        group_id, owner_id, corner_pair, measured = inputs
        row_at = (group_id * TILE + corner_pair[0]).astype(jnp.int32)
        column = (owner_id * TILE + corner_pair[1]).astype(jnp.int32)
        patch = lax.dynamic_slice(object_field, (anchor, anchor, row_at, column), (SLICES, 2, P_SIZE, P_SIZE)).astype(jnp.float32)
        layers = complex_of(patch)
        wavefield = complex_of(lax.dynamic_index_in_dim(probe_modes, group_id, 0, keepdims=False))
        wavefields = []
        leaving = wavefield
        for layer in range(SLICES):
            wavefields.append(wavefield)
            leaving = wavefield * layers[layer]
            if layer < SLICES - 1:
                wavefield = inverse_transform(kernel * forward_transform(leaving))
        farfield = forward_transform(leaving)
        intensity = lax.optimization_barrier(jnp.sum(jnp.real(farfield) * jnp.real(farfield) + jnp.imag(farfield) * jnp.imag(farfield), axis=0))
        modelled = jnp.sqrt(jnp.maximum(intensity, 1.0))
        adjoint = inverse_transform(farfield * (1.0 - measured / modelled))
        gradients = [None] * SLICES
        for layer in reversed(range(SLICES)):
            gradients[layer] = lax.optimization_barrier(jnp.sum(jnp.conj(wavefields[layer]) * adjoint, axis=0))
            adjoint = jnp.conj(layers[layer]) * adjoint
            if layer > 0:
                adjoint = inverse_transform(jnp.conj(kernel) * forward_transform(adjoint))
        patch_grad = pair_of(jnp.stack(gradients))
        window = lax.dynamic_slice(object_grad, (anchor, anchor, row_at, column), (SLICES, 2, P_SIZE, P_SIZE))
        object_grad = lax.dynamic_update_slice(object_grad, window + patch_grad, (anchor, anchor, row_at, column))
        probe_grad = probe_grad.at[group_id].add(pair_of(adjoint) / POS_DEV)
        return ((object_grad, probe_grad), None)
    start = (jnp.zeros((SLICES, 2, ROWS, COLS), jnp.float32), jnp.zeros((GROUPS, MODES, 2, P_SIZE, P_SIZE), jnp.float32))
    (object_grad, probe_grad), unused = lax.scan(visit, start, (group_ids, owners_all, corners_all, measured_all))
    return (object_grad / peak_power, probe_grad)
```

```python
from functools import partial
import math

import jax
import jax.numpy as jnp
from jax import lax
from jax.sharding import PartitionSpec as P

HIGHEST_PRECISION = lax.Precision.HIGHEST


def fourier_blocks(length, sign):
    counter = jnp.arange(length, dtype=jnp.int32)
    product = counter[:, None] * counter[None, :] % length
    angles = product.astype(jnp.float32) * (2.0 * math.pi / length)
    norming = 1.0 / math.sqrt(length)
    cosine = jnp.cos(angles) * norming
    sine_part = jnp.sin(angles) * (sign * norming)
    return jnp.stack([jnp.stack([cosine, sine_part]), jnp.stack([-sine_part, cosine])])


def transform(field, blocks):
    across = jnp.einsum("...chn,cdnk->...dhk", field, blocks, precision=HIGHEST_PRECISION)
    return jnp.einsum("cdkn,...cnw->...dkw", blocks, across, precision=HIGHEST_PRECISION)


def complex_times(left, right):
    left_re, left_im = (left[..., 0, :, :], left[..., 1, :, :])
    right_re, right_im = (right[..., 0, :, :], right[..., 1, :, :])
    return jnp.stack(
        [left_re * right_re - left_im * right_im, left_re * right_im + left_im * right_re], axis=-3
    )


def conj_times(left, right):
    left_re, left_im = (left[..., 0, :, :], left[..., 1, :, :])
    right_re, right_im = (right[..., 0, :, :], right[..., 1, :, :])
    return jnp.stack(
        [left_re * right_re + left_im * right_im, left_re * right_im - left_im * right_re], axis=-3
    )


def slot_numbers(targets, members, capacity):
    matches = (targets[:, None] == jnp.arange(members, dtype=jnp.int32)[None, :]).astype(jnp.int32)
    before = jnp.cumsum(matches, axis=0) - matches
    return targets * capacity + jnp.sum(before * matches, axis=1)


def selectors(offsets, patch_side, tile_cells, dtype):
    inner = jnp.arange(patch_side, dtype=jnp.int32)
    cells = jnp.arange(tile_cells, dtype=jnp.int32)
    hit = offsets[:, None, None] + inner[None, :, None] == cells[None, None, :]
    return hit.astype(dtype)


def cut_windows(tiles, requests, patch_side):
    tile_cells = tiles.shape[-1]
    valid = requests[:, 0].astype(jnp.bfloat16)
    row_sel = selectors(requests[:, 1], patch_side, tile_cells, jnp.bfloat16) * valid[:, None, None]
    col_sel = selectors(requests[:, 2], patch_side, tile_cells, jnp.bfloat16)
    rows = jnp.einsum("kit,sctu->kscui", row_sel, tiles, preferred_element_type=jnp.float32)
    rows = rows.astype(jnp.bfloat16)
    window = jnp.einsum("kscui,kju->kscij", rows, col_sel, preferred_element_type=jnp.float32)
    return window.astype(jnp.bfloat16)


def accumulate(terms, requests, tile_cells):
    patch_side = terms.shape[-1]
    high = lax.reduce_precision(terms, exponent_bits=8, mantissa_bits=7)
    low = terms - high
    parts = jnp.concatenate([high, low], axis=0).astype(jnp.bfloat16)
    doubled = jnp.concatenate([requests, requests], axis=0)
    row_sel = selectors(doubled[:, 1], patch_side, tile_cells, jnp.bfloat16)
    col_sel = selectors(doubled[:, 2], patch_side, tile_cells, jnp.bfloat16)
    widened = jnp.einsum("kscij,kju->kiscu", parts, col_sel,
                         preferred_element_type=jnp.float32).astype(jnp.bfloat16)
    return jnp.einsum("kit,kiscu->sctu", row_sel, widened, preferred_element_type=jnp.float32)


def on_device(object_field, probe_modes, prop_phase, amplitude, tile_owner, corner):
    members = lax.axis_size("member")
    pos_dev = tile_owner.shape[1]
    capacity = max(2, (2 * pos_dev + members - 1) // members)
    slot_count = members * capacity
    slice_count = object_field.shape[0]
    tile_cells = object_field.shape[2]
    patch_side = prop_phase.shape[0]
    modes = probe_modes.shape[1]
    flat_slots = slot_numbers(tile_owner[0, :, 0], members, capacity)
    entries = jnp.concatenate([jnp.ones((pos_dev, 1), jnp.int32), corner[0]], axis=1)
    chosen = (flat_slots[:, None] == jnp.arange(slot_count, dtype=jnp.int32)[None, :]).astype(
        jnp.int32
    )
    outgoing = jnp.sum(chosen[:, :, None] * entries[:, None, :], axis=0)
    requests = lax.all_to_all(
        outgoing.reshape(members, capacity, 3), "member", split_axis=0, concat_axis=0, tiled=True
    ).reshape(slot_count, 3)
    extent = (slice_count, 2, patch_side, patch_side)
    pieces = cut_windows(object_field, requests, patch_side)
    arrived = lax.all_to_all(
        pieces.reshape((members, capacity) + extent),
        "member",
        split_axis=0,
        concat_axis=0,
        tiled=True,
    )
    arrived = arrived.reshape((slot_count,) + extent)[flat_slots]
    layers = [arrived[:, layer] for layer in range(slice_count)]
    forward_blocks = fourier_blocks(patch_side, -1.0)
    inverse_blocks = fourier_blocks(patch_side, 1.0)
    kernel = jnp.stack([jnp.cos(prop_phase), jnp.sin(prop_phase)])
    wavefield = jnp.broadcast_to(probe_modes, (pos_dev, modes, 2, patch_side, patch_side))
    transmit = [layer_patch.astype(jnp.float32)[:, None] for layer_patch in layers]
    wavefields = []
    leaving = wavefield
    for layer in range(slice_count):
        wavefields.append(wavefield)
        leaving = complex_times(wavefield, transmit[layer])
        if layer < slice_count - 1:
            wavefield = transform(
                complex_times(kernel, transform(leaving, forward_blocks)), inverse_blocks
            )
    farfield = transform(leaving, forward_blocks)
    intensity = jnp.sum(farfield * farfield, axis=(1, 2))
    factor = 1.0 - amplitude[0] / jnp.sqrt(jnp.maximum(intensity, 1.0))
    adjoint = transform(farfield * factor[:, None, None], inverse_blocks)
    gradients = [None] * slice_count
    for layer in reversed(range(slice_count)):
        gradients[layer] = jnp.sum(conj_times(wavefields[layer], adjoint), axis=1)
        adjoint = conj_times(transmit[layer], adjoint)
        if layer > 0:
            adjoint = transform(
                conj_times(kernel, transform(adjoint, forward_blocks)), inverse_blocks
            )
    local_probe = jnp.sum(adjoint, axis=0) / pos_dev
    probe_grad = lax.psum(local_probe, "member")[None]
    power = jnp.max(jnp.sum(probe_modes * probe_modes, axis=(1, 2)))
    peak_power = lax.pmax(power, "group") + 1e-06
    stacked = jnp.stack(gradients, axis=1)
    piece_shape = stacked.shape[1:]
    outgoing = jnp.zeros((slot_count,) + piece_shape, jnp.float32).at[flat_slots].set(stacked)
    returned = lax.all_to_all(
        outgoing.reshape((members, capacity) + piece_shape),
        "member",
        split_axis=0,
        concat_axis=0,
        tiled=True,
    )
    summed = accumulate(returned.reshape((slot_count,) + piece_shape), requests, tile_cells)
    return (summed / peak_power, probe_grad)


def solution(mesh):
    return jax.shard_map(
        on_device,
        mesh=mesh,
        in_specs=(
            P(None, None, "group", "member"),
            P("group", None, None, None, None),
            P(),
            P("group", "member", None, None),
            P("group", "member", None),
            P("group", "member", None),
        ),
        out_specs=(P(None, None, "group", "member"), P("group", None, None, None, None)),
        check_vma=False,
    )
```

```python
from functools import partial
import math

import jax
import jax.numpy as jnp
from jax import lax
from jax.sharding import PartitionSpec as P

HIGHEST_PRECISION = lax.Precision.HIGHEST


def fourier_blocks(length, sign):
    counter = jnp.arange(length, dtype=jnp.int32)
    product = counter[:, None] * counter[None, :] % length
    angles = product.astype(jnp.float32) * (2.0 * math.pi / length)
    norming = 1.0 / math.sqrt(length)
    cosine = jnp.cos(angles) * norming
    sine_part = jnp.sin(angles) * (sign * norming)
    return jnp.stack([jnp.stack([cosine, sine_part]), jnp.stack([-sine_part, cosine])])


def transform(field, blocks):
    across = jnp.einsum("...chn,cdnk->...dhk", field, blocks, precision=HIGHEST_PRECISION)
    return jnp.einsum("cdkn,...cnw->...dkw", blocks, across, precision=HIGHEST_PRECISION)


def complex_times(left, right):
    left_re, left_im = (left[..., 0, :, :], left[..., 1, :, :])
    right_re, right_im = (right[..., 0, :, :], right[..., 1, :, :])
    return jnp.stack(
        [left_re * right_re - left_im * right_im, left_re * right_im + left_im * right_re], axis=-3
    )


def conj_times(left, right):
    left_re, left_im = (left[..., 0, :, :], left[..., 1, :, :])
    right_re, right_im = (right[..., 0, :, :], right[..., 1, :, :])
    return jnp.stack(
        [left_re * right_re + left_im * right_im, left_re * right_im - left_im * right_re], axis=-3
    )


def slot_numbers(targets, members, capacity):
    matches = (targets[:, None] == jnp.arange(members, dtype=jnp.int32)[None, :]).astype(jnp.int32)
    before = jnp.cumsum(matches, axis=0) - matches
    return targets * capacity + jnp.sum(before * matches, axis=1)


def selectors(offsets, patch_side, tile_cells, dtype):
    inner = jnp.arange(patch_side, dtype=jnp.int32)
    cells = jnp.arange(tile_cells, dtype=jnp.int32)
    hit = offsets[:, None, None] + inner[None, :, None] == cells[None, None, :]
    return hit.astype(dtype)


def cut_windows(tiles, requests, patch_side):
    tile_cells = tiles.shape[-1]
    valid = requests[:, 0].astype(jnp.bfloat16)
    row_sel = selectors(requests[:, 1], patch_side, tile_cells, jnp.bfloat16) * valid[:, None, None]
    col_sel = selectors(requests[:, 2], patch_side, tile_cells, jnp.bfloat16)
    rows = jnp.einsum("kit,sctu->kscui", row_sel, tiles, preferred_element_type=jnp.float32)
    rows = rows.astype(jnp.bfloat16)
    window = jnp.einsum("kscui,kju->kscij", rows, col_sel, preferred_element_type=jnp.float32)
    return window.astype(jnp.bfloat16)


def accumulate(terms, requests, tile_cells):
    patch_side = terms.shape[-1]
    high = lax.reduce_precision(terms, exponent_bits=8, mantissa_bits=7)
    low = terms - high
    parts = jnp.concatenate([high, low], axis=0).astype(jnp.bfloat16)
    doubled = jnp.concatenate([requests, requests], axis=0)
    row_sel = selectors(doubled[:, 1], patch_side, tile_cells, jnp.bfloat16)
    col_sel = selectors(doubled[:, 2], patch_side, tile_cells, jnp.bfloat16)
    widened = jnp.einsum("kscij,kju->kiscu", parts, col_sel,
                         preferred_element_type=jnp.float32).astype(jnp.bfloat16)
    return jnp.einsum("kit,kiscu->sctu", row_sel, widened, preferred_element_type=jnp.float32)


def propagate(patches, measured, probe_modes, kernel, forward_blocks, inverse_blocks):
    count = patches.shape[0]
    slice_count = patches.shape[1]
    modes = probe_modes.shape[1]
    patch_side = patches.shape[-1]
    wavefield = jnp.broadcast_to(probe_modes, (count, modes, 2, patch_side, patch_side))
    transmit = [patches[:, layer].astype(jnp.float32)[:, None] for layer in range(slice_count)]
    wavefields = []
    leaving = wavefield
    for layer in range(slice_count):
        wavefields.append(wavefield)
        leaving = complex_times(wavefield, transmit[layer])
        if layer < slice_count - 1:
            wavefield = transform(
                complex_times(kernel, transform(leaving, forward_blocks)), inverse_blocks
            )
    farfield = transform(leaving, forward_blocks)
    intensity = jnp.sum(farfield * farfield, axis=(1, 2))
    factor = 1.0 - measured / jnp.sqrt(jnp.maximum(intensity, 1.0))
    adjoint = transform(farfield * factor[:, None, None], inverse_blocks)
    gradients = [None] * slice_count
    for layer in reversed(range(slice_count)):
        gradients[layer] = jnp.sum(conj_times(wavefields[layer], adjoint), axis=1)
        adjoint = conj_times(transmit[layer], adjoint)
        if layer > 0:
            adjoint = transform(
                conj_times(kernel, transform(adjoint, forward_blocks)), inverse_blocks
            )
    return jnp.stack(gradients, axis=1), jnp.sum(adjoint, axis=0)


def on_device(object_field, probe_modes, prop_phase, amplitude, tile_owner, corner):
    members = lax.axis_size("member")
    pos_dev = tile_owner.shape[1]
    capacity = max(2, (2 * pos_dev + members - 1) // members)
    slot_count = members * capacity
    tile_cells = object_field.shape[2]
    patch_side = prop_phase.shape[0]
    power = jnp.max(jnp.sum(probe_modes * probe_modes, axis=(1, 2)))
    powers = lax.all_gather(power[None], "group", tiled=True)
    peak_power = jnp.max(powers) + 1e-06
    flat_slots = slot_numbers(tile_owner[0, :, 0], members, capacity)
    entries = jnp.concatenate([jnp.ones((pos_dev, 1), jnp.int32), corner[0]], axis=1)
    chosen = (flat_slots[:, None] == jnp.arange(slot_count, dtype=jnp.int32)[None, :]).astype(
        jnp.int32
    )
    outgoing = jnp.sum(chosen[:, :, None] * entries[:, None, :], axis=0)
    requests = lax.all_to_all(
        outgoing.reshape(members, capacity, 3), "member", split_axis=0, concat_axis=0, tiled=True
    ).reshape(slot_count, 3)
    sent = jnp.zeros((slot_count, patch_side, patch_side), jnp.float32).at[flat_slots].set(
        amplitude[0]
    )
    measured = lax.all_to_all(
        sent.reshape(members, capacity, patch_side, patch_side),
        "member",
        split_axis=0,
        concat_axis=0,
        tiled=True,
    ).reshape(slot_count, patch_side, patch_side)
    patches = cut_windows(object_field, requests, patch_side)
    forward_blocks = fourier_blocks(patch_side, -1.0)
    inverse_blocks = fourier_blocks(patch_side, 1.0)
    kernel = jnp.stack([jnp.cos(prop_phase), jnp.sin(prop_phase)])
    chunk = math.gcd(slot_count, 32)
    chunks = slot_count // chunk
    work = partial(
        propagate,
        probe_modes=probe_modes,
        kernel=kernel,
        forward_blocks=forward_blocks,
        inverse_blocks=inverse_blocks,
    )
    if chunks == 1:
        gradients, adjoint_sum = work(patches, measured)
    else:
        gradients, adjoint_sums = lax.map(
            lambda pair: work(*pair),
            (
                patches.reshape((chunks, chunk) + patches.shape[1:]),
                measured.reshape(chunks, chunk, patch_side, patch_side),
            ),
        )
        gradients = gradients.reshape((slot_count,) + gradients.shape[2:])
        adjoint_sum = jnp.sum(adjoint_sums, axis=0)
    probe_grad = lax.psum(adjoint_sum / pos_dev, "member")[None]
    summed = accumulate(gradients, requests, tile_cells)
    return (summed / peak_power, probe_grad)


def solution(mesh):
    return jax.shard_map(
        on_device,
        mesh=mesh,
        in_specs=(
            P(None, None, "group", "member"),
            P("group", None, None, None, None),
            P(),
            P("group", "member", None, None),
            P("group", "member", None),
            P("group", "member", None),
        ),
        out_specs=(P(None, None, "group", "member"), P("group", None, None, None, None)),
        check_vma=False,
    )
```

```python
from functools import partial
import math

import jax
import jax.numpy as jnp
from jax import lax
from jax.sharding import PartitionSpec as P

DFT_PRECISION = lax.Precision.HIGH


def fourier_blocks(length, sign):
    counter = jnp.arange(length, dtype=jnp.int32)
    product = counter[:, None] * counter[None, :] % length
    angles = product.astype(jnp.float32) * (2.0 * math.pi / length)
    norming = 1.0 / math.sqrt(length)
    cosine = jnp.cos(angles) * norming
    sine_part = jnp.sin(angles) * (sign * norming)
    return jnp.stack([jnp.stack([cosine, sine_part]), jnp.stack([-sine_part, cosine])])


def transform(field, blocks):
    across = jnp.einsum("...chn,cdnk->...dhk", field, blocks, precision=DFT_PRECISION)
    return jnp.einsum("cdkn,...cnw->...dkw", blocks, across, precision=DFT_PRECISION)


def complex_times(left, right):
    left_re, left_im = (left[..., 0, :, :], left[..., 1, :, :])
    right_re, right_im = (right[..., 0, :, :], right[..., 1, :, :])
    return jnp.stack(
        [left_re * right_re - left_im * right_im, left_re * right_im + left_im * right_re], axis=-3
    )


def conj_times(left, right):
    left_re, left_im = (left[..., 0, :, :], left[..., 1, :, :])
    right_re, right_im = (right[..., 0, :, :], right[..., 1, :, :])
    return jnp.stack(
        [left_re * right_re + left_im * right_im, left_re * right_im - left_im * right_re], axis=-3
    )


def slot_numbers(targets, members, capacity):
    matches = (targets[:, None] == jnp.arange(members, dtype=jnp.int32)[None, :]).astype(jnp.int32)
    before = jnp.cumsum(matches, axis=0) - matches
    return targets * capacity + jnp.sum(before * matches, axis=1)


def selectors(offsets, patch_side, tile_cells, dtype):
    inner = jnp.arange(patch_side, dtype=jnp.int32)
    cells = jnp.arange(tile_cells, dtype=jnp.int32)
    hit = offsets[:, None, None] + inner[None, :, None] == cells[None, None, :]
    return hit.astype(dtype)


def cut_windows(tiles, requests, patch_side):
    tile_cells = tiles.shape[-1]
    valid = requests[:, 0].astype(jnp.bfloat16)
    row_sel = selectors(requests[:, 1], patch_side, tile_cells, jnp.bfloat16) * valid[:, None, None]
    col_sel = selectors(requests[:, 2], patch_side, tile_cells, jnp.bfloat16)
    rows = jnp.einsum("kit,sctu->kscui", row_sel, tiles, preferred_element_type=jnp.float32)
    rows = rows.astype(jnp.bfloat16)
    window = jnp.einsum("kscui,kju->kscij", rows, col_sel, preferred_element_type=jnp.float32)
    return window.astype(jnp.bfloat16)


def accumulate(terms, requests, tile_cells):
    patch_side = terms.shape[-1]
    high = lax.reduce_precision(terms, exponent_bits=8, mantissa_bits=7)
    low = terms - high
    parts = jnp.concatenate([high, low], axis=0).astype(jnp.bfloat16)
    doubled = jnp.concatenate([requests, requests], axis=0)
    row_sel = selectors(doubled[:, 1], patch_side, tile_cells, jnp.bfloat16)
    col_sel = selectors(doubled[:, 2], patch_side, tile_cells, jnp.bfloat16)
    widened = jnp.einsum("kscij,kju->kiscu", parts, col_sel,
                         preferred_element_type=jnp.float32).astype(jnp.bfloat16)
    return jnp.einsum("kit,kiscu->sctu", row_sel, widened, preferred_element_type=jnp.float32)


def propagate(patches, measured, probe_modes, kernel, forward_blocks, inverse_blocks):
    count = patches.shape[0]
    slice_count = patches.shape[1]
    modes = probe_modes.shape[1]
    patch_side = patches.shape[-1]
    wavefield = jnp.broadcast_to(probe_modes, (count, modes, 2, patch_side, patch_side))
    transmit = [patches[:, layer].astype(jnp.float32)[:, None] for layer in range(slice_count)]
    wavefields = []
    leaving = wavefield
    for layer in range(slice_count):
        wavefields.append(wavefield)
        leaving = complex_times(wavefield, transmit[layer])
        if layer < slice_count - 1:
            wavefield = transform(
                complex_times(kernel, transform(leaving, forward_blocks)), inverse_blocks
            )
    farfield = transform(leaving, forward_blocks)
    intensity = jnp.sum(farfield * farfield, axis=(1, 2))
    factor = 1.0 - measured / jnp.sqrt(jnp.maximum(intensity, 1.0))
    adjoint = transform(farfield * factor[:, None, None], inverse_blocks)
    gradients = [None] * slice_count
    for layer in reversed(range(slice_count)):
        gradients[layer] = jnp.sum(conj_times(wavefields[layer], adjoint), axis=1)
        adjoint = conj_times(transmit[layer], adjoint)
        if layer > 0:
            adjoint = transform(
                conj_times(kernel, transform(adjoint, forward_blocks)), inverse_blocks
            )
    return jnp.stack(gradients, axis=1), jnp.sum(adjoint, axis=0)


def on_device(object_field, probe_modes, prop_phase, amplitude, tile_owner, corner):
    members = lax.axis_size("member")
    pos_dev = tile_owner.shape[1]
    capacity = max(2, (2 * pos_dev + members - 1) // members)
    slot_count = members * capacity
    tile_cells = object_field.shape[2]
    patch_side = prop_phase.shape[0]
    power = jnp.max(jnp.sum(probe_modes * probe_modes, axis=(1, 2)))
    powers = lax.all_gather(power[None], "group", tiled=True)
    peak_power = jnp.max(powers) + 1e-06
    flat_slots = slot_numbers(tile_owner[0, :, 0], members, capacity)
    entries = jnp.concatenate([jnp.ones((pos_dev, 1), jnp.int32), corner[0]], axis=1)
    chosen = (flat_slots[:, None] == jnp.arange(slot_count, dtype=jnp.int32)[None, :]).astype(
        jnp.int32
    )
    outgoing = jnp.sum(chosen[:, :, None] * entries[:, None, :], axis=0)
    requests = lax.all_to_all(
        outgoing.reshape(members, capacity, 3), "member", split_axis=0, concat_axis=0, tiled=True
    ).reshape(slot_count, 3)
    sent = jnp.zeros((slot_count, patch_side, patch_side), jnp.float32).at[flat_slots].set(
        amplitude[0]
    )
    measured = lax.all_to_all(
        sent.reshape(members, capacity, patch_side, patch_side),
        "member",
        split_axis=0,
        concat_axis=0,
        tiled=True,
    ).reshape(slot_count, patch_side, patch_side)
    patches = cut_windows(object_field, requests, patch_side)
    forward_blocks = fourier_blocks(patch_side, -1.0)
    inverse_blocks = fourier_blocks(patch_side, 1.0)
    kernel = jnp.stack([jnp.cos(prop_phase), jnp.sin(prop_phase)])
    chunk = math.gcd(slot_count, 32)
    chunks = slot_count // chunk
    work = partial(
        propagate,
        probe_modes=probe_modes,
        kernel=kernel,
        forward_blocks=forward_blocks,
        inverse_blocks=inverse_blocks,
    )
    if chunks == 1:
        gradients, adjoint_sum = work(patches, measured)
    else:
        gradients, adjoint_sums = lax.map(
            lambda pair: work(*pair),
            (
                patches.reshape((chunks, chunk) + patches.shape[1:]),
                measured.reshape(chunks, chunk, patch_side, patch_side),
            ),
        )
        gradients = gradients.reshape((slot_count,) + gradients.shape[2:])
        adjoint_sum = jnp.sum(adjoint_sums, axis=0)
    probe_grad = lax.psum(adjoint_sum / pos_dev, "member")[None]
    summed = accumulate(gradients, requests, tile_cells)
    return (summed / peak_power, probe_grad)


def solution(mesh):
    return jax.shard_map(
        on_device,
        mesh=mesh,
        in_specs=(
            P(None, None, "group", "member"),
            P("group", None, None, None, None),
            P(),
            P("group", "member", None, None),
            P("group", "member", None),
            P("group", "member", None),
        ),
        out_specs=(P(None, None, "group", "member"), P("group", None, None, None, None)),
        check_vma=False,
    )
```

```python
from functools import partial
import math

import jax
import jax.numpy as jnp
from jax import lax
from jax.experimental import pallas as pl
from jax.experimental.pallas import tpu as pltpu
from jax.sharding import PartitionSpec as P

DFT_PRECISION = lax.Precision.HIGH


def fourier_blocks(length, sign):
    counter = jnp.arange(length, dtype=jnp.int32)
    product = counter[:, None] * counter[None, :] % length
    angles = product.astype(jnp.float32) * (2.0 * math.pi / length)
    norming = 1.0 / math.sqrt(length)
    cosine = jnp.cos(angles) * norming
    sine_part = jnp.sin(angles) * (sign * norming)
    return jnp.stack([jnp.stack([cosine, sine_part]), jnp.stack([-sine_part, cosine])])


def transform(field, blocks):
    across = jnp.einsum("...chn,cdnk->...dhk", field, blocks, precision=DFT_PRECISION)
    return jnp.einsum("cdkn,...cnw->...dkw", blocks, across, precision=DFT_PRECISION)


def complex_times(left, right):
    left_re, left_im = (left[..., 0, :, :], left[..., 1, :, :])
    right_re, right_im = (right[..., 0, :, :], right[..., 1, :, :])
    return jnp.stack(
        [left_re * right_re - left_im * right_im, left_re * right_im + left_im * right_re], axis=-3
    )


def conj_times(left, right):
    left_re, left_im = (left[..., 0, :, :], left[..., 1, :, :])
    right_re, right_im = (right[..., 0, :, :], right[..., 1, :, :])
    return jnp.stack(
        [left_re * right_re + left_im * right_im, left_re * right_im - left_im * right_re], axis=-3
    )


def slot_numbers(targets, members, capacity):
    matches = (targets[:, None] == jnp.arange(members, dtype=jnp.int32)[None, :]).astype(jnp.int32)
    before = jnp.cumsum(matches, axis=0) - matches
    return targets * capacity + jnp.sum(before * matches, axis=1)


def selectors(offsets, patch_side, tile_cells, dtype):
    inner = jnp.arange(patch_side, dtype=jnp.int32)
    cells = jnp.arange(tile_cells, dtype=jnp.int32)
    hit = offsets[:, None, None] + inner[None, :, None] == cells[None, None, :]
    return hit.astype(dtype)


def cut_windows(tiles, requests, patch_side):
    tile_cells = tiles.shape[-1]
    valid = requests[:, 0].astype(jnp.bfloat16)
    row_sel = selectors(requests[:, 1], patch_side, tile_cells, jnp.bfloat16) * valid[:, None, None]
    col_sel = selectors(requests[:, 2], patch_side, tile_cells, jnp.bfloat16)
    rows = jnp.einsum("kit,sctu->kscui", row_sel, tiles, preferred_element_type=jnp.float32)
    rows = rows.astype(jnp.bfloat16)
    window = jnp.einsum("kscui,kju->kscij", rows, col_sel, preferred_element_type=jnp.float32)
    return window.astype(jnp.bfloat16)


def place_kernel(requests, terms, out, total):
    slot = pl.program_id(0)
    slice_count = terms.shape[1]
    patch_side = terms.shape[-1]
    tile_cells = out.shape[-1]

    @pl.when(slot == 0)
    def _():
        total[...] = jnp.zeros_like(total)

    row = requests[slot, 1]
    col = requests[slot, 2]
    row_base = pl.multiple_of((row // 8) * 8, 8)
    col_base = pl.multiple_of((col // 128) * 128, 128)
    row_rest = row - row_base
    col_rest = col - col_base
    band_rows = patch_side + 8
    band_cols = 2 * patch_side
    row_pick = (
        lax.broadcasted_iota(jnp.int32, (band_rows, patch_side), 0)
        == lax.broadcasted_iota(jnp.int32, (band_rows, patch_side), 1) + row_rest
    ).astype(jnp.bfloat16)
    col_pick = (
        lax.broadcasted_iota(jnp.int32, (patch_side, band_cols), 1)
        == lax.broadcasted_iota(jnp.int32, (patch_side, band_cols), 0) + col_rest
    ).astype(jnp.bfloat16)
    for layer in range(slice_count):
        for part in range(2):
            term = terms[0, layer, part]
            high = term.astype(jnp.bfloat16)
            low = (term - high.astype(jnp.float32)).astype(jnp.bfloat16)
            band = jnp.zeros((band_rows, band_cols), jnp.float32)
            for piece in (high, low):
                wide = jnp.dot(piece, col_pick, preferred_element_type=jnp.float32)
                band = band + jnp.dot(
                    row_pick, wide.astype(jnp.bfloat16), preferred_element_type=jnp.float32
                )
            window = total.at[layer, part, pl.ds(row_base, band_rows), pl.ds(col_base, band_cols)]
            window[...] = window[...] + band

    @pl.when(slot == pl.num_programs(0) - 1)
    def _():
        out[...] = total[:, :, :tile_cells, :tile_cells]


def accumulate(terms, requests, tile_cells):
    slot_count, slice_count = terms.shape[:2]
    patch_side = terms.shape[-1]
    grid_spec = pltpu.PrefetchScalarGridSpec(
        num_scalar_prefetch=1,
        grid=(slot_count,),
        in_specs=[
            pl.BlockSpec(
                (1, slice_count, 2, patch_side, patch_side), lambda k, req: (k, 0, 0, 0, 0)
            )
        ],
        out_specs=pl.BlockSpec(
            (slice_count, 2, tile_cells, tile_cells), lambda k, req: (0, 0, 0, 0)
        ),
        scratch_shapes=[
            pltpu.VMEM(
                (slice_count, 2, tile_cells + 8, tile_cells + patch_side), jnp.float32
            )
        ],
    )
    return pl.pallas_call(
        place_kernel,
        grid_spec=grid_spec,
        out_shape=jax.ShapeDtypeStruct((slice_count, 2, tile_cells, tile_cells), jnp.float32),
        compiler_params=pltpu.CompilerParams(dimension_semantics=("arbitrary",)),
    )(requests, terms)


def propagate(patches, measured, probe_modes, kernel, forward_blocks, inverse_blocks):
    count = patches.shape[0]
    slice_count = patches.shape[1]
    modes = probe_modes.shape[1]
    patch_side = patches.shape[-1]
    wavefield = jnp.broadcast_to(probe_modes, (count, modes, 2, patch_side, patch_side))
    transmit = [patches[:, layer].astype(jnp.float32)[:, None] for layer in range(slice_count)]
    wavefields = []
    leaving = wavefield
    for layer in range(slice_count):
        wavefields.append(wavefield)
        leaving = complex_times(wavefield, transmit[layer])
        if layer < slice_count - 1:
            wavefield = transform(
                complex_times(kernel, transform(leaving, forward_blocks)), inverse_blocks
            )
    farfield = transform(leaving, forward_blocks)
    intensity = jnp.sum(farfield * farfield, axis=(1, 2))
    factor = 1.0 - measured / jnp.sqrt(jnp.maximum(intensity, 1.0))
    adjoint = transform(farfield * factor[:, None, None], inverse_blocks)
    gradients = [None] * slice_count
    for layer in reversed(range(slice_count)):
        gradients[layer] = jnp.sum(conj_times(wavefields[layer], adjoint), axis=1)
        adjoint = conj_times(transmit[layer], adjoint)
        if layer > 0:
            adjoint = transform(
                conj_times(kernel, transform(adjoint, forward_blocks)), inverse_blocks
            )
    return jnp.stack(gradients, axis=1), jnp.sum(adjoint, axis=0)


def on_device(object_field, probe_modes, prop_phase, amplitude, tile_owner, corner):
    members = lax.axis_size("member")
    pos_dev = tile_owner.shape[1]
    capacity = max(2, (2 * pos_dev + members - 1) // members)
    slot_count = members * capacity
    tile_cells = object_field.shape[2]
    patch_side = prop_phase.shape[0]
    power = jnp.max(jnp.sum(probe_modes * probe_modes, axis=(1, 2)))
    powers = lax.all_gather(power[None], "group", tiled=True)
    peak_power = jnp.max(powers) + 1e-06
    flat_slots = slot_numbers(tile_owner[0, :, 0], members, capacity)
    entries = jnp.concatenate([jnp.ones((pos_dev, 1), jnp.int32), corner[0]], axis=1)
    chosen = (flat_slots[:, None] == jnp.arange(slot_count, dtype=jnp.int32)[None, :]).astype(
        jnp.int32
    )
    outgoing = jnp.sum(chosen[:, :, None] * entries[:, None, :], axis=0)
    requests = lax.all_to_all(
        outgoing.reshape(members, capacity, 3), "member", split_axis=0, concat_axis=0, tiled=True
    ).reshape(slot_count, 3)
    sent = jnp.zeros((slot_count, patch_side, patch_side), jnp.float32).at[flat_slots].set(
        amplitude[0]
    )
    measured = lax.all_to_all(
        sent.reshape(members, capacity, patch_side, patch_side),
        "member",
        split_axis=0,
        concat_axis=0,
        tiled=True,
    ).reshape(slot_count, patch_side, patch_side)
    patches = cut_windows(object_field, requests, patch_side)
    forward_blocks = fourier_blocks(patch_side, -1.0)
    inverse_blocks = fourier_blocks(patch_side, 1.0)
    kernel = jnp.stack([jnp.cos(prop_phase), jnp.sin(prop_phase)])
    chunk = math.gcd(slot_count, 32)
    chunks = slot_count // chunk
    work = partial(
        propagate,
        probe_modes=probe_modes,
        kernel=kernel,
        forward_blocks=forward_blocks,
        inverse_blocks=inverse_blocks,
    )
    if chunks == 1:
        gradients, adjoint_sum = work(patches, measured)
    else:
        gradients, adjoint_sums = lax.map(
            lambda pair: work(*pair),
            (
                patches.reshape((chunks, chunk) + patches.shape[1:]),
                measured.reshape(chunks, chunk, patch_side, patch_side),
            ),
        )
        gradients = gradients.reshape((slot_count,) + gradients.shape[2:])
        adjoint_sum = jnp.sum(adjoint_sums, axis=0)
    probe_grad = lax.psum(adjoint_sum / pos_dev, "member")[None]
    summed = accumulate(gradients, requests, tile_cells)
    return (summed / peak_power, probe_grad)


def solution(mesh):
    return jax.shard_map(
        on_device,
        mesh=mesh,
        in_specs=(
            P(None, None, "group", "member"),
            P("group", None, None, None, None),
            P(),
            P("group", "member", None, None),
            P("group", "member", None),
            P("group", "member", None),
        ),
        out_specs=(P(None, None, "group", "member"), P("group", None, None, None, None)),
        check_vma=False,
    )
```

```python
from functools import partial
import math

import jax
import jax.numpy as jnp
from jax import lax
from jax.experimental import pallas as pl
from jax.experimental.pallas import tpu as pltpu
from jax.sharding import PartitionSpec as P

DFT_PRECISION = lax.Precision.HIGH


def fourier_blocks(length, sign):
    counter = jnp.arange(length, dtype=jnp.int32)
    product = counter[:, None] * counter[None, :] % length
    angles = product.astype(jnp.float32) * (2.0 * math.pi / length)
    norming = 1.0 / math.sqrt(length)
    cosine = jnp.cos(angles) * norming
    sine_part = jnp.sin(angles) * (sign * norming)
    return jnp.stack([jnp.stack([cosine, sine_part]), jnp.stack([-sine_part, cosine])])


def transform(field, blocks):
    across = jnp.einsum("...chn,cdnk->...dhk", field, blocks, precision=DFT_PRECISION)
    return jnp.einsum("cdkn,...cnw->...dkw", blocks, across, precision=DFT_PRECISION)


def complex_times(left, right):
    left_re, left_im = (left[..., 0, :, :], left[..., 1, :, :])
    right_re, right_im = (right[..., 0, :, :], right[..., 1, :, :])
    return jnp.stack(
        [left_re * right_re - left_im * right_im, left_re * right_im + left_im * right_re], axis=-3
    )


def conj_times(left, right):
    left_re, left_im = (left[..., 0, :, :], left[..., 1, :, :])
    right_re, right_im = (right[..., 0, :, :], right[..., 1, :, :])
    return jnp.stack(
        [left_re * right_re + left_im * right_im, left_re * right_im - left_im * right_re], axis=-3
    )


def slot_numbers(targets, members, capacity):
    matches = (targets[:, None] == jnp.arange(members, dtype=jnp.int32)[None, :]).astype(jnp.int32)
    before = jnp.cumsum(matches, axis=0) - matches
    return targets * capacity + jnp.sum(before * matches, axis=1)


def selectors(offsets, patch_side, tile_cells, dtype):
    inner = jnp.arange(patch_side, dtype=jnp.int32)
    cells = jnp.arange(tile_cells, dtype=jnp.int32)
    hit = offsets[:, None, None] + inner[None, :, None] == cells[None, None, :]
    return hit.astype(dtype)


def cut_windows(tiles, requests, patch_side):
    tile_cells = tiles.shape[-1]
    valid = requests[:, 0].astype(jnp.bfloat16)
    row_sel = selectors(requests[:, 1], patch_side, tile_cells, jnp.bfloat16) * valid[:, None, None]
    col_sel = selectors(requests[:, 2], patch_side, tile_cells, jnp.bfloat16)
    rows = jnp.einsum("kit,sctu->kscui", row_sel, tiles, preferred_element_type=jnp.float32)
    rows = rows.astype(jnp.bfloat16)
    window = jnp.einsum("kscui,kju->kscij", rows, col_sel, preferred_element_type=jnp.float32)
    return window.astype(jnp.bfloat16)


def place_kernel(requests, peak, terms, out, total):
    slot = pl.program_id(0)
    slice_count = terms.shape[1]
    patch_side = terms.shape[-1]
    tile_cells = out.shape[-1]

    @pl.when(slot == 0)
    def _():
        total[...] = jnp.zeros_like(total)

    row = requests[slot, 1]
    col = requests[slot, 2]
    row_base = pl.multiple_of((row // 8) * 8, 8)
    col_base = pl.multiple_of((col // 128) * 128, 128)
    row_rest = row - row_base
    col_rest = col - col_base
    band_rows = patch_side + 8
    band_cols = 2 * patch_side
    row_pick = (
        lax.broadcasted_iota(jnp.int32, (band_rows, patch_side), 0)
        == lax.broadcasted_iota(jnp.int32, (band_rows, patch_side), 1) + row_rest
    ).astype(jnp.bfloat16)
    col_pick = (
        lax.broadcasted_iota(jnp.int32, (patch_side, band_cols), 1)
        == lax.broadcasted_iota(jnp.int32, (patch_side, band_cols), 0) + col_rest
    ).astype(jnp.bfloat16)
    pieces = []
    for layer in range(slice_count):
        for part in range(2):
            term = terms[0, layer, part]
            high = term.astype(jnp.bfloat16)
            low = (term - high.astype(jnp.float32)).astype(jnp.bfloat16)
            pieces += [high, low]
    side_by_side = jnp.concatenate(pieces, axis=1)
    shifted = jnp.dot(row_pick, side_by_side, preferred_element_type=jnp.float32)
    shifted = shifted.astype(jnp.bfloat16)
    stacked = jnp.concatenate(
        [shifted[:, index * patch_side:(index + 1) * patch_side] for index in range(len(pieces))],
        axis=0,
    )
    placed = jnp.dot(stacked, col_pick, preferred_element_type=jnp.float32)
    for layer in range(slice_count):
        for part in range(2):
            index = 2 * (2 * layer + part)
            band = (
                placed[index * band_rows:(index + 1) * band_rows]
                + placed[(index + 1) * band_rows:(index + 2) * band_rows]
            )
            window = total.at[layer, part, pl.ds(row_base, band_rows), pl.ds(col_base, band_cols)]
            window[...] = window[...] + band

    @pl.when(slot == pl.num_programs(0) - 1)
    def _():
        out[...] = total[:, :, :tile_cells, :tile_cells] / peak[0, 0]


def accumulate(terms, requests, peak, tile_cells):
    slot_count, slice_count = terms.shape[:2]
    patch_side = terms.shape[-1]
    grid_spec = pltpu.PrefetchScalarGridSpec(
        num_scalar_prefetch=1,
        grid=(slot_count,),
        in_specs=[
            pl.BlockSpec(memory_space=pltpu.SMEM),
            pl.BlockSpec(
                (1, slice_count, 2, patch_side, patch_side), lambda k, req: (k, 0, 0, 0, 0)
            ),
        ],
        out_specs=pl.BlockSpec(
            (slice_count, 2, tile_cells, tile_cells), lambda k, req: (0, 0, 0, 0)
        ),
        scratch_shapes=[
            pltpu.VMEM(
                (slice_count, 2, tile_cells + 8, tile_cells + patch_side), jnp.float32
            )
        ],
    )
    return pl.pallas_call(
        place_kernel,
        grid_spec=grid_spec,
        out_shape=jax.ShapeDtypeStruct((slice_count, 2, tile_cells, tile_cells), jnp.float32),
        compiler_params=pltpu.CompilerParams(dimension_semantics=("arbitrary",)),
    )(requests, peak.reshape(1, 1), terms)


def group_max(value):
    count = lax.axis_size("group")
    if count & (count - 1) == 0:
        step = 1
        while step < count:
            pairs = [(index, index ^ step) for index in range(count)]
            value = jnp.maximum(value, lax.ppermute(value, "group", pairs))
            step *= 2
        return value
    running = value
    pairs = [(index, (index + 1) % count) for index in range(count)]
    for _ in range(count - 1):
        value = lax.ppermute(value, "group", pairs)
        running = jnp.maximum(running, value)
    return running


def propagate(patches, measured, probe_modes, kernel, forward_blocks, inverse_blocks):
    count = patches.shape[0]
    slice_count = patches.shape[1]
    modes = probe_modes.shape[1]
    patch_side = patches.shape[-1]
    wavefield = jnp.broadcast_to(probe_modes, (count, modes, 2, patch_side, patch_side))
    transmit = [patches[:, layer].astype(jnp.float32)[:, None] for layer in range(slice_count)]
    wavefields = []
    leaving = wavefield
    for layer in range(slice_count):
        wavefields.append(wavefield)
        leaving = complex_times(wavefield, transmit[layer])
        if layer < slice_count - 1:
            wavefield = transform(
                complex_times(kernel, transform(leaving, forward_blocks)), inverse_blocks
            )
    farfield = transform(leaving, forward_blocks)
    intensity = jnp.sum(farfield * farfield, axis=(1, 2))
    factor = 1.0 - measured / jnp.sqrt(jnp.maximum(intensity, 1.0))
    adjoint = transform(farfield * factor[:, None, None], inverse_blocks)
    gradients = [None] * slice_count
    for layer in reversed(range(slice_count)):
        gradients[layer] = jnp.sum(conj_times(wavefields[layer], adjoint), axis=1)
        adjoint = conj_times(transmit[layer], adjoint)
        if layer > 0:
            adjoint = transform(
                conj_times(kernel, transform(adjoint, forward_blocks)), inverse_blocks
            )
    return jnp.stack(gradients, axis=1), jnp.sum(adjoint, axis=0)


def on_device(object_field, probe_modes, prop_phase, amplitude, tile_owner, corner):
    members = lax.axis_size("member")
    pos_dev = tile_owner.shape[1]
    capacity = max(2, (2 * pos_dev + members - 1) // members)
    slot_count = members * capacity
    tile_cells = object_field.shape[2]
    patch_side = prop_phase.shape[0]
    power = jnp.max(jnp.sum(probe_modes * probe_modes, axis=(1, 2)))
    peak_power = group_max(power) + 1e-06
    flat_slots = slot_numbers(tile_owner[0, :, 0], members, capacity)
    entries = jnp.concatenate([jnp.ones((pos_dev, 1), jnp.int32), corner[0]], axis=1)
    chosen = (flat_slots[:, None] == jnp.arange(slot_count, dtype=jnp.int32)[None, :]).astype(
        jnp.int32
    )
    outgoing = jnp.sum(chosen[:, :, None] * entries[:, None, :], axis=0)
    requests = lax.all_to_all(
        outgoing.reshape(members, capacity, 3), "member", split_axis=0, concat_axis=0, tiled=True
    ).reshape(slot_count, 3)
    sent = jnp.zeros((slot_count, patch_side, patch_side), jnp.float32).at[flat_slots].set(
        amplitude[0]
    )
    measured = lax.all_to_all(
        sent.reshape(members, capacity, patch_side, patch_side),
        "member",
        split_axis=0,
        concat_axis=0,
        tiled=True,
    ).reshape(slot_count, patch_side, patch_side)
    patches = cut_windows(object_field, requests, patch_side)
    forward_blocks = fourier_blocks(patch_side, -1.0)
    inverse_blocks = fourier_blocks(patch_side, 1.0)
    kernel = jnp.stack([jnp.cos(prop_phase), jnp.sin(prop_phase)])
    chunk = math.gcd(slot_count, 32)
    chunks = slot_count // chunk
    work = partial(
        propagate,
        probe_modes=probe_modes,
        kernel=kernel,
        forward_blocks=forward_blocks,
        inverse_blocks=inverse_blocks,
    )
    if chunks == 1:
        gradients, adjoint_sum = work(patches, measured)
    else:
        gradients, adjoint_sums = lax.map(
            lambda pair: work(*pair),
            (
                patches.reshape((chunks, chunk) + patches.shape[1:]),
                measured.reshape(chunks, chunk, patch_side, patch_side),
            ),
        )
        gradients = gradients.reshape((slot_count,) + gradients.shape[2:])
        adjoint_sum = jnp.sum(adjoint_sums, axis=0)
    probe_grad = lax.psum(adjoint_sum / pos_dev, "member")[None]
    object_grad = accumulate(gradients, requests, peak_power, tile_cells)
    return (object_grad, probe_grad)


def solution(mesh):
    return jax.shard_map(
        on_device,
        mesh=mesh,
        in_specs=(
            P(None, None, "group", "member"),
            P("group", None, None, None, None),
            P(),
            P("group", "member", None, None),
            P("group", "member", None),
            P("group", "member", None),
        ),
        out_specs=(P(None, None, "group", "member"), P("group", None, None, None, None)),
        check_vma=False,
    )
```

```python
from functools import partial
import math

import jax
import jax.numpy as jnp
from jax import lax
from jax.experimental import pallas as pl
from jax.experimental.pallas import tpu as pltpu
from jax.sharding import PartitionSpec as P

DFT_PRECISION = lax.Precision.HIGH


def fourier_blocks(length, sign):
    counter = jnp.arange(length, dtype=jnp.int32)
    product = counter[:, None] * counter[None, :] % length
    angles = product.astype(jnp.float32) * (2.0 * math.pi / length)
    norming = 1.0 / math.sqrt(length)
    cosine = jnp.cos(angles) * norming
    sine_part = jnp.sin(angles) * (sign * norming)
    return jnp.stack([jnp.stack([cosine, sine_part]), jnp.stack([-sine_part, cosine])])


def transform(field, blocks):
    across = jnp.einsum("...chn,cdnk->...dhk", field, blocks, precision=DFT_PRECISION)
    return jnp.einsum("cdkn,...cnw->...dkw", blocks, across, precision=DFT_PRECISION)


def complex_times(left, right):
    left_re, left_im = (left[..., 0, :, :], left[..., 1, :, :])
    right_re, right_im = (right[..., 0, :, :], right[..., 1, :, :])
    return jnp.stack(
        [left_re * right_re - left_im * right_im, left_re * right_im + left_im * right_re], axis=-3
    )


def conj_times(left, right):
    left_re, left_im = (left[..., 0, :, :], left[..., 1, :, :])
    right_re, right_im = (right[..., 0, :, :], right[..., 1, :, :])
    return jnp.stack(
        [left_re * right_re + left_im * right_im, left_re * right_im - left_im * right_re], axis=-3
    )


def slot_numbers(targets, members, capacity):
    matches = (targets[:, None] == jnp.arange(members, dtype=jnp.int32)[None, :]).astype(jnp.int32)
    before = jnp.cumsum(matches, axis=0) - matches
    return targets * capacity + jnp.sum(before * matches, axis=1)


def selectors(offsets, patch_side, tile_cells, dtype):
    inner = jnp.arange(patch_side, dtype=jnp.int32)
    cells = jnp.arange(tile_cells, dtype=jnp.int32)
    hit = offsets[:, None, None] + inner[None, :, None] == cells[None, None, :]
    return hit.astype(dtype)


def cut_windows(tiles, requests, patch_side):
    tile_cells = tiles.shape[-1]
    valid = requests[:, 0].astype(jnp.bfloat16)
    row_sel = selectors(requests[:, 1], patch_side, tile_cells, jnp.bfloat16) * valid[:, None, None]
    col_sel = selectors(requests[:, 2], patch_side, tile_cells, jnp.bfloat16)
    rows = jnp.einsum("kit,sctu->kscui", row_sel, tiles, preferred_element_type=jnp.float32)
    rows = rows.astype(jnp.bfloat16)
    window = jnp.einsum("kscui,kju->kscij", rows, col_sel, preferred_element_type=jnp.float32)
    return window.astype(jnp.bfloat16)


def place_kernel(requests, peak, terms, out, total):
    slot = pl.program_id(0)
    slice_count = terms.shape[1]
    patch_side = terms.shape[-1]
    tile_cells = out.shape[-1]

    @pl.when(slot == 0)
    def _():
        total[...] = jnp.zeros_like(total)

    row = requests[slot, 1]
    col = requests[slot, 2]
    row_base = pl.multiple_of((row // 8) * 8, 8)
    col_base = pl.multiple_of((col // 128) * 128, 128)
    row_rest = row - row_base
    col_rest = col - col_base
    band_rows = patch_side + 8
    band_cols = 2 * patch_side
    row_pick = (
        lax.broadcasted_iota(jnp.int32, (band_rows, patch_side), 0)
        == lax.broadcasted_iota(jnp.int32, (band_rows, patch_side), 1) + row_rest
    ).astype(jnp.bfloat16)
    col_pick = (
        lax.broadcasted_iota(jnp.int32, (patch_side, band_cols), 1)
        == lax.broadcasted_iota(jnp.int32, (patch_side, band_cols), 0) + col_rest
    ).astype(jnp.bfloat16)
    pieces = []
    for layer in range(slice_count):
        for part in range(2):
            term = terms[0, layer, part]
            high = term.astype(jnp.bfloat16)
            low = (term - high.astype(jnp.float32)).astype(jnp.bfloat16)
            pieces += [high, low]
    side_by_side = jnp.concatenate(pieces, axis=1)
    shifted = jnp.dot(row_pick, side_by_side, preferred_element_type=jnp.float32)
    shifted = shifted.astype(jnp.bfloat16)
    stacked = jnp.concatenate(
        [shifted[:, index * patch_side:(index + 1) * patch_side] for index in range(len(pieces))],
        axis=0,
    )
    placed = jnp.dot(stacked, col_pick, preferred_element_type=jnp.float32)
    for layer in range(slice_count):
        for part in range(2):
            index = 2 * (2 * layer + part)
            band = (
                placed[index * band_rows:(index + 1) * band_rows]
                + placed[(index + 1) * band_rows:(index + 2) * band_rows]
            )
            window = total.at[layer, part, pl.ds(row_base, band_rows), pl.ds(col_base, band_cols)]
            window[...] = window[...] + band

    @pl.when(slot == pl.num_programs(0) - 1)
    def _():
        out[...] = total[:, :, :tile_cells, :tile_cells] / peak[0, 0]


def accumulate(terms, requests, peak, tile_cells):
    slot_count, slice_count = terms.shape[:2]
    patch_side = terms.shape[-1]
    grid_spec = pltpu.PrefetchScalarGridSpec(
        num_scalar_prefetch=1,
        grid=(slot_count,),
        in_specs=[
            pl.BlockSpec(memory_space=pltpu.SMEM),
            pl.BlockSpec(
                (1, slice_count, 2, patch_side, patch_side), lambda k, req: (k, 0, 0, 0, 0)
            ),
        ],
        out_specs=pl.BlockSpec(
            (slice_count, 2, tile_cells, tile_cells), lambda k, req: (0, 0, 0, 0)
        ),
        scratch_shapes=[
            pltpu.VMEM(
                (slice_count, 2, tile_cells + 8, tile_cells + patch_side), jnp.float32
            )
        ],
    )
    return pl.pallas_call(
        place_kernel,
        grid_spec=grid_spec,
        out_shape=jax.ShapeDtypeStruct((slice_count, 2, tile_cells, tile_cells), jnp.float32),
        compiler_params=pltpu.CompilerParams(dimension_semantics=("arbitrary",)),
    )(requests, peak.reshape(1, 1), terms)


def group_max(value):
    count = lax.axis_size("group")
    if count & (count - 1) == 0:
        step = 1
        while step < count:
            pairs = [(index, index ^ step) for index in range(count)]
            value = jnp.maximum(value, lax.ppermute(value, "group", pairs))
            step *= 2
        return value
    running = value
    pairs = [(index, (index + 1) % count) for index in range(count)]
    for _ in range(count - 1):
        value = lax.ppermute(value, "group", pairs)
        running = jnp.maximum(running, value)
    return running


def split_pair(value):
    high = value.astype(jnp.bfloat16)
    low = (value - high.astype(jnp.float32)).astype(jnp.bfloat16)
    return high, low


def times_right(value, pair):
    high, low = split_pair(value)
    return (
        jnp.dot(high, pair[0], preferred_element_type=jnp.float32)
        + jnp.dot(low, pair[0], preferred_element_type=jnp.float32)
        + jnp.dot(high, pair[1], preferred_element_type=jnp.float32)
    )


def times_left(pair, value):
    high, low = split_pair(value)
    return (
        jnp.dot(pair[0], high, preferred_element_type=jnp.float32)
        + jnp.dot(pair[0], low, preferred_element_type=jnp.float32)
        + jnp.dot(pair[1], high, preferred_element_type=jnp.float32)
    )


def fourier_2d(real, imag, across, down, inverse):
    side = real.shape[0]
    right = times_right(jnp.concatenate([real, imag], axis=0), across)
    real_c, real_s = right[:side, :side], right[:side, side:]
    imag_c, imag_s = right[side:, :side], right[side:, side:]
    if inverse:
        mid_real, mid_imag = real_c - imag_s, imag_c + real_s
    else:
        mid_real, mid_imag = real_c + imag_s, imag_c - real_s
    left = times_left(down, jnp.concatenate([mid_real, mid_imag], axis=1))
    c_real, c_imag = left[:side, :side], left[:side, side:]
    s_real, s_imag = left[side:, :side], left[side:, side:]
    if inverse:
        return c_real - s_imag, c_imag + s_real
    return c_real + s_imag, c_imag - s_real


def propagate_kernel(patch_ref, measured_ref, probe_ref, kern_ref, across_ref, down_ref,
                     grad_ref, probe_sum_ref):
    slot = pl.program_id(0)
    slice_count = patch_ref.shape[1]
    modes = probe_ref.shape[0]
    across = (across_ref[0], across_ref[1])
    down = (down_ref[0], down_ref[1])
    kern_real, kern_imag = kern_ref[0], kern_ref[1]
    waves = [(probe_ref[m, 0], probe_ref[m, 1]) for m in range(modes)]
    history = []
    leaving = None
    for layer in range(slice_count):
        history.append(waves)
        patch_real = patch_ref[0, layer, 0].astype(jnp.float32)
        patch_imag = patch_ref[0, layer, 1].astype(jnp.float32)
        leaving = [
            (wr * patch_real - wi * patch_imag, wr * patch_imag + wi * patch_real)
            for wr, wi in waves
        ]
        if layer < slice_count - 1:
            waves = []
            for lr, li in leaving:
                fr, fi = fourier_2d(lr, li, across, down, False)
                tr = kern_real * fr - kern_imag * fi
                ti = kern_real * fi + kern_imag * fr
                waves.append(fourier_2d(tr, ti, across, down, True))
    far = [fourier_2d(lr, li, across, down, False) for lr, li in leaving]
    intensity = None
    for fr, fi in far:
        power = fr * fr + fi * fi
        intensity = power if intensity is None else intensity + power
    factor = 1.0 - measured_ref[0] / jnp.sqrt(jnp.maximum(intensity, 1.0))
    back = [fourier_2d(fr * factor, fi * factor, across, down, True) for fr, fi in far]
    for layer in reversed(range(slice_count)):
        grad_real = None
        grad_imag = None
        for (wr, wi), (br, bi) in zip(history[layer], back):
            term_real = wr * br + wi * bi
            term_imag = wr * bi - wi * br
            grad_real = term_real if grad_real is None else grad_real + term_real
            grad_imag = term_imag if grad_imag is None else grad_imag + term_imag
        grad_ref[0, layer, 0] = grad_real
        grad_ref[0, layer, 1] = grad_imag
        patch_real = patch_ref[0, layer, 0].astype(jnp.float32)
        patch_imag = patch_ref[0, layer, 1].astype(jnp.float32)
        back = [
            (patch_real * br + patch_imag * bi, patch_real * bi - patch_imag * br)
            for br, bi in back
        ]
        if layer > 0:
            moved = []
            for br, bi in back:
                fr, fi = fourier_2d(br, bi, across, down, False)
                tr = kern_real * fr + kern_imag * fi
                ti = kern_real * fi - kern_imag * fr
                moved.append(fourier_2d(tr, ti, across, down, True))
            back = moved

    @pl.when(slot == 0)
    def _():
        probe_sum_ref[...] = jnp.zeros_like(probe_sum_ref)

    for mode, (br, bi) in enumerate(back):
        probe_sum_ref[mode, 0] = probe_sum_ref[mode, 0] + br
        probe_sum_ref[mode, 1] = probe_sum_ref[mode, 1] + bi


def dft_pairs(length):
    counter = jnp.arange(length, dtype=jnp.int32)
    product = counter[:, None] * counter[None, :] % length
    angles = product.astype(jnp.float32) * (2.0 * math.pi / length)
    norming = 1.0 / math.sqrt(length)
    cosine = jnp.cos(angles) * norming
    sine = jnp.sin(angles) * norming
    across = jnp.concatenate([cosine, sine], axis=1)
    down = jnp.concatenate([cosine, sine], axis=0)

    def pair(value):
        high = lax.reduce_precision(value, exponent_bits=8, mantissa_bits=7)
        return jnp.stack([high, value - high]).astype(jnp.bfloat16)

    return pair(across), pair(down)


def propagate(patches, measured, probe_modes, prop_phase):
    count, slice_count = patches.shape[:2]
    modes = probe_modes.shape[0]
    side = patches.shape[-1]
    kern = jnp.stack([jnp.cos(prop_phase), jnp.sin(prop_phase)])
    across, down = dft_pairs(side)
    whole = lambda shape: pl.BlockSpec(shape, lambda k: (0,) * len(shape))
    return pl.pallas_call(
        propagate_kernel,
        grid=(count,),
        in_specs=[
            pl.BlockSpec((1, slice_count, 2, side, side), lambda k: (k, 0, 0, 0, 0)),
            pl.BlockSpec((1, side, side), lambda k: (k, 0, 0)),
            whole((modes, 2, side, side)),
            whole((2, side, side)),
            whole((2, side, 2 * side)),
            whole((2, 2 * side, side)),
        ],
        out_specs=[
            pl.BlockSpec((1, slice_count, 2, side, side), lambda k: (k, 0, 0, 0, 0)),
            whole((modes, 2, side, side)),
        ],
        out_shape=[
            jax.ShapeDtypeStruct((count, slice_count, 2, side, side), jnp.float32),
            jax.ShapeDtypeStruct((modes, 2, side, side), jnp.float32),
        ],
        compiler_params=pltpu.CompilerParams(dimension_semantics=("arbitrary",)),
    )(patches, measured, probe_modes, kern, across, down)


def on_device(object_field, probe_modes, prop_phase, amplitude, tile_owner, corner):
    members = lax.axis_size("member")
    pos_dev = tile_owner.shape[1]
    capacity = max(2, (2 * pos_dev + members - 1) // members)
    slot_count = members * capacity
    tile_cells = object_field.shape[2]
    patch_side = prop_phase.shape[0]
    power = jnp.max(jnp.sum(probe_modes * probe_modes, axis=(1, 2)))
    peak_power = group_max(power) + 1e-06
    flat_slots = slot_numbers(tile_owner[0, :, 0], members, capacity)
    entries = jnp.concatenate([jnp.ones((pos_dev, 1), jnp.int32), corner[0]], axis=1)
    chosen = (flat_slots[:, None] == jnp.arange(slot_count, dtype=jnp.int32)[None, :]).astype(
        jnp.int32
    )
    outgoing = jnp.sum(chosen[:, :, None] * entries[:, None, :], axis=0)
    requests = lax.all_to_all(
        outgoing.reshape(members, capacity, 3), "member", split_axis=0, concat_axis=0, tiled=True
    ).reshape(slot_count, 3)
    sent = jnp.zeros((slot_count, patch_side, patch_side), jnp.float32).at[flat_slots].set(
        amplitude[0]
    )
    measured = lax.all_to_all(
        sent.reshape(members, capacity, patch_side, patch_side),
        "member",
        split_axis=0,
        concat_axis=0,
        tiled=True,
    ).reshape(slot_count, patch_side, patch_side)
    patches = cut_windows(object_field, requests, patch_side)
    gradients, adjoint_sum = propagate(patches, measured, probe_modes[0], prop_phase)
    probe_grad = lax.psum(adjoint_sum / pos_dev, "member")[None]
    object_grad = accumulate(gradients, requests, peak_power, tile_cells)
    return (object_grad, probe_grad)


def solution(mesh):
    return jax.shard_map(
        on_device,
        mesh=mesh,
        in_specs=(
            P(None, None, "group", "member"),
            P("group", None, None, None, None),
            P(),
            P("group", "member", None, None),
            P("group", "member", None),
            P("group", "member", None),
        ),
        out_specs=(P(None, None, "group", "member"), P("group", None, None, None, None)),
        check_vma=False,
    )
```

```python
from functools import partial
import math

import jax
import jax.numpy as jnp
from jax import lax
from jax.experimental import pallas as pl
from jax.experimental.pallas import tpu as pltpu
from jax.sharding import PartitionSpec as P

DFT_PRECISION = lax.Precision.HIGH


def fourier_blocks(length, sign):
    counter = jnp.arange(length, dtype=jnp.int32)
    product = counter[:, None] * counter[None, :] % length
    angles = product.astype(jnp.float32) * (2.0 * math.pi / length)
    norming = 1.0 / math.sqrt(length)
    cosine = jnp.cos(angles) * norming
    sine_part = jnp.sin(angles) * (sign * norming)
    return jnp.stack([jnp.stack([cosine, sine_part]), jnp.stack([-sine_part, cosine])])


def transform(field, blocks):
    across = jnp.einsum("...chn,cdnk->...dhk", field, blocks, precision=DFT_PRECISION)
    return jnp.einsum("cdkn,...cnw->...dkw", blocks, across, precision=DFT_PRECISION)


def complex_times(left, right):
    left_re, left_im = (left[..., 0, :, :], left[..., 1, :, :])
    right_re, right_im = (right[..., 0, :, :], right[..., 1, :, :])
    return jnp.stack(
        [left_re * right_re - left_im * right_im, left_re * right_im + left_im * right_re], axis=-3
    )


def conj_times(left, right):
    left_re, left_im = (left[..., 0, :, :], left[..., 1, :, :])
    right_re, right_im = (right[..., 0, :, :], right[..., 1, :, :])
    return jnp.stack(
        [left_re * right_re + left_im * right_im, left_re * right_im - left_im * right_re], axis=-3
    )


def slot_numbers(targets, members, capacity):
    matches = (targets[:, None] == jnp.arange(members, dtype=jnp.int32)[None, :]).astype(jnp.int32)
    before = jnp.cumsum(matches, axis=0) - matches
    return targets * capacity + jnp.sum(before * matches, axis=1)


def selectors(offsets, patch_side, tile_cells, dtype):
    inner = jnp.arange(patch_side, dtype=jnp.int32)
    cells = jnp.arange(tile_cells, dtype=jnp.int32)
    hit = offsets[:, None, None] + inner[None, :, None] == cells[None, None, :]
    return hit.astype(dtype)


def cut_windows(tiles, requests, patch_side):
    tile_cells = tiles.shape[-1]
    valid = requests[:, 0].astype(jnp.bfloat16)
    row_sel = selectors(requests[:, 1], patch_side, tile_cells, jnp.bfloat16) * valid[:, None, None]
    col_sel = selectors(requests[:, 2], patch_side, tile_cells, jnp.bfloat16)
    rows = jnp.einsum("kit,sctu->kscui", row_sel, tiles, preferred_element_type=jnp.float32)
    rows = rows.astype(jnp.bfloat16)
    window = jnp.einsum("kscui,kju->kscij", rows, col_sel, preferred_element_type=jnp.float32)
    return window.astype(jnp.bfloat16)


def place_kernel(requests, peak, terms, out, total):
    slot = pl.program_id(0)
    slice_count = terms.shape[1]
    patch_side = terms.shape[-1]
    tile_cells = out.shape[-1]

    @pl.when(slot == 0)
    def _():
        total[...] = jnp.zeros_like(total)

    row = requests[slot, 1]
    col = requests[slot, 2]
    row_base = pl.multiple_of((row // 8) * 8, 8)
    col_base = pl.multiple_of((col // 128) * 128, 128)
    row_rest = row - row_base
    col_rest = col - col_base
    band_rows = patch_side + 8
    band_cols = 2 * patch_side
    row_pick = (
        lax.broadcasted_iota(jnp.int32, (band_rows, patch_side), 0)
        == lax.broadcasted_iota(jnp.int32, (band_rows, patch_side), 1) + row_rest
    ).astype(jnp.bfloat16)
    col_pick = (
        lax.broadcasted_iota(jnp.int32, (patch_side, band_cols), 1)
        == lax.broadcasted_iota(jnp.int32, (patch_side, band_cols), 0) + col_rest
    ).astype(jnp.bfloat16)
    pieces = []
    for layer in range(slice_count):
        for part in range(2):
            term = terms[0, layer, part]
            high = term.astype(jnp.bfloat16)
            low = (term - high.astype(jnp.float32)).astype(jnp.bfloat16)
            pieces += [high, low]
    side_by_side = jnp.concatenate(pieces, axis=1)
    shifted = jnp.dot(row_pick, side_by_side, preferred_element_type=jnp.float32)
    shifted = shifted.astype(jnp.bfloat16)
    stacked = jnp.concatenate(
        [shifted[:, index * patch_side:(index + 1) * patch_side] for index in range(len(pieces))],
        axis=0,
    )
    placed = jnp.dot(stacked, col_pick, preferred_element_type=jnp.float32)
    for layer in range(slice_count):
        for part in range(2):
            index = 2 * (2 * layer + part)
            band = (
                placed[index * band_rows:(index + 1) * band_rows]
                + placed[(index + 1) * band_rows:(index + 2) * band_rows]
            )
            window = total.at[layer, part, pl.ds(row_base, band_rows), pl.ds(col_base, band_cols)]
            window[...] = window[...] + band

    @pl.when(slot == pl.num_programs(0) - 1)
    def _():
        out[...] = total[:, :, :tile_cells, :tile_cells] / peak[0, 0]


def accumulate(terms, requests, peak, tile_cells):
    slot_count, slice_count = terms.shape[:2]
    patch_side = terms.shape[-1]
    grid_spec = pltpu.PrefetchScalarGridSpec(
        num_scalar_prefetch=1,
        grid=(slot_count,),
        in_specs=[
            pl.BlockSpec(memory_space=pltpu.SMEM),
            pl.BlockSpec(
                (1, slice_count, 2, patch_side, patch_side), lambda k, req: (k, 0, 0, 0, 0)
            ),
        ],
        out_specs=pl.BlockSpec(
            (slice_count, 2, tile_cells, tile_cells), lambda k, req: (0, 0, 0, 0)
        ),
        scratch_shapes=[
            pltpu.VMEM(
                (slice_count, 2, tile_cells + 8, tile_cells + patch_side), jnp.float32
            )
        ],
    )
    return pl.pallas_call(
        place_kernel,
        grid_spec=grid_spec,
        out_shape=jax.ShapeDtypeStruct((slice_count, 2, tile_cells, tile_cells), jnp.float32),
        compiler_params=pltpu.CompilerParams(dimension_semantics=("arbitrary",)),
    )(requests, peak.reshape(1, 1), terms)


def group_max(value):
    count = lax.axis_size("group")
    if count & (count - 1) == 0:
        step = 1
        while step < count:
            pairs = [(index, index ^ step) for index in range(count)]
            value = jnp.maximum(value, lax.ppermute(value, "group", pairs))
            step *= 2
        return value
    running = value
    pairs = [(index, (index + 1) % count) for index in range(count)]
    for _ in range(count - 1):
        value = lax.ppermute(value, "group", pairs)
        running = jnp.maximum(running, value)
    return running


def split_pair(value):
    high = value.astype(jnp.bfloat16)
    low = (value - high.astype(jnp.float32)).astype(jnp.bfloat16)
    return high, low


def stack_three(value, axis):
    high = value.astype(jnp.bfloat16)
    low = (value - high.astype(jnp.float32)).astype(jnp.bfloat16)
    return jnp.concatenate([high, low, high], axis=axis)


def fourier_2d(fields, right_mat, left_mat):
    side = fields[0][0].shape[0]
    count = len(fields)
    rows = jnp.concatenate([jnp.concatenate([re, im], axis=1) for re, im in fields], axis=0)
    mid = jnp.dot(stack_three(rows, 1), right_mat, preferred_element_type=jnp.float32)
    parted = jnp.concatenate(
        [
            jnp.concatenate([mid[m * side:(m + 1) * side, :side] for m in range(count)], axis=1),
            jnp.concatenate([mid[m * side:(m + 1) * side, side:] for m in range(count)], axis=1),
        ],
        axis=0,
    )
    out = jnp.dot(left_mat, stack_three(parted, 0), preferred_element_type=jnp.float32)
    return [
        (out[:side, m * side:(m + 1) * side], out[side:, m * side:(m + 1) * side])
        for m in range(count)
    ]


def propagate_kernel(patch_ref, measured_ref, probe_ref, kern_ref, mats_right, mats_left,
                     grad_ref, probe_sum_ref):
    slot = pl.program_id(0)
    slice_count = patch_ref.shape[1]
    modes = probe_ref.shape[0]
    forward = lambda fields: fourier_2d(fields, mats_right[0], mats_left[0])
    inverse = lambda fields: fourier_2d(fields, mats_right[1], mats_left[1])
    kern_real, kern_imag = kern_ref[0], kern_ref[1]
    waves = [(probe_ref[m, 0], probe_ref[m, 1]) for m in range(modes)]
    history = []
    leaving = None
    for layer in range(slice_count):
        history.append(waves)
        patch_real = patch_ref[0, layer, 0].astype(jnp.float32)
        patch_imag = patch_ref[0, layer, 1].astype(jnp.float32)
        leaving = [
            (wr * patch_real - wi * patch_imag, wr * patch_imag + wi * patch_real)
            for wr, wi in waves
        ]
        if layer < slice_count - 1:
            spectra = forward(leaving)
            waves = inverse(
                [
                    (kern_real * fr - kern_imag * fi, kern_real * fi + kern_imag * fr)
                    for fr, fi in spectra
                ]
            )
    far = forward(leaving)
    intensity = None
    for fr, fi in far:
        power = fr * fr + fi * fi
        intensity = power if intensity is None else intensity + power
    factor = 1.0 - measured_ref[0] / jnp.sqrt(jnp.maximum(intensity, 1.0))
    back = inverse([(fr * factor, fi * factor) for fr, fi in far])
    for layer in reversed(range(slice_count)):
        grad_real = None
        grad_imag = None
        for (wr, wi), (br, bi) in zip(history[layer], back):
            term_real = wr * br + wi * bi
            term_imag = wr * bi - wi * br
            grad_real = term_real if grad_real is None else grad_real + term_real
            grad_imag = term_imag if grad_imag is None else grad_imag + term_imag
        grad_ref[0, layer, 0] = grad_real
        grad_ref[0, layer, 1] = grad_imag
        patch_real = patch_ref[0, layer, 0].astype(jnp.float32)
        patch_imag = patch_ref[0, layer, 1].astype(jnp.float32)
        back = [
            (patch_real * br + patch_imag * bi, patch_real * bi - patch_imag * br)
            for br, bi in back
        ]
        if layer > 0:
            spectra = forward(back)
            back = inverse(
                [
                    (kern_real * fr + kern_imag * fi, kern_real * fi - kern_imag * fr)
                    for fr, fi in spectra
                ]
            )

    @pl.when(slot == 0)
    def _():
        probe_sum_ref[...] = jnp.zeros_like(probe_sum_ref)

    for mode, (br, bi) in enumerate(back):
        probe_sum_ref[mode, 0] = probe_sum_ref[mode, 0] + br
        probe_sum_ref[mode, 1] = probe_sum_ref[mode, 1] + bi


def dft_mats(length):
    counter = jnp.arange(length, dtype=jnp.int32)
    product = counter[:, None] * counter[None, :] % length
    angles = product.astype(jnp.float32) * (2.0 * math.pi / length)
    norming = 1.0 / math.sqrt(length)
    cosine = jnp.cos(angles) * norming
    sine = jnp.sin(angles) * norming
    minus = jnp.concatenate(
        [jnp.concatenate([cosine, -sine], axis=1), jnp.concatenate([sine, cosine], axis=1)], axis=0
    )
    plus = jnp.concatenate(
        [jnp.concatenate([cosine, sine], axis=1), jnp.concatenate([-sine, cosine], axis=1)], axis=0
    )

    def parts(value):
        high = lax.reduce_precision(value, exponent_bits=8, mantissa_bits=7)
        return high.astype(jnp.bfloat16), (value - high).astype(jnp.bfloat16)

    def right(value):
        high, low = parts(value)
        return jnp.concatenate([high, high, low], axis=0)

    def left(value):
        high, low = parts(value)
        return jnp.concatenate([high, high, low], axis=1)

    mats_right = jnp.stack([right(minus), right(plus)])
    mats_left = jnp.stack([left(plus), left(minus)])
    return mats_right, mats_left


def propagate(patches, measured, probe_modes, prop_phase):
    count, slice_count = patches.shape[:2]
    modes = probe_modes.shape[0]
    side = patches.shape[-1]
    kern = jnp.stack([jnp.cos(prop_phase), jnp.sin(prop_phase)])
    mats_right, mats_left = dft_mats(side)
    whole = lambda shape: pl.BlockSpec(shape, lambda k: (0,) * len(shape))
    return pl.pallas_call(
        propagate_kernel,
        grid=(count,),
        in_specs=[
            pl.BlockSpec((1, slice_count, 2, side, side), lambda k: (k, 0, 0, 0, 0)),
            pl.BlockSpec((1, side, side), lambda k: (k, 0, 0)),
            whole((modes, 2, side, side)),
            whole((2, side, side)),
            whole((2, 6 * side, 2 * side)),
            whole((2, 2 * side, 6 * side)),
        ],
        out_specs=[
            pl.BlockSpec((1, slice_count, 2, side, side), lambda k: (k, 0, 0, 0, 0)),
            whole((modes, 2, side, side)),
        ],
        out_shape=[
            jax.ShapeDtypeStruct((count, slice_count, 2, side, side), jnp.float32),
            jax.ShapeDtypeStruct((modes, 2, side, side), jnp.float32),
        ],
        compiler_params=pltpu.CompilerParams(dimension_semantics=("arbitrary",)),
    )(patches, measured, probe_modes, kern, mats_right, mats_left)


def on_device(object_field, probe_modes, prop_phase, amplitude, tile_owner, corner):
    members = lax.axis_size("member")
    pos_dev = tile_owner.shape[1]
    capacity = max(2, (2 * pos_dev + members - 1) // members)
    slot_count = members * capacity
    tile_cells = object_field.shape[2]
    patch_side = prop_phase.shape[0]
    power = jnp.max(jnp.sum(probe_modes * probe_modes, axis=(1, 2)))
    peak_power = group_max(power) + 1e-06
    flat_slots = slot_numbers(tile_owner[0, :, 0], members, capacity)
    entries = jnp.concatenate([jnp.ones((pos_dev, 1), jnp.int32), corner[0]], axis=1)
    chosen = (flat_slots[:, None] == jnp.arange(slot_count, dtype=jnp.int32)[None, :]).astype(
        jnp.int32
    )
    outgoing = jnp.sum(chosen[:, :, None] * entries[:, None, :], axis=0)
    requests = lax.all_to_all(
        outgoing.reshape(members, capacity, 3), "member", split_axis=0, concat_axis=0, tiled=True
    ).reshape(slot_count, 3)
    sent = jnp.zeros((slot_count, patch_side, patch_side), jnp.float32).at[flat_slots].set(
        amplitude[0]
    )
    measured = lax.all_to_all(
        sent.reshape(members, capacity, patch_side, patch_side),
        "member",
        split_axis=0,
        concat_axis=0,
        tiled=True,
    ).reshape(slot_count, patch_side, patch_side)
    patches = cut_windows(object_field, requests, patch_side)
    gradients, adjoint_sum = propagate(patches, measured, probe_modes[0], prop_phase)
    probe_grad = lax.psum(adjoint_sum / pos_dev, "member")[None]
    object_grad = accumulate(gradients, requests, peak_power, tile_cells)
    return (object_grad, probe_grad)


def solution(mesh):
    return jax.shard_map(
        on_device,
        mesh=mesh,
        in_specs=(
            P(None, None, "group", "member"),
            P("group", None, None, None, None),
            P(),
            P("group", "member", None, None),
            P("group", "member", None),
            P("group", "member", None),
        ),
        out_specs=(P(None, None, "group", "member"), P("group", None, None, None, None)),
        check_vma=False,
    )
```

```python
from functools import partial
import math

import jax
import jax.numpy as jnp
from jax import lax
from jax.experimental import pallas as pl
from jax.experimental.pallas import tpu as pltpu
from jax.sharding import PartitionSpec as P

DFT_PRECISION = lax.Precision.HIGH


def fourier_blocks(length, sign):
    counter = jnp.arange(length, dtype=jnp.int32)
    product = counter[:, None] * counter[None, :] % length
    angles = product.astype(jnp.float32) * (2.0 * math.pi / length)
    norming = 1.0 / math.sqrt(length)
    cosine = jnp.cos(angles) * norming
    sine_part = jnp.sin(angles) * (sign * norming)
    return jnp.stack([jnp.stack([cosine, sine_part]), jnp.stack([-sine_part, cosine])])


def transform(field, blocks):
    across = jnp.einsum("...chn,cdnk->...dhk", field, blocks, precision=DFT_PRECISION)
    return jnp.einsum("cdkn,...cnw->...dkw", blocks, across, precision=DFT_PRECISION)


def complex_times(left, right):
    left_re, left_im = (left[..., 0, :, :], left[..., 1, :, :])
    right_re, right_im = (right[..., 0, :, :], right[..., 1, :, :])
    return jnp.stack(
        [left_re * right_re - left_im * right_im, left_re * right_im + left_im * right_re], axis=-3
    )


def conj_times(left, right):
    left_re, left_im = (left[..., 0, :, :], left[..., 1, :, :])
    right_re, right_im = (right[..., 0, :, :], right[..., 1, :, :])
    return jnp.stack(
        [left_re * right_re + left_im * right_im, left_re * right_im - left_im * right_re], axis=-3
    )


def slot_numbers(targets, members, capacity):
    matches = (targets[:, None] == jnp.arange(members, dtype=jnp.int32)[None, :]).astype(jnp.int32)
    before = jnp.cumsum(matches, axis=0) - matches
    return targets * capacity + jnp.sum(before * matches, axis=1)


def selectors(offsets, patch_side, tile_cells, dtype):
    inner = jnp.arange(patch_side, dtype=jnp.int32)
    cells = jnp.arange(tile_cells, dtype=jnp.int32)
    hit = offsets[:, None, None] + inner[None, :, None] == cells[None, None, :]
    return hit.astype(dtype)


def cut_windows(tiles, requests, patch_side):
    tile_cells = tiles.shape[-1]
    valid = requests[:, 0].astype(jnp.bfloat16)
    row_sel = selectors(requests[:, 1], patch_side, tile_cells, jnp.bfloat16) * valid[:, None, None]
    col_sel = selectors(requests[:, 2], patch_side, tile_cells, jnp.bfloat16)
    rows = jnp.einsum("kit,sctu->kscui", row_sel, tiles, preferred_element_type=jnp.float32)
    rows = rows.astype(jnp.bfloat16)
    window = jnp.einsum("kscui,kju->kscij", rows, col_sel, preferred_element_type=jnp.float32)
    return window.astype(jnp.bfloat16)


def place_kernel(requests, peak, terms, out, total):
    slot = pl.program_id(0)
    slice_count = terms.shape[1]
    patch_side = terms.shape[-1]
    tile_cells = out.shape[-1]

    @pl.when(slot == 0)
    def _():
        total[...] = jnp.zeros_like(total)

    row = requests[slot, 1]
    col = requests[slot, 2]
    row_base = pl.multiple_of((row // 8) * 8, 8)
    col_base = pl.multiple_of((col // 128) * 128, 128)
    row_rest = row - row_base
    col_rest = col - col_base
    band_rows = patch_side + 8
    band_cols = 2 * patch_side
    row_pick = (
        lax.broadcasted_iota(jnp.int32, (band_rows, patch_side), 0)
        == lax.broadcasted_iota(jnp.int32, (band_rows, patch_side), 1) + row_rest
    ).astype(jnp.bfloat16)
    col_pick = (
        lax.broadcasted_iota(jnp.int32, (patch_side, band_cols), 1)
        == lax.broadcasted_iota(jnp.int32, (patch_side, band_cols), 0) + col_rest
    ).astype(jnp.bfloat16)
    pieces = []
    for layer in range(slice_count):
        for part in range(2):
            term = terms[0, layer, part]
            high = term.astype(jnp.bfloat16)
            low = (term - high.astype(jnp.float32)).astype(jnp.bfloat16)
            pieces += [high, low]
    side_by_side = jnp.concatenate(pieces, axis=1)
    shifted = jnp.dot(row_pick, side_by_side, preferred_element_type=jnp.float32)
    shifted = shifted.astype(jnp.bfloat16)
    stacked = jnp.concatenate(
        [shifted[:, index * patch_side:(index + 1) * patch_side] for index in range(len(pieces))],
        axis=0,
    )
    placed = jnp.dot(stacked, col_pick, preferred_element_type=jnp.float32)
    for layer in range(slice_count):
        for part in range(2):
            index = 2 * (2 * layer + part)
            band = (
                placed[index * band_rows:(index + 1) * band_rows]
                + placed[(index + 1) * band_rows:(index + 2) * band_rows]
            )
            window = total.at[layer, part, pl.ds(row_base, band_rows), pl.ds(col_base, band_cols)]
            window[...] = window[...] + band

    @pl.when(slot == pl.num_programs(0) - 1)
    def _():
        out[...] = total[:, :, :tile_cells, :tile_cells] / peak[0, 0]


def accumulate(terms, requests, peak, tile_cells):
    slot_count, slice_count = terms.shape[:2]
    patch_side = terms.shape[-1]
    grid_spec = pltpu.PrefetchScalarGridSpec(
        num_scalar_prefetch=1,
        grid=(slot_count,),
        in_specs=[
            pl.BlockSpec(memory_space=pltpu.SMEM),
            pl.BlockSpec(
                (1, slice_count, 2, patch_side, patch_side), lambda k, req: (k, 0, 0, 0, 0)
            ),
        ],
        out_specs=pl.BlockSpec(
            (slice_count, 2, tile_cells, tile_cells), lambda k, req: (0, 0, 0, 0)
        ),
        scratch_shapes=[
            pltpu.VMEM(
                (slice_count, 2, tile_cells + 8, tile_cells + patch_side), jnp.float32
            )
        ],
    )
    return pl.pallas_call(
        place_kernel,
        grid_spec=grid_spec,
        out_shape=jax.ShapeDtypeStruct((slice_count, 2, tile_cells, tile_cells), jnp.float32),
        compiler_params=pltpu.CompilerParams(dimension_semantics=("arbitrary",)),
    )(requests, peak.reshape(1, 1), terms)


def group_max(value):
    count = lax.axis_size("group")
    if count & (count - 1) == 0:
        step = 1
        while step < count:
            pairs = [(index, index ^ step) for index in range(count)]
            value = jnp.maximum(value, lax.ppermute(value, "group", pairs))
            step *= 2
        return value
    running = value
    pairs = [(index, (index + 1) % count) for index in range(count)]
    for _ in range(count - 1):
        value = lax.ppermute(value, "group", pairs)
        running = jnp.maximum(running, value)
    return running


def split_pair(value):
    high = value.astype(jnp.bfloat16)
    low = (value - high.astype(jnp.float32)).astype(jnp.bfloat16)
    return high, low


def stack_three(value, axis):
    high = value.astype(jnp.bfloat16)
    low = (value - high.astype(jnp.float32)).astype(jnp.bfloat16)
    return jnp.concatenate([high, low, high], axis=axis)


def fourier_2d(fields, right_mat, left_mat):
    side = fields[0][0].shape[0]
    count = len(fields)
    rows = jnp.concatenate([jnp.concatenate([re, im], axis=1) for re, im in fields], axis=0)
    mid = jnp.dot(stack_three(rows, 1), right_mat, preferred_element_type=jnp.float32)
    parted = jnp.concatenate(
        [
            jnp.concatenate([mid[m * side:(m + 1) * side, :side] for m in range(count)], axis=1),
            jnp.concatenate([mid[m * side:(m + 1) * side, side:] for m in range(count)], axis=1),
        ],
        axis=0,
    )
    out = jnp.dot(left_mat, stack_three(parted, 0), preferred_element_type=jnp.float32)
    return [
        (out[:side, m * side:(m + 1) * side], out[side:, m * side:(m + 1) * side])
        for m in range(count)
    ]


def propagate_kernel(patch_ref, measured_ref, probe_ref, kern_ref, mats_right, mats_left,
                     peak_ref, grad_ref, probe_sum_ref):
    @pl.when(pl.program_id(0) == 0)
    def _():
        probe_sum_ref[...] = jnp.zeros_like(probe_sum_ref)

    for held in range(patch_ref.shape[0]):
        propagate_one(held, patch_ref, measured_ref, probe_ref, kern_ref, mats_right, mats_left,
                      grad_ref, probe_sum_ref)


def propagate_one(held, patch_ref, measured_ref, probe_ref, kern_ref, mats_right, mats_left,
                  grad_ref, probe_sum_ref):
    slice_count = patch_ref.shape[1]
    modes = probe_ref.shape[0]
    forward = lambda fields: fourier_2d(fields, mats_right[0], mats_left[0])
    inverse = lambda fields: fourier_2d(fields, mats_right[1], mats_left[1])
    kern_real, kern_imag = kern_ref[0], kern_ref[1]
    waves = [(probe_ref[m, 0], probe_ref[m, 1]) for m in range(modes)]
    history = []
    leaving = None
    for layer in range(slice_count):
        history.append(waves)
        patch_real = patch_ref[held, layer, 0].astype(jnp.float32)
        patch_imag = patch_ref[held, layer, 1].astype(jnp.float32)
        leaving = [
            (wr * patch_real - wi * patch_imag, wr * patch_imag + wi * patch_real)
            for wr, wi in waves
        ]
        if layer < slice_count - 1:
            spectra = forward(leaving)
            waves = inverse(
                [
                    (kern_real * fr - kern_imag * fi, kern_real * fi + kern_imag * fr)
                    for fr, fi in spectra
                ]
            )
    far = forward(leaving)
    intensity = None
    for fr, fi in far:
        power = fr * fr + fi * fi
        intensity = power if intensity is None else intensity + power
    factor = 1.0 - measured_ref[held] / jnp.sqrt(jnp.maximum(intensity, 1.0))
    back = inverse([(fr * factor, fi * factor) for fr, fi in far])
    for layer in reversed(range(slice_count)):
        grad_real = None
        grad_imag = None
        for (wr, wi), (br, bi) in zip(history[layer], back):
            term_real = wr * br + wi * bi
            term_imag = wr * bi - wi * br
            grad_real = term_real if grad_real is None else grad_real + term_real
            grad_imag = term_imag if grad_imag is None else grad_imag + term_imag
        grad_ref[held, layer, 0] = grad_real
        grad_ref[held, layer, 1] = grad_imag
        patch_real = patch_ref[held, layer, 0].astype(jnp.float32)
        patch_imag = patch_ref[held, layer, 1].astype(jnp.float32)
        back = [
            (patch_real * br + patch_imag * bi, patch_real * bi - patch_imag * br)
            for br, bi in back
        ]
        if layer > 0:
            spectra = forward(back)
            back = inverse(
                [
                    (kern_real * fr + kern_imag * fi, kern_real * fi - kern_imag * fr)
                    for fr, fi in spectra
                ]
            )

    for mode, (br, bi) in enumerate(back):
        probe_sum_ref[mode, 0] = probe_sum_ref[mode, 0] + br
        probe_sum_ref[mode, 1] = probe_sum_ref[mode, 1] + bi


def dft_mats(length):
    counter = jnp.arange(length, dtype=jnp.int32)
    product = counter[:, None] * counter[None, :] % length
    angles = product.astype(jnp.float32) * (2.0 * math.pi / length)
    norming = 1.0 / math.sqrt(length)
    cosine = jnp.cos(angles) * norming
    sine = jnp.sin(angles) * norming
    minus = jnp.concatenate(
        [jnp.concatenate([cosine, -sine], axis=1), jnp.concatenate([sine, cosine], axis=1)], axis=0
    )
    plus = jnp.concatenate(
        [jnp.concatenate([cosine, sine], axis=1), jnp.concatenate([-sine, cosine], axis=1)], axis=0
    )

    def parts(value):
        high = lax.reduce_precision(value, exponent_bits=8, mantissa_bits=7)
        return high.astype(jnp.bfloat16), (value - high).astype(jnp.bfloat16)

    def right(value):
        high, low = parts(value)
        return jnp.concatenate([high, high, low], axis=0)

    def left(value):
        high, low = parts(value)
        return jnp.concatenate([high, high, low], axis=1)

    mats_right = jnp.stack([right(minus), right(plus)])
    mats_left = jnp.stack([left(plus), left(minus)])
    return mats_right, mats_left


def propagate(patches, measured, probe_modes, prop_phase, peak):
    count, slice_count = patches.shape[:2]
    modes = probe_modes.shape[0]
    side = patches.shape[-1]
    kern = jnp.stack([jnp.cos(prop_phase), jnp.sin(prop_phase)])
    mats_right, mats_left = dft_mats(side)
    held = 2 if count % 2 == 0 else 1
    whole = lambda shape: pl.BlockSpec(shape, lambda k: (0,) * len(shape))
    return pl.pallas_call(
        propagate_kernel,
        grid=(count // held,),
        in_specs=[
            pl.BlockSpec((held, slice_count, 2, side, side), lambda k: (k, 0, 0, 0, 0)),
            pl.BlockSpec((held, side, side), lambda k: (k, 0, 0)),
            whole((modes, 2, side, side)),
            whole((2, side, side)),
            whole((2, 6 * side, 2 * side)),
            whole((2, 2 * side, 6 * side)),
            pl.BlockSpec(memory_space=pltpu.SMEM),
        ],
        out_specs=[
            pl.BlockSpec((held, slice_count, 2, side, side), lambda k: (k, 0, 0, 0, 0)),
            whole((modes, 2, side, side)),
        ],
        out_shape=[
            jax.ShapeDtypeStruct((count, slice_count, 2, side, side), jnp.float32),
            jax.ShapeDtypeStruct((modes, 2, side, side), jnp.float32),
        ],
        compiler_params=pltpu.CompilerParams(dimension_semantics=("arbitrary",)),
    )(patches, measured, probe_modes, kern, mats_right, mats_left, peak.reshape(1, 1))


def member_sum(value, members):
    flat = value.reshape(members, -1)
    pieces = lax.all_to_all(flat, "member", split_axis=0, concat_axis=0, tiled=True)
    mine = jnp.sum(pieces, axis=0, keepdims=True)
    spread = jnp.broadcast_to(mine, flat.shape)
    whole = lax.all_to_all(spread, "member", split_axis=0, concat_axis=0, tiled=True)
    return whole.reshape(value.shape)


def on_device(object_field, probe_modes, prop_phase, amplitude, tile_owner, corner):
    members = lax.axis_size("member")
    pos_dev = tile_owner.shape[1]
    capacity = max(2, (2 * pos_dev + members - 1) // members)
    slot_count = members * capacity
    tile_cells = object_field.shape[2]
    patch_side = prop_phase.shape[0]
    power = jnp.max(jnp.sum(probe_modes * probe_modes, axis=(1, 2)))
    peak_power = group_max(power) + 1e-06
    flat_slots = slot_numbers(tile_owner[0, :, 0], members, capacity)
    entries = jnp.concatenate([jnp.ones((pos_dev, 1), jnp.int32), corner[0]], axis=1)
    chosen = (flat_slots[:, None] == jnp.arange(slot_count, dtype=jnp.int32)[None, :]).astype(
        jnp.int32
    )
    outgoing = jnp.sum(chosen[:, :, None] * entries[:, None, :], axis=0)
    requests = lax.all_to_all(
        outgoing.reshape(members, capacity, 3), "member", split_axis=0, concat_axis=0, tiled=True
    ).reshape(slot_count, 3)
    sent = jnp.zeros((slot_count, patch_side, patch_side), jnp.float32).at[flat_slots].set(
        amplitude[0]
    )
    measured = lax.all_to_all(
        sent.reshape(members, capacity, patch_side, patch_side),
        "member",
        split_axis=0,
        concat_axis=0,
        tiled=True,
    ).reshape(slot_count, patch_side, patch_side)
    patches = cut_windows(object_field, requests, patch_side)
    gradients, adjoint_sum = propagate(patches, measured, probe_modes[0], prop_phase, peak_power)
    probe_grad = member_sum(adjoint_sum / pos_dev, members)[None]
    object_grad = accumulate(gradients, requests, peak_power, tile_cells)
    return (object_grad, probe_grad)


def solution(mesh):
    return jax.shard_map(
        on_device,
        mesh=mesh,
        in_specs=(
            P(None, None, "group", "member"),
            P("group", None, None, None, None),
            P(),
            P("group", "member", None, None),
            P("group", "member", None),
            P("group", "member", None),
        ),
        out_specs=(P(None, None, "group", "member"), P("group", None, None, None, None)),
        check_vma=False,
    )
```

```python
from functools import partial
import math

import jax
import jax.numpy as jnp
from jax import lax
from jax.experimental import pallas as pl
from jax.experimental.pallas import tpu as pltpu
from jax.sharding import PartitionSpec as P

DFT_PRECISION = lax.Precision.HIGH


def fourier_blocks(length, sign):
    counter = jnp.arange(length, dtype=jnp.int32)
    product = counter[:, None] * counter[None, :] % length
    angles = product.astype(jnp.float32) * (2.0 * math.pi / length)
    norming = 1.0 / math.sqrt(length)
    cosine = jnp.cos(angles) * norming
    sine_part = jnp.sin(angles) * (sign * norming)
    return jnp.stack([jnp.stack([cosine, sine_part]), jnp.stack([-sine_part, cosine])])


def transform(field, blocks):
    across = jnp.einsum("...chn,cdnk->...dhk", field, blocks, precision=DFT_PRECISION)
    return jnp.einsum("cdkn,...cnw->...dkw", blocks, across, precision=DFT_PRECISION)


def complex_times(left, right):
    left_re, left_im = (left[..., 0, :, :], left[..., 1, :, :])
    right_re, right_im = (right[..., 0, :, :], right[..., 1, :, :])
    return jnp.stack(
        [left_re * right_re - left_im * right_im, left_re * right_im + left_im * right_re], axis=-3
    )


def conj_times(left, right):
    left_re, left_im = (left[..., 0, :, :], left[..., 1, :, :])
    right_re, right_im = (right[..., 0, :, :], right[..., 1, :, :])
    return jnp.stack(
        [left_re * right_re + left_im * right_im, left_re * right_im - left_im * right_re], axis=-3
    )


def slot_numbers(targets, members, capacity):
    matches = (targets[:, None] == jnp.arange(members, dtype=jnp.int32)[None, :]).astype(jnp.int32)
    before = jnp.cumsum(matches, axis=0) - matches
    return targets * capacity + jnp.sum(before * matches, axis=1)


def selectors(offsets, patch_side, tile_cells, dtype):
    inner = jnp.arange(patch_side, dtype=jnp.int32)
    cells = jnp.arange(tile_cells, dtype=jnp.int32)
    hit = offsets[:, None, None] + inner[None, :, None] == cells[None, None, :]
    return hit.astype(dtype)


def cut_windows(tiles, requests, patch_side):
    tile_cells = tiles.shape[-1]
    valid = requests[:, 0].astype(jnp.bfloat16)
    row_sel = selectors(requests[:, 1], patch_side, tile_cells, jnp.bfloat16) * valid[:, None, None]
    col_sel = selectors(requests[:, 2], patch_side, tile_cells, jnp.bfloat16)
    rows = jnp.einsum("kit,sctu->kscui", row_sel, tiles, preferred_element_type=jnp.float32)
    rows = rows.astype(jnp.bfloat16)
    window = jnp.einsum("kscui,kju->kscij", rows, col_sel, preferred_element_type=jnp.float32)
    return window.astype(jnp.bfloat16)


def place_kernel(requests, peak, terms, out, total):
    step = pl.program_id(0)
    held = terms.shape[0]
    tile_cells = out.shape[-1]

    @pl.when(step == 0)
    def _():
        total[...] = jnp.zeros_like(total)

    for index in range(held):
        place_one(step * held + index, index, requests, terms, total)

    @pl.when(step == pl.num_programs(0) - 1)
    def _():
        out[...] = total[:, :, :tile_cells, :tile_cells] / peak[0, 0]


def place_one(slot, index, requests, terms, total):
    slice_count = terms.shape[1]
    patch_side = terms.shape[-1]
    row = requests[slot, 1]
    col = requests[slot, 2]
    row_base = pl.multiple_of((row // 8) * 8, 8)
    col_base = pl.multiple_of((col // 128) * 128, 128)
    row_rest = row - row_base
    col_rest = col - col_base
    band_rows = patch_side + 8
    band_cols = 2 * patch_side
    row_pick = (
        lax.broadcasted_iota(jnp.int32, (band_rows, patch_side), 0)
        == lax.broadcasted_iota(jnp.int32, (band_rows, patch_side), 1) + row_rest
    ).astype(jnp.bfloat16)
    col_pick = (
        lax.broadcasted_iota(jnp.int32, (patch_side, band_cols), 1)
        == lax.broadcasted_iota(jnp.int32, (patch_side, band_cols), 0) + col_rest
    ).astype(jnp.bfloat16)
    pieces = []
    for layer in range(slice_count):
        for part in range(2):
            term = terms[index, layer, part]
            high = term.astype(jnp.bfloat16)
            low = (term - high.astype(jnp.float32)).astype(jnp.bfloat16)
            pieces += [high, low]
    side_by_side = jnp.concatenate(pieces, axis=1)
    shifted = jnp.dot(row_pick, side_by_side, preferred_element_type=jnp.float32)
    shifted = shifted.astype(jnp.bfloat16)
    stacked = jnp.concatenate(
        [shifted[:, index * patch_side:(index + 1) * patch_side] for index in range(len(pieces))],
        axis=0,
    )
    placed = jnp.dot(stacked, col_pick, preferred_element_type=jnp.float32)
    for layer in range(slice_count):
        for part in range(2):
            index = 2 * (2 * layer + part)
            band = (
                placed[index * band_rows:(index + 1) * band_rows]
                + placed[(index + 1) * band_rows:(index + 2) * band_rows]
            )
            window = total.at[layer, part, pl.ds(row_base, band_rows), pl.ds(col_base, band_cols)]
            window[...] = window[...] + band


def accumulate(terms, requests, peak, tile_cells):
    slot_count, slice_count = terms.shape[:2]
    patch_side = terms.shape[-1]
    held = math.gcd(slot_count, 4)
    grid_spec = pltpu.PrefetchScalarGridSpec(
        num_scalar_prefetch=1,
        grid=(slot_count // held,),
        in_specs=[
            pl.BlockSpec(memory_space=pltpu.SMEM),
            pl.BlockSpec(
                (held, slice_count, 2, patch_side, patch_side), lambda k, req: (k, 0, 0, 0, 0)
            ),
        ],
        out_specs=pl.BlockSpec(
            (slice_count, 2, tile_cells, tile_cells), lambda k, req: (0, 0, 0, 0)
        ),
        scratch_shapes=[
            pltpu.VMEM(
                (slice_count, 2, tile_cells + 8, tile_cells + patch_side), jnp.float32
            )
        ],
    )
    return pl.pallas_call(
        place_kernel,
        grid_spec=grid_spec,
        out_shape=jax.ShapeDtypeStruct((slice_count, 2, tile_cells, tile_cells), jnp.float32),
        compiler_params=pltpu.CompilerParams(dimension_semantics=("arbitrary",)),
    )(requests, peak.reshape(1, 1), terms)


def group_max(value):
    count = lax.axis_size("group")
    if count & (count - 1) == 0:
        step = 1
        while step < count:
            pairs = [(index, index ^ step) for index in range(count)]
            value = jnp.maximum(value, lax.ppermute(value, "group", pairs))
            step *= 2
        return value
    running = value
    pairs = [(index, (index + 1) % count) for index in range(count)]
    for _ in range(count - 1):
        value = lax.ppermute(value, "group", pairs)
        running = jnp.maximum(running, value)
    return running


def split_pair(value):
    high = value.astype(jnp.bfloat16)
    low = (value - high.astype(jnp.float32)).astype(jnp.bfloat16)
    return high, low


def stack_three(value, axis):
    high = value.astype(jnp.bfloat16)
    low = (value - high.astype(jnp.float32)).astype(jnp.bfloat16)
    return jnp.concatenate([high, low, high], axis=axis)


def fourier_2d(fields, right_mat, left_mat):
    side = fields[0][0].shape[0]
    count = len(fields)
    rows = jnp.concatenate([jnp.concatenate([re, im], axis=1) for re, im in fields], axis=0)
    mid = jnp.dot(stack_three(rows, 1), right_mat, preferred_element_type=jnp.float32)
    parted = jnp.concatenate(
        [
            jnp.concatenate([mid[m * side:(m + 1) * side, :side] for m in range(count)], axis=1),
            jnp.concatenate([mid[m * side:(m + 1) * side, side:] for m in range(count)], axis=1),
        ],
        axis=0,
    )
    out = jnp.dot(left_mat, stack_three(parted, 0), preferred_element_type=jnp.float32)
    return [
        (out[:side, m * side:(m + 1) * side], out[side:, m * side:(m + 1) * side])
        for m in range(count)
    ]


def propagate_kernel(patch_ref, measured_ref, probe_ref, kern_ref, mats_right, mats_left,
                     peak_ref, grad_ref, probe_sum_ref):
    @pl.when(pl.program_id(0) == 0)
    def _():
        probe_sum_ref[...] = jnp.zeros_like(probe_sum_ref)

    for held in range(patch_ref.shape[0]):
        propagate_one(held, patch_ref, measured_ref, probe_ref, kern_ref, mats_right, mats_left,
                      grad_ref, probe_sum_ref)


def propagate_one(held, patch_ref, measured_ref, probe_ref, kern_ref, mats_right, mats_left,
                  grad_ref, probe_sum_ref):
    slice_count = patch_ref.shape[1]
    modes = probe_ref.shape[0]
    forward = lambda fields: fourier_2d(fields, mats_right[0], mats_left[0])
    inverse = lambda fields: fourier_2d(fields, mats_right[1], mats_left[1])
    kern_real, kern_imag = kern_ref[0], kern_ref[1]
    waves = [(probe_ref[m, 0], probe_ref[m, 1]) for m in range(modes)]
    history = []
    leaving = None
    for layer in range(slice_count):
        history.append(waves)
        patch_real = patch_ref[held, layer, 0].astype(jnp.float32)
        patch_imag = patch_ref[held, layer, 1].astype(jnp.float32)
        leaving = [
            (wr * patch_real - wi * patch_imag, wr * patch_imag + wi * patch_real)
            for wr, wi in waves
        ]
        if layer < slice_count - 1:
            spectra = forward(leaving)
            waves = inverse(
                [
                    (kern_real * fr - kern_imag * fi, kern_real * fi + kern_imag * fr)
                    for fr, fi in spectra
                ]
            )
    far = forward(leaving)
    intensity = None
    for fr, fi in far:
        power = fr * fr + fi * fi
        intensity = power if intensity is None else intensity + power
    factor = 1.0 - measured_ref[held] / jnp.sqrt(jnp.maximum(intensity, 1.0))
    back = inverse([(fr * factor, fi * factor) for fr, fi in far])
    for layer in reversed(range(slice_count)):
        grad_real = None
        grad_imag = None
        for (wr, wi), (br, bi) in zip(history[layer], back):
            term_real = wr * br + wi * bi
            term_imag = wr * bi - wi * br
            grad_real = term_real if grad_real is None else grad_real + term_real
            grad_imag = term_imag if grad_imag is None else grad_imag + term_imag
        grad_ref[held, layer, 0] = grad_real
        grad_ref[held, layer, 1] = grad_imag
        patch_real = patch_ref[held, layer, 0].astype(jnp.float32)
        patch_imag = patch_ref[held, layer, 1].astype(jnp.float32)
        back = [
            (patch_real * br + patch_imag * bi, patch_real * bi - patch_imag * br)
            for br, bi in back
        ]
        if layer > 0:
            spectra = forward(back)
            back = inverse(
                [
                    (kern_real * fr + kern_imag * fi, kern_real * fi - kern_imag * fr)
                    for fr, fi in spectra
                ]
            )

    for mode, (br, bi) in enumerate(back):
        probe_sum_ref[mode, 0] = probe_sum_ref[mode, 0] + br
        probe_sum_ref[mode, 1] = probe_sum_ref[mode, 1] + bi


def dft_mats(length):
    counter = jnp.arange(length, dtype=jnp.int32)
    product = counter[:, None] * counter[None, :] % length
    angles = product.astype(jnp.float32) * (2.0 * math.pi / length)
    norming = 1.0 / math.sqrt(length)
    cosine = jnp.cos(angles) * norming
    sine = jnp.sin(angles) * norming
    minus = jnp.concatenate(
        [jnp.concatenate([cosine, -sine], axis=1), jnp.concatenate([sine, cosine], axis=1)], axis=0
    )
    plus = jnp.concatenate(
        [jnp.concatenate([cosine, sine], axis=1), jnp.concatenate([-sine, cosine], axis=1)], axis=0
    )

    def parts(value):
        high = lax.reduce_precision(value, exponent_bits=8, mantissa_bits=7)
        return high.astype(jnp.bfloat16), (value - high).astype(jnp.bfloat16)

    def right(value):
        high, low = parts(value)
        return jnp.concatenate([high, high, low], axis=0)

    def left(value):
        high, low = parts(value)
        return jnp.concatenate([high, high, low], axis=1)

    mats_right = jnp.stack([right(minus), right(plus)])
    mats_left = jnp.stack([left(plus), left(minus)])
    return mats_right, mats_left


def propagate(patches, measured, probe_modes, prop_phase, peak):
    count, slice_count = patches.shape[:2]
    modes = probe_modes.shape[0]
    side = patches.shape[-1]
    kern = jnp.stack([jnp.cos(prop_phase), jnp.sin(prop_phase)])
    mats_right, mats_left = dft_mats(side)
    held = math.gcd(count, 4)
    whole = lambda shape: pl.BlockSpec(shape, lambda k: (0,) * len(shape))
    return pl.pallas_call(
        propagate_kernel,
        grid=(count // held,),
        in_specs=[
            pl.BlockSpec((held, slice_count, 2, side, side), lambda k: (k, 0, 0, 0, 0)),
            pl.BlockSpec((held, side, side), lambda k: (k, 0, 0)),
            whole((modes, 2, side, side)),
            whole((2, side, side)),
            whole((2, 6 * side, 2 * side)),
            whole((2, 2 * side, 6 * side)),
            pl.BlockSpec(memory_space=pltpu.SMEM),
        ],
        out_specs=[
            pl.BlockSpec((held, slice_count, 2, side, side), lambda k: (k, 0, 0, 0, 0)),
            whole((modes, 2, side, side)),
        ],
        out_shape=[
            jax.ShapeDtypeStruct((count, slice_count, 2, side, side), jnp.float32),
            jax.ShapeDtypeStruct((modes, 2, side, side), jnp.float32),
        ],
        compiler_params=pltpu.CompilerParams(dimension_semantics=("arbitrary",)),
    )(patches, measured, probe_modes, kern, mats_right, mats_left, peak.reshape(1, 1))


def member_sum(value, members):
    flat = value.reshape(members, -1)
    pieces = lax.all_to_all(flat, "member", split_axis=0, concat_axis=0, tiled=True)
    mine = jnp.sum(pieces, axis=0, keepdims=True)
    spread = jnp.broadcast_to(mine, flat.shape)
    whole = lax.all_to_all(spread, "member", split_axis=0, concat_axis=0, tiled=True)
    return whole.reshape(value.shape)


def on_device(object_field, probe_modes, prop_phase, amplitude, tile_owner, corner):
    members = lax.axis_size("member")
    pos_dev = tile_owner.shape[1]
    capacity = max(2, (2 * pos_dev + members - 1) // members)
    slot_count = members * capacity
    tile_cells = object_field.shape[2]
    patch_side = prop_phase.shape[0]
    power = jnp.max(jnp.sum(probe_modes * probe_modes, axis=(1, 2)))
    peak_power = group_max(power) + 1e-06
    flat_slots = slot_numbers(tile_owner[0, :, 0], members, capacity)
    entries = jnp.concatenate([jnp.ones((pos_dev, 1), jnp.int32), corner[0]], axis=1)
    chosen = (flat_slots[:, None] == jnp.arange(slot_count, dtype=jnp.int32)[None, :]).astype(
        jnp.int32
    )
    outgoing = jnp.sum(chosen[:, :, None] * entries[:, None, :], axis=0)
    requests = lax.all_to_all(
        outgoing.reshape(members, capacity, 3), "member", split_axis=0, concat_axis=0, tiled=True
    ).reshape(slot_count, 3)
    sent = jnp.zeros((slot_count, patch_side, patch_side), jnp.float32).at[flat_slots].set(
        amplitude[0]
    )
    measured = lax.all_to_all(
        sent.reshape(members, capacity, patch_side, patch_side),
        "member",
        split_axis=0,
        concat_axis=0,
        tiled=True,
    ).reshape(slot_count, patch_side, patch_side)
    patches = cut_windows(object_field, requests, patch_side)
    gradients, adjoint_sum = propagate(patches, measured, probe_modes[0], prop_phase, peak_power)
    probe_grad = member_sum(adjoint_sum / pos_dev, members)[None]
    object_grad = accumulate(gradients, requests, peak_power, tile_cells)
    return (object_grad, probe_grad)


def solution(mesh):
    return jax.shard_map(
        on_device,
        mesh=mesh,
        in_specs=(
            P(None, None, "group", "member"),
            P("group", None, None, None, None),
            P(),
            P("group", "member", None, None),
            P("group", "member", None),
            P("group", "member", None),
        ),
        out_specs=(P(None, None, "group", "member"), P("group", None, None, None, None)),
        check_vma=False,
    )
```

```python
from functools import partial
import math

import jax
import jax.numpy as jnp
from jax import lax
from jax.experimental import pallas as pl
from jax.experimental.pallas import tpu as pltpu
from jax.sharding import PartitionSpec as P

DFT_PRECISION = lax.Precision.HIGH


def fourier_blocks(length, sign):
    counter = jnp.arange(length, dtype=jnp.int32)
    product = counter[:, None] * counter[None, :] % length
    angles = product.astype(jnp.float32) * (2.0 * math.pi / length)
    norming = 1.0 / math.sqrt(length)
    cosine = jnp.cos(angles) * norming
    sine_part = jnp.sin(angles) * (sign * norming)
    return jnp.stack([jnp.stack([cosine, sine_part]), jnp.stack([-sine_part, cosine])])


def transform(field, blocks):
    across = jnp.einsum("...chn,cdnk->...dhk", field, blocks, precision=DFT_PRECISION)
    return jnp.einsum("cdkn,...cnw->...dkw", blocks, across, precision=DFT_PRECISION)


def complex_times(left, right):
    left_re, left_im = (left[..., 0, :, :], left[..., 1, :, :])
    right_re, right_im = (right[..., 0, :, :], right[..., 1, :, :])
    return jnp.stack(
        [left_re * right_re - left_im * right_im, left_re * right_im + left_im * right_re], axis=-3
    )


def conj_times(left, right):
    left_re, left_im = (left[..., 0, :, :], left[..., 1, :, :])
    right_re, right_im = (right[..., 0, :, :], right[..., 1, :, :])
    return jnp.stack(
        [left_re * right_re + left_im * right_im, left_re * right_im - left_im * right_re], axis=-3
    )


def slot_numbers(targets, members, capacity):
    matches = (targets[:, None] == jnp.arange(members, dtype=jnp.int32)[None, :]).astype(jnp.int32)
    before = jnp.cumsum(matches, axis=0) - matches
    return targets * capacity + jnp.sum(before * matches, axis=1)


def selectors(offsets, patch_side, tile_cells, dtype):
    inner = jnp.arange(patch_side, dtype=jnp.int32)
    cells = jnp.arange(tile_cells, dtype=jnp.int32)
    hit = offsets[:, None, None] + inner[None, :, None] == cells[None, None, :]
    return hit.astype(dtype)


def cut_windows(tiles, requests, patch_side):
    tile_cells = tiles.shape[-1]
    valid = requests[:, 0].astype(jnp.bfloat16)
    row_sel = selectors(requests[:, 1], patch_side, tile_cells, jnp.bfloat16) * valid[:, None, None]
    col_sel = selectors(requests[:, 2], patch_side, tile_cells, jnp.bfloat16)
    rows = jnp.einsum("kit,sctu->kscui", row_sel, tiles, preferred_element_type=jnp.float32)
    rows = rows.astype(jnp.bfloat16)
    window = jnp.einsum("kscui,kju->kscij", rows, col_sel, preferred_element_type=jnp.float32)
    return window.astype(jnp.bfloat16)


def place_kernel(requests, peak, terms, out, total):
    step = pl.program_id(0)
    held = terms.shape[0]
    tile_cells = out.shape[-1]

    @pl.when(step == 0)
    def _():
        total[...] = jnp.zeros_like(total)

    for index in range(held):
        place_one(step * held + index, index, requests, terms, total)

    @pl.when(step == pl.num_programs(0) - 1)
    def _():
        out[...] = total[:, :, :tile_cells, :tile_cells] / peak[0, 0]


def place_one(slot, index, requests, terms, total):
    slice_count = terms.shape[1]
    patch_side = terms.shape[-1]
    row = requests[slot, 1]
    col = requests[slot, 2]
    row_base = pl.multiple_of((row // 8) * 8, 8)
    col_base = pl.multiple_of((col // 128) * 128, 128)
    row_rest = row - row_base
    col_rest = col - col_base
    band_rows = patch_side + 8
    band_cols = 2 * patch_side
    row_pick = (
        lax.broadcasted_iota(jnp.int32, (band_rows, patch_side), 0)
        == lax.broadcasted_iota(jnp.int32, (band_rows, patch_side), 1) + row_rest
    ).astype(jnp.bfloat16)
    col_pick = (
        lax.broadcasted_iota(jnp.int32, (patch_side, band_cols), 1)
        == lax.broadcasted_iota(jnp.int32, (patch_side, band_cols), 0) + col_rest
    ).astype(jnp.bfloat16)
    pieces = []
    for layer in range(slice_count):
        for part in range(2):
            term = terms[index, layer, part]
            high = term.astype(jnp.bfloat16)
            low = (term - high.astype(jnp.float32)).astype(jnp.bfloat16)
            pieces += [high, low]
    side_by_side = jnp.concatenate(pieces, axis=1)
    shifted = jnp.dot(row_pick, side_by_side, preferred_element_type=jnp.float32)
    shifted = shifted.astype(jnp.bfloat16)
    stacked = jnp.concatenate(
        [shifted[:, index * patch_side:(index + 1) * patch_side] for index in range(len(pieces))],
        axis=0,
    )
    placed = jnp.dot(stacked, col_pick, preferred_element_type=jnp.float32)
    for layer in range(slice_count):
        for part in range(2):
            index = 2 * (2 * layer + part)
            band = (
                placed[index * band_rows:(index + 1) * band_rows]
                + placed[(index + 1) * band_rows:(index + 2) * band_rows]
            )
            window = total.at[layer, part, pl.ds(row_base, band_rows), pl.ds(col_base, band_cols)]
            window[...] = window[...] + band


def accumulate(terms, requests, peak, tile_cells):
    slot_count, slice_count = terms.shape[:2]
    patch_side = terms.shape[-1]
    held = math.gcd(slot_count, 8)
    grid_spec = pltpu.PrefetchScalarGridSpec(
        num_scalar_prefetch=1,
        grid=(slot_count // held,),
        in_specs=[
            pl.BlockSpec(memory_space=pltpu.SMEM),
            pl.BlockSpec(
                (held, slice_count, 2, patch_side, patch_side), lambda k, req: (k, 0, 0, 0, 0)
            ),
        ],
        out_specs=pl.BlockSpec(
            (slice_count, 2, tile_cells, tile_cells), lambda k, req: (0, 0, 0, 0)
        ),
        scratch_shapes=[
            pltpu.VMEM(
                (slice_count, 2, tile_cells + 8, tile_cells + patch_side), jnp.float32
            )
        ],
    )
    return pl.pallas_call(
        place_kernel,
        grid_spec=grid_spec,
        out_shape=jax.ShapeDtypeStruct((slice_count, 2, tile_cells, tile_cells), jnp.float32),
        compiler_params=pltpu.CompilerParams(dimension_semantics=("arbitrary",)),
    )(requests, peak.reshape(1, 1), terms)


def group_max(value):
    count = lax.axis_size("group")
    if count & (count - 1) == 0:
        step = 1
        while step < count:
            pairs = [(index, index ^ step) for index in range(count)]
            value = jnp.maximum(value, lax.ppermute(value, "group", pairs))
            step *= 2
        return value
    running = value
    pairs = [(index, (index + 1) % count) for index in range(count)]
    for _ in range(count - 1):
        value = lax.ppermute(value, "group", pairs)
        running = jnp.maximum(running, value)
    return running


def split_pair(value):
    high = value.astype(jnp.bfloat16)
    low = (value - high.astype(jnp.float32)).astype(jnp.bfloat16)
    return high, low


def stack_three(value, axis):
    high = value.astype(jnp.bfloat16)
    low = (value - high.astype(jnp.float32)).astype(jnp.bfloat16)
    return jnp.concatenate([high, low, high], axis=axis)


def fourier_2d(fields, right_mat, left_mat):
    side = fields[0][0].shape[0]
    count = len(fields)
    rows = jnp.concatenate([jnp.concatenate([re, im], axis=1) for re, im in fields], axis=0)
    mid = jnp.dot(stack_three(rows, 1), right_mat, preferred_element_type=jnp.float32)
    parted = jnp.concatenate(
        [
            jnp.concatenate([mid[m * side:(m + 1) * side, :side] for m in range(count)], axis=1),
            jnp.concatenate([mid[m * side:(m + 1) * side, side:] for m in range(count)], axis=1),
        ],
        axis=0,
    )
    out = jnp.dot(left_mat, stack_three(parted, 0), preferred_element_type=jnp.float32)
    return [
        (out[:side, m * side:(m + 1) * side], out[side:, m * side:(m + 1) * side])
        for m in range(count)
    ]


def propagate_kernel(patch_ref, measured_ref, probe_ref, kern_ref, mats_right, mats_left,
                     peak_ref, grad_ref, probe_sum_ref):
    @pl.when(pl.program_id(0) == 0)
    def _():
        probe_sum_ref[...] = jnp.zeros_like(probe_sum_ref)

    for held in range(patch_ref.shape[0]):
        propagate_one(held, patch_ref, measured_ref, probe_ref, kern_ref, mats_right, mats_left,
                      grad_ref, probe_sum_ref)


def propagate_one(held, patch_ref, measured_ref, probe_ref, kern_ref, mats_right, mats_left,
                  grad_ref, probe_sum_ref):
    slice_count = patch_ref.shape[1]
    modes = probe_ref.shape[0]
    forward = lambda fields: fourier_2d(fields, mats_right[0], mats_left[0])
    inverse = lambda fields: fourier_2d(fields, mats_right[1], mats_left[1])
    kern_real, kern_imag = kern_ref[0], kern_ref[1]
    waves = [(probe_ref[m, 0], probe_ref[m, 1]) for m in range(modes)]
    history = []
    leaving = None
    for layer in range(slice_count):
        history.append(waves)
        patch_real = patch_ref[held, layer, 0].astype(jnp.float32)
        patch_imag = patch_ref[held, layer, 1].astype(jnp.float32)
        leaving = [
            (wr * patch_real - wi * patch_imag, wr * patch_imag + wi * patch_real)
            for wr, wi in waves
        ]
        if layer < slice_count - 1:
            spectra = forward(leaving)
            waves = inverse(
                [
                    (kern_real * fr - kern_imag * fi, kern_real * fi + kern_imag * fr)
                    for fr, fi in spectra
                ]
            )
    far = forward(leaving)
    intensity = None
    for fr, fi in far:
        power = fr * fr + fi * fi
        intensity = power if intensity is None else intensity + power
    factor = 1.0 - measured_ref[held] / jnp.sqrt(jnp.maximum(intensity, 1.0))
    back = inverse([(fr * factor, fi * factor) for fr, fi in far])
    for layer in reversed(range(slice_count)):
        grad_real = None
        grad_imag = None
        for (wr, wi), (br, bi) in zip(history[layer], back):
            term_real = wr * br + wi * bi
            term_imag = wr * bi - wi * br
            grad_real = term_real if grad_real is None else grad_real + term_real
            grad_imag = term_imag if grad_imag is None else grad_imag + term_imag
        grad_ref[held, layer, 0] = grad_real
        grad_ref[held, layer, 1] = grad_imag
        patch_real = patch_ref[held, layer, 0].astype(jnp.float32)
        patch_imag = patch_ref[held, layer, 1].astype(jnp.float32)
        back = [
            (patch_real * br + patch_imag * bi, patch_real * bi - patch_imag * br)
            for br, bi in back
        ]
        if layer > 0:
            spectra = forward(back)
            back = inverse(
                [
                    (kern_real * fr + kern_imag * fi, kern_real * fi - kern_imag * fr)
                    for fr, fi in spectra
                ]
            )

    for mode, (br, bi) in enumerate(back):
        probe_sum_ref[mode, 0] = probe_sum_ref[mode, 0] + br
        probe_sum_ref[mode, 1] = probe_sum_ref[mode, 1] + bi


def dft_mats(length):
    counter = jnp.arange(length, dtype=jnp.int32)
    product = counter[:, None] * counter[None, :] % length
    angles = product.astype(jnp.float32) * (2.0 * math.pi / length)
    norming = 1.0 / math.sqrt(length)
    cosine = jnp.cos(angles) * norming
    sine = jnp.sin(angles) * norming
    minus = jnp.concatenate(
        [jnp.concatenate([cosine, -sine], axis=1), jnp.concatenate([sine, cosine], axis=1)], axis=0
    )
    plus = jnp.concatenate(
        [jnp.concatenate([cosine, sine], axis=1), jnp.concatenate([-sine, cosine], axis=1)], axis=0
    )

    def parts(value):
        high = lax.reduce_precision(value, exponent_bits=8, mantissa_bits=7)
        return high.astype(jnp.bfloat16), (value - high).astype(jnp.bfloat16)

    def right(value):
        high, low = parts(value)
        return jnp.concatenate([high, high, low], axis=0)

    def left(value):
        high, low = parts(value)
        return jnp.concatenate([high, high, low], axis=1)

    mats_right = jnp.stack([right(minus), right(plus)])
    mats_left = jnp.stack([left(plus), left(minus)])
    return mats_right, mats_left


def propagate(patches, measured, probe_modes, prop_phase, peak):
    count, slice_count = patches.shape[:2]
    modes = probe_modes.shape[0]
    side = patches.shape[-1]
    kern = jnp.stack([jnp.cos(prop_phase), jnp.sin(prop_phase)])
    mats_right, mats_left = dft_mats(side)
    held = math.gcd(count, 8)
    whole = lambda shape: pl.BlockSpec(shape, lambda k: (0,) * len(shape))
    return pl.pallas_call(
        propagate_kernel,
        grid=(count // held,),
        in_specs=[
            pl.BlockSpec((held, slice_count, 2, side, side), lambda k: (k, 0, 0, 0, 0)),
            pl.BlockSpec((held, side, side), lambda k: (k, 0, 0)),
            whole((modes, 2, side, side)),
            whole((2, side, side)),
            whole((2, 6 * side, 2 * side)),
            whole((2, 2 * side, 6 * side)),
            pl.BlockSpec(memory_space=pltpu.SMEM),
        ],
        out_specs=[
            pl.BlockSpec((held, slice_count, 2, side, side), lambda k: (k, 0, 0, 0, 0)),
            whole((modes, 2, side, side)),
        ],
        out_shape=[
            jax.ShapeDtypeStruct((count, slice_count, 2, side, side), jnp.float32),
            jax.ShapeDtypeStruct((modes, 2, side, side), jnp.float32),
        ],
        compiler_params=pltpu.CompilerParams(dimension_semantics=("arbitrary",)),
    )(patches, measured, probe_modes, kern, mats_right, mats_left, peak.reshape(1, 1))


def member_sum(value, members):
    flat = value.reshape(members, -1)
    pieces = lax.all_to_all(flat, "member", split_axis=0, concat_axis=0, tiled=True)
    mine = jnp.sum(pieces, axis=0, keepdims=True)
    spread = jnp.broadcast_to(mine, flat.shape)
    whole = lax.all_to_all(spread, "member", split_axis=0, concat_axis=0, tiled=True)
    return whole.reshape(value.shape)


def on_device(object_field, probe_modes, prop_phase, amplitude, tile_owner, corner):
    members = lax.axis_size("member")
    pos_dev = tile_owner.shape[1]
    capacity = max(2, (2 * pos_dev + members - 1) // members)
    slot_count = members * capacity
    tile_cells = object_field.shape[2]
    patch_side = prop_phase.shape[0]
    power = jnp.max(jnp.sum(probe_modes * probe_modes, axis=(1, 2)))
    peak_power = group_max(power) + 1e-06
    flat_slots = slot_numbers(tile_owner[0, :, 0], members, capacity)
    entries = jnp.concatenate([jnp.ones((pos_dev, 1), jnp.int32), corner[0]], axis=1)
    chosen = (flat_slots[:, None] == jnp.arange(slot_count, dtype=jnp.int32)[None, :]).astype(
        jnp.int32
    )
    outgoing = jnp.sum(chosen[:, :, None] * entries[:, None, :], axis=0)
    requests = lax.all_to_all(
        outgoing.reshape(members, capacity, 3), "member", split_axis=0, concat_axis=0, tiled=True
    ).reshape(slot_count, 3)
    sent = jnp.zeros((slot_count, patch_side, patch_side), jnp.float32).at[flat_slots].set(
        amplitude[0]
    )
    measured = lax.all_to_all(
        sent.reshape(members, capacity, patch_side, patch_side),
        "member",
        split_axis=0,
        concat_axis=0,
        tiled=True,
    ).reshape(slot_count, patch_side, patch_side)
    patches = cut_windows(object_field, requests, patch_side)
    gradients, adjoint_sum = propagate(patches, measured, probe_modes[0], prop_phase, peak_power)
    probe_grad = member_sum(adjoint_sum / pos_dev, members)[None]
    object_grad = accumulate(gradients, requests, peak_power, tile_cells)
    return (object_grad, probe_grad)


def solution(mesh):
    return jax.shard_map(
        on_device,
        mesh=mesh,
        in_specs=(
            P(None, None, "group", "member"),
            P("group", None, None, None, None),
            P(),
            P("group", "member", None, None),
            P("group", "member", None),
            P("group", "member", None),
        ),
        out_specs=(P(None, None, "group", "member"), P("group", None, None, None, None)),
        check_vma=False,
    )
```

```python
from functools import partial
import math

import jax
import jax.numpy as jnp
from jax import lax
from jax.experimental import pallas as pl
from jax.experimental.pallas import tpu as pltpu
from jax.sharding import PartitionSpec as P

DFT_PRECISION = lax.Precision.HIGH


def fourier_blocks(length, sign):
    counter = jnp.arange(length, dtype=jnp.int32)
    product = counter[:, None] * counter[None, :] % length
    angles = product.astype(jnp.float32) * (2.0 * math.pi / length)
    norming = 1.0 / math.sqrt(length)
    cosine = jnp.cos(angles) * norming
    sine_part = jnp.sin(angles) * (sign * norming)
    return jnp.stack([jnp.stack([cosine, sine_part]), jnp.stack([-sine_part, cosine])])


def transform(field, blocks):
    across = jnp.einsum("...chn,cdnk->...dhk", field, blocks, precision=DFT_PRECISION)
    return jnp.einsum("cdkn,...cnw->...dkw", blocks, across, precision=DFT_PRECISION)


def complex_times(left, right):
    left_re, left_im = (left[..., 0, :, :], left[..., 1, :, :])
    right_re, right_im = (right[..., 0, :, :], right[..., 1, :, :])
    return jnp.stack(
        [left_re * right_re - left_im * right_im, left_re * right_im + left_im * right_re], axis=-3
    )


def conj_times(left, right):
    left_re, left_im = (left[..., 0, :, :], left[..., 1, :, :])
    right_re, right_im = (right[..., 0, :, :], right[..., 1, :, :])
    return jnp.stack(
        [left_re * right_re + left_im * right_im, left_re * right_im - left_im * right_re], axis=-3
    )


def slot_numbers(targets, members, capacity):
    matches = (targets[:, None] == jnp.arange(members, dtype=jnp.int32)[None, :]).astype(jnp.int32)
    before = jnp.cumsum(matches, axis=0) - matches
    return targets * capacity + jnp.sum(before * matches, axis=1)


def selectors(offsets, patch_side, tile_cells, dtype):
    inner = jnp.arange(patch_side, dtype=jnp.int32)
    cells = jnp.arange(tile_cells, dtype=jnp.int32)
    hit = offsets[:, None, None] + inner[None, :, None] == cells[None, None, :]
    return hit.astype(dtype)


def cut_windows(tiles, requests, patch_side):
    tile_cells = tiles.shape[-1]
    valid = requests[:, 0].astype(jnp.bfloat16)
    row_sel = selectors(requests[:, 1], patch_side, tile_cells, jnp.bfloat16) * valid[:, None, None]
    col_sel = selectors(requests[:, 2], patch_side, tile_cells, jnp.bfloat16)
    rows = jnp.einsum("kit,sctu->kscui", row_sel, tiles, preferred_element_type=jnp.float32)
    rows = rows.astype(jnp.bfloat16)
    window = jnp.einsum("kscui,kju->kscij", rows, col_sel, preferred_element_type=jnp.float32)
    return window.astype(jnp.bfloat16)


def place_kernel(requests, peak, terms, out, total):
    step = pl.program_id(0)
    held = terms.shape[0]
    tile_cells = out.shape[-1]

    @pl.when(step == 0)
    def _():
        total[...] = jnp.zeros_like(total)

    for index in range(held):
        place_one(step * held + index, index, requests, terms, total)

    @pl.when(step == pl.num_programs(0) - 1)
    def _():
        out[...] = total[:, :, :tile_cells, :tile_cells] / peak[0, 0]


def place_one(slot, index, requests, terms, total):
    slice_count = terms.shape[1]
    patch_side = terms.shape[-1]
    row = requests[slot, 1]
    col = requests[slot, 2]
    row_base = pl.multiple_of((row // 8) * 8, 8)
    col_base = pl.multiple_of((col // 128) * 128, 128)
    row_rest = row - row_base
    col_rest = col - col_base
    band_rows = patch_side + 8
    band_cols = 2 * patch_side
    row_pick = (
        lax.broadcasted_iota(jnp.int32, (band_rows, patch_side), 0)
        == lax.broadcasted_iota(jnp.int32, (band_rows, patch_side), 1) + row_rest
    ).astype(jnp.bfloat16)
    col_pick = (
        lax.broadcasted_iota(jnp.int32, (patch_side, band_cols), 1)
        == lax.broadcasted_iota(jnp.int32, (patch_side, band_cols), 0) + col_rest
    ).astype(jnp.bfloat16)
    pieces = []
    for layer in range(slice_count):
        for part in range(2):
            term = terms[index, layer, part]
            high = term.astype(jnp.bfloat16)
            low = (term - high.astype(jnp.float32)).astype(jnp.bfloat16)
            pieces += [high, low]
    side_by_side = jnp.concatenate(pieces, axis=1)
    shifted = jnp.dot(row_pick, side_by_side, preferred_element_type=jnp.float32)
    shifted = shifted.astype(jnp.bfloat16)
    stacked = jnp.concatenate(
        [shifted[:, index * patch_side:(index + 1) * patch_side] for index in range(len(pieces))],
        axis=0,
    )
    placed = jnp.dot(stacked, col_pick, preferred_element_type=jnp.float32)
    for layer in range(slice_count):
        for part in range(2):
            index = 2 * (2 * layer + part)
            band = (
                placed[index * band_rows:(index + 1) * band_rows]
                + placed[(index + 1) * band_rows:(index + 2) * band_rows]
            )
            window = total.at[layer, part, pl.ds(row_base, band_rows), pl.ds(col_base, band_cols)]
            window[...] = window[...] + band


def accumulate(terms, requests, peak, tile_cells):
    slot_count, slice_count = terms.shape[:2]
    patch_side = terms.shape[-1]
    held = math.gcd(slot_count, 8)
    grid_spec = pltpu.PrefetchScalarGridSpec(
        num_scalar_prefetch=1,
        grid=(slot_count // held,),
        in_specs=[
            pl.BlockSpec(memory_space=pltpu.SMEM),
            pl.BlockSpec(
                (held, slice_count, 2, patch_side, patch_side), lambda k, req: (k, 0, 0, 0, 0)
            ),
        ],
        out_specs=pl.BlockSpec(
            (slice_count, 2, tile_cells, tile_cells), lambda k, req: (0, 0, 0, 0)
        ),
        scratch_shapes=[
            pltpu.VMEM(
                (slice_count, 2, tile_cells + 8, tile_cells + patch_side), jnp.float32
            )
        ],
    )
    return pl.pallas_call(
        place_kernel,
        grid_spec=grid_spec,
        out_shape=jax.ShapeDtypeStruct((slice_count, 2, tile_cells, tile_cells), jnp.float32),
        compiler_params=pltpu.CompilerParams(dimension_semantics=("arbitrary",)),
    )(requests, peak.reshape(1, 1), terms)


def group_max(value):
    count = lax.axis_size("group")
    if count & (count - 1) == 0:
        step = 1
        while step < count:
            pairs = [(index, index ^ step) for index in range(count)]
            value = jnp.maximum(value, lax.ppermute(value, "group", pairs))
            step *= 2
        return value
    running = value
    pairs = [(index, (index + 1) % count) for index in range(count)]
    for _ in range(count - 1):
        value = lax.ppermute(value, "group", pairs)
        running = jnp.maximum(running, value)
    return running


def split_pair(value):
    high = value.astype(jnp.bfloat16)
    low = (value - high.astype(jnp.float32)).astype(jnp.bfloat16)
    return high, low


def stack_three(value, axis):
    high = value.astype(jnp.bfloat16)
    low = (value - high.astype(jnp.float32)).astype(jnp.bfloat16)
    return jnp.concatenate([high, low, high], axis=axis)


def fourier_2d(fields, right_mat, left_mat):
    side = fields[0][0].shape[0]
    count = len(fields)
    rows = jnp.concatenate([jnp.concatenate([re, im], axis=1) for re, im in fields], axis=0)
    mid = jnp.dot(stack_three(rows, 1), right_mat, preferred_element_type=jnp.float32)
    parted = jnp.concatenate(
        [
            jnp.concatenate([mid[m * side:(m + 1) * side, :side] for m in range(count)], axis=1),
            jnp.concatenate([mid[m * side:(m + 1) * side, side:] for m in range(count)], axis=1),
        ],
        axis=0,
    )
    out = jnp.dot(left_mat, stack_three(parted, 0), preferred_element_type=jnp.float32)
    return [
        (out[:side, m * side:(m + 1) * side], out[side:, m * side:(m + 1) * side])
        for m in range(count)
    ]


def propagate_kernel(patch_ref, measured_ref, probe_ref, kern_ref, mats_right, mats_left,
                     peak_ref, grad_ref, probe_sum_ref):
    @pl.when(pl.program_id(0) == 0)
    def _():
        probe_sum_ref[...] = jnp.zeros_like(probe_sum_ref)

    for held in range(patch_ref.shape[0]):
        propagate_one(held, patch_ref, measured_ref, probe_ref, kern_ref, mats_right, mats_left,
                      grad_ref, probe_sum_ref)


def propagate_one(held, patch_ref, measured_ref, probe_ref, kern_ref, mats_right, mats_left,
                  grad_ref, probe_sum_ref):
    slice_count = patch_ref.shape[1]
    modes = probe_ref.shape[0]
    forward = lambda fields: fourier_2d(fields, mats_right[0], mats_left[0])
    inverse = lambda fields: fourier_2d(fields, mats_right[1], mats_left[1])
    kern_real, kern_imag = kern_ref[0], kern_ref[1]
    waves = [(probe_ref[m, 0], probe_ref[m, 1]) for m in range(modes)]
    history = []
    leaving = None
    for layer in range(slice_count):
        history.append(waves)
        patch_real = patch_ref[held, layer, 0].astype(jnp.float32)
        patch_imag = patch_ref[held, layer, 1].astype(jnp.float32)
        leaving = [
            (wr * patch_real - wi * patch_imag, wr * patch_imag + wi * patch_real)
            for wr, wi in waves
        ]
        if layer < slice_count - 1:
            spectra = forward(leaving)
            waves = inverse(
                [
                    (kern_real * fr - kern_imag * fi, kern_real * fi + kern_imag * fr)
                    for fr, fi in spectra
                ]
            )
    far = forward(leaving)
    intensity = None
    for fr, fi in far:
        power = fr * fr + fi * fi
        intensity = power if intensity is None else intensity + power
    factor = 1.0 - measured_ref[held] / jnp.sqrt(jnp.maximum(intensity, 1.0))
    back = inverse([(fr * factor, fi * factor) for fr, fi in far])
    for layer in reversed(range(slice_count)):
        grad_real = None
        grad_imag = None
        for (wr, wi), (br, bi) in zip(history[layer], back):
            term_real = wr * br + wi * bi
            term_imag = wr * bi - wi * br
            grad_real = term_real if grad_real is None else grad_real + term_real
            grad_imag = term_imag if grad_imag is None else grad_imag + term_imag
        grad_ref[held, layer, 0] = grad_real
        grad_ref[held, layer, 1] = grad_imag
        patch_real = patch_ref[held, layer, 0].astype(jnp.float32)
        patch_imag = patch_ref[held, layer, 1].astype(jnp.float32)
        back = [
            (patch_real * br + patch_imag * bi, patch_real * bi - patch_imag * br)
            for br, bi in back
        ]
        if layer > 0:
            spectra = forward(back)
            back = inverse(
                [
                    (kern_real * fr + kern_imag * fi, kern_real * fi - kern_imag * fr)
                    for fr, fi in spectra
                ]
            )

    for mode, (br, bi) in enumerate(back):
        probe_sum_ref[mode, 0] = probe_sum_ref[mode, 0] + br
        probe_sum_ref[mode, 1] = probe_sum_ref[mode, 1] + bi


def dft_mats(length):
    counter = jnp.arange(length, dtype=jnp.int32)
    product = counter[:, None] * counter[None, :] % length
    angles = product.astype(jnp.float32) * (2.0 * math.pi / length)
    norming = 1.0 / math.sqrt(length)
    cosine = jnp.cos(angles) * norming
    sine = jnp.sin(angles) * norming
    minus = jnp.concatenate(
        [jnp.concatenate([cosine, -sine], axis=1), jnp.concatenate([sine, cosine], axis=1)], axis=0
    )
    plus = jnp.concatenate(
        [jnp.concatenate([cosine, sine], axis=1), jnp.concatenate([-sine, cosine], axis=1)], axis=0
    )

    def parts(value):
        high = lax.reduce_precision(value, exponent_bits=8, mantissa_bits=7)
        return high.astype(jnp.bfloat16), (value - high).astype(jnp.bfloat16)

    def right(value):
        high, low = parts(value)
        return jnp.concatenate([high, high, low], axis=0)

    def left(value):
        high, low = parts(value)
        return jnp.concatenate([high, high, low], axis=1)

    mats_right = jnp.stack([right(minus), right(plus)])
    mats_left = jnp.stack([left(plus), left(minus)])
    return mats_right, mats_left


def propagate(patches, measured, probe_modes, prop_phase, peak):
    count, slice_count = patches.shape[:2]
    modes = probe_modes.shape[0]
    side = patches.shape[-1]
    kern = jnp.stack([jnp.cos(prop_phase), jnp.sin(prop_phase)])
    mats_right, mats_left = dft_mats(side)
    held = math.gcd(count, 8)
    whole = lambda shape: pl.BlockSpec(shape, lambda k: (0,) * len(shape))
    return pl.pallas_call(
        propagate_kernel,
        grid=(count // held,),
        in_specs=[
            pl.BlockSpec((held, slice_count, 2, side, side), lambda k: (k, 0, 0, 0, 0)),
            pl.BlockSpec((held, side, side), lambda k: (k, 0, 0)),
            whole((modes, 2, side, side)),
            whole((2, side, side)),
            whole((2, 6 * side, 2 * side)),
            whole((2, 2 * side, 6 * side)),
            pl.BlockSpec(memory_space=pltpu.SMEM),
        ],
        out_specs=[
            pl.BlockSpec((held, slice_count, 2, side, side), lambda k: (k, 0, 0, 0, 0)),
            whole((modes, 2, side, side)),
        ],
        out_shape=[
            jax.ShapeDtypeStruct((count, slice_count, 2, side, side), jnp.float32),
            jax.ShapeDtypeStruct((modes, 2, side, side), jnp.float32),
        ],
        compiler_params=pltpu.CompilerParams(dimension_semantics=("arbitrary",)),
    )(patches, measured, probe_modes, kern, mats_right, mats_left, peak.reshape(1, 1))


def member_sum(value, members):
    flat = value.reshape(members, -1)
    pieces = lax.all_to_all(flat, "member", split_axis=0, concat_axis=0, tiled=True)
    mine = jnp.sum(pieces, axis=0, keepdims=True)
    spread = jnp.broadcast_to(mine, flat.shape)
    whole = lax.all_to_all(spread, "member", split_axis=0, concat_axis=0, tiled=True)
    return whole.reshape(value.shape)


def on_device(object_field, probe_modes, prop_phase, amplitude, tile_owner, corner):
    members = lax.axis_size("member")
    pos_dev = tile_owner.shape[1]
    capacity = max(2, (2 * pos_dev + members - 1) // members)
    slot_count = members * capacity
    tile_cells = object_field.shape[2]
    patch_side = prop_phase.shape[0]
    power = jnp.max(jnp.sum(probe_modes * probe_modes, axis=(1, 2)))
    peak_power = group_max(power) + 1e-06
    flat_slots = slot_numbers(tile_owner[0, :, 0], members, capacity)
    listed = lax.all_gather(jnp.concatenate([tile_owner[0], corner[0]], axis=1), "member")
    owners, corners = listed[:, :, 0], listed[:, :, 1:]
    ranks = jax.vmap(lambda row: slot_numbers(row, members, capacity) - row * capacity)(owners)
    senders = jnp.arange(members, dtype=jnp.int32)[:, None]
    mine = (owners == lax.axis_index("member")).reshape(-1)
    targets = (senders * capacity + ranks).reshape(-1)
    entries = jnp.concatenate(
        [jnp.ones((members * pos_dev, 1), jnp.int32), corners.reshape(members * pos_dev, 2)], axis=1
    )
    chosen = (
        (targets[:, None] == jnp.arange(slot_count, dtype=jnp.int32)[None, :]) & mine[:, None]
    ).astype(jnp.int32)
    requests = jnp.sum(chosen[:, :, None] * entries[:, None, :], axis=0)
    sent = jnp.zeros((slot_count, patch_side, patch_side), jnp.float32).at[flat_slots].set(
        amplitude[0]
    )
    measured = lax.all_to_all(
        sent.reshape(members, capacity, patch_side, patch_side),
        "member",
        split_axis=0,
        concat_axis=0,
        tiled=True,
    ).reshape(slot_count, patch_side, patch_side)
    patches = cut_windows(object_field, requests, patch_side)
    gradients, adjoint_sum = propagate(patches, measured, probe_modes[0], prop_phase, peak_power)
    probe_grad = member_sum(adjoint_sum / pos_dev, members)[None]
    object_grad = accumulate(gradients, requests, peak_power, tile_cells)
    return (object_grad, probe_grad)


def solution(mesh):
    return jax.shard_map(
        on_device,
        mesh=mesh,
        in_specs=(
            P(None, None, "group", "member"),
            P("group", None, None, None, None),
            P(),
            P("group", "member", None, None),
            P("group", "member", None),
            P("group", "member", None),
        ),
        out_specs=(P(None, None, "group", "member"), P("group", None, None, None, None)),
        check_vma=False,
    )
```

```python
from functools import partial
import math

import jax
import jax.numpy as jnp
from jax import lax
from jax.experimental import pallas as pl
from jax.experimental.pallas import tpu as pltpu
from jax.sharding import PartitionSpec as P

DFT_PRECISION = lax.Precision.HIGH


def fourier_blocks(length, sign):
    counter = jnp.arange(length, dtype=jnp.int32)
    product = counter[:, None] * counter[None, :] % length
    angles = product.astype(jnp.float32) * (2.0 * math.pi / length)
    norming = 1.0 / math.sqrt(length)
    cosine = jnp.cos(angles) * norming
    sine_part = jnp.sin(angles) * (sign * norming)
    return jnp.stack([jnp.stack([cosine, sine_part]), jnp.stack([-sine_part, cosine])])


def transform(field, blocks):
    across = jnp.einsum("...chn,cdnk->...dhk", field, blocks, precision=DFT_PRECISION)
    return jnp.einsum("cdkn,...cnw->...dkw", blocks, across, precision=DFT_PRECISION)


def complex_times(left, right):
    left_re, left_im = (left[..., 0, :, :], left[..., 1, :, :])
    right_re, right_im = (right[..., 0, :, :], right[..., 1, :, :])
    return jnp.stack(
        [left_re * right_re - left_im * right_im, left_re * right_im + left_im * right_re], axis=-3
    )


def conj_times(left, right):
    left_re, left_im = (left[..., 0, :, :], left[..., 1, :, :])
    right_re, right_im = (right[..., 0, :, :], right[..., 1, :, :])
    return jnp.stack(
        [left_re * right_re + left_im * right_im, left_re * right_im - left_im * right_re], axis=-3
    )


def slot_numbers(targets, members, capacity):
    matches = (targets[:, None] == jnp.arange(members, dtype=jnp.int32)[None, :]).astype(jnp.int32)
    before = jnp.cumsum(matches, axis=0) - matches
    return targets * capacity + jnp.sum(before * matches, axis=1)


def selectors(offsets, patch_side, tile_cells, dtype):
    inner = jnp.arange(patch_side, dtype=jnp.int32)
    cells = jnp.arange(tile_cells, dtype=jnp.int32)
    hit = offsets[:, None, None] + inner[None, :, None] == cells[None, None, :]
    return hit.astype(dtype)


def cut_windows(tiles, requests, patch_side):
    tile_cells = tiles.shape[-1]
    valid = requests[:, 0].astype(jnp.bfloat16)
    row_sel = selectors(requests[:, 1], patch_side, tile_cells, jnp.bfloat16) * valid[:, None, None]
    col_sel = selectors(requests[:, 2], patch_side, tile_cells, jnp.bfloat16)
    rows = jnp.einsum("kit,sctu->kscui", row_sel, tiles, preferred_element_type=jnp.float32)
    rows = rows.astype(jnp.bfloat16)
    window = jnp.einsum("kscui,kju->kscij", rows, col_sel, preferred_element_type=jnp.float32)
    return window.astype(jnp.bfloat16)


def place_kernel(requests, peak, terms, out, total):
    step = pl.program_id(0)
    held = terms.shape[0]
    tile_cells = out.shape[-1]

    @pl.when(step == 0)
    def _():
        total[...] = jnp.zeros_like(total)

    for index in range(held):
        place_one(step * held + index, index, requests, terms, total)

    @pl.when(step == pl.num_programs(0) - 1)
    def _():
        out[...] = total[:, :, :tile_cells, :tile_cells] / peak[0, 0]


def place_one(slot, index, requests, terms, total):
    slice_count = terms.shape[1]
    patch_side = terms.shape[-1]
    row = requests[slot, 1]
    col = requests[slot, 2]
    row_base = pl.multiple_of((row // 8) * 8, 8)
    col_base = pl.multiple_of((col // 128) * 128, 128)
    row_rest = row - row_base
    col_rest = col - col_base
    band_rows = patch_side + 8
    band_cols = 2 * patch_side
    row_pick = (
        lax.broadcasted_iota(jnp.int32, (band_rows, patch_side), 0)
        == lax.broadcasted_iota(jnp.int32, (band_rows, patch_side), 1) + row_rest
    ).astype(jnp.bfloat16)
    col_pick = (
        lax.broadcasted_iota(jnp.int32, (patch_side, band_cols), 1)
        == lax.broadcasted_iota(jnp.int32, (patch_side, band_cols), 0) + col_rest
    ).astype(jnp.bfloat16)
    pieces = []
    for layer in range(slice_count):
        for part in range(2):
            term = terms[index, layer, part]
            high = term.astype(jnp.bfloat16)
            low = (term - high.astype(jnp.float32)).astype(jnp.bfloat16)
            pieces += [high, low]
    side_by_side = jnp.concatenate(pieces, axis=1)
    shifted = jnp.dot(row_pick, side_by_side, preferred_element_type=jnp.float32)
    shifted = shifted.astype(jnp.bfloat16)
    stacked = jnp.concatenate(
        [shifted[:, index * patch_side:(index + 1) * patch_side] for index in range(len(pieces))],
        axis=0,
    )
    placed = jnp.dot(stacked, col_pick, preferred_element_type=jnp.float32)
    for layer in range(slice_count):
        for part in range(2):
            index = 2 * (2 * layer + part)
            band = (
                placed[index * band_rows:(index + 1) * band_rows]
                + placed[(index + 1) * band_rows:(index + 2) * band_rows]
            )
            window = total.at[layer, part, pl.ds(row_base, band_rows), pl.ds(col_base, band_cols)]
            window[...] = window[...] + band


def accumulate(terms, requests, peak, tile_cells):
    slot_count, slice_count = terms.shape[:2]
    patch_side = terms.shape[-1]
    held = math.gcd(slot_count, 8)
    grid_spec = pltpu.PrefetchScalarGridSpec(
        num_scalar_prefetch=1,
        grid=(slot_count // held,),
        in_specs=[
            pl.BlockSpec(memory_space=pltpu.SMEM),
            pl.BlockSpec(
                (held, slice_count, 2, patch_side, patch_side), lambda k, req: (k, 0, 0, 0, 0)
            ),
        ],
        out_specs=pl.BlockSpec(
            (slice_count, 2, tile_cells, tile_cells), lambda k, req: (0, 0, 0, 0)
        ),
        scratch_shapes=[
            pltpu.VMEM(
                (slice_count, 2, tile_cells + 8, tile_cells + patch_side), jnp.float32
            )
        ],
    )
    return pl.pallas_call(
        place_kernel,
        grid_spec=grid_spec,
        out_shape=jax.ShapeDtypeStruct((slice_count, 2, tile_cells, tile_cells), jnp.float32),
        compiler_params=pltpu.CompilerParams(dimension_semantics=("arbitrary",)),
    )(requests, peak.reshape(1, 1), terms)


def group_max(value):
    count = lax.axis_size("group")
    if count & (count - 1) == 0:
        step = 1
        while step < count:
            pairs = [(index, index ^ step) for index in range(count)]
            value = jnp.maximum(value, lax.ppermute(value, "group", pairs))
            step *= 2
        return value
    running = value
    pairs = [(index, (index + 1) % count) for index in range(count)]
    for _ in range(count - 1):
        value = lax.ppermute(value, "group", pairs)
        running = jnp.maximum(running, value)
    return running


def split_pair(value):
    high = value.astype(jnp.bfloat16)
    low = (value - high.astype(jnp.float32)).astype(jnp.bfloat16)
    return high, low


def stack_three(value, axis):
    high = value.astype(jnp.bfloat16)
    low = (value - high.astype(jnp.float32)).astype(jnp.bfloat16)
    return jnp.concatenate([high, low, high], axis=axis)


def fourier_2d(fields, right_mat, left_mat):
    side = fields[0][0].shape[0]
    count = len(fields)
    rows = jnp.concatenate([jnp.concatenate([re, im], axis=1) for re, im in fields], axis=0)
    mid = jnp.dot(stack_three(rows, 1), right_mat, preferred_element_type=jnp.float32)
    parted = jnp.concatenate(
        [
            jnp.concatenate([mid[m * side:(m + 1) * side, :side] for m in range(count)], axis=1),
            jnp.concatenate([mid[m * side:(m + 1) * side, side:] for m in range(count)], axis=1),
        ],
        axis=0,
    )
    out = jnp.dot(left_mat, stack_three(parted, 0), preferred_element_type=jnp.float32)
    return [
        (out[:side, m * side:(m + 1) * side], out[side:, m * side:(m + 1) * side])
        for m in range(count)
    ]


def propagate_kernel(patch_ref, measured_ref, probe_ref, kern_ref, mats_right, mats_left,
                     peak_ref, grad_ref, probe_sum_ref):
    @pl.when(pl.program_id(0) == 0)
    def _():
        probe_sum_ref[...] = jnp.zeros_like(probe_sum_ref)

    for held in range(patch_ref.shape[0]):
        propagate_one(held, patch_ref, measured_ref, probe_ref, kern_ref, mats_right, mats_left,
                      grad_ref, probe_sum_ref)


def propagate_one(held, patch_ref, measured_ref, probe_ref, kern_ref, mats_right, mats_left,
                  grad_ref, probe_sum_ref):
    slice_count = patch_ref.shape[1]
    modes = probe_ref.shape[0]
    forward = lambda fields: fourier_2d(fields, mats_right[0], mats_left[0])
    inverse = lambda fields: fourier_2d(fields, mats_right[1], mats_left[1])
    kern_real, kern_imag = kern_ref[0], kern_ref[1]
    waves = [(probe_ref[m, 0], probe_ref[m, 1]) for m in range(modes)]
    history = []
    leaving = None
    for layer in range(slice_count):
        history.append(waves)
        patch_real = patch_ref[held, layer, 0].astype(jnp.float32)
        patch_imag = patch_ref[held, layer, 1].astype(jnp.float32)
        leaving = [
            (wr * patch_real - wi * patch_imag, wr * patch_imag + wi * patch_real)
            for wr, wi in waves
        ]
        if layer < slice_count - 1:
            spectra = forward(leaving)
            waves = inverse(
                [
                    (kern_real * fr - kern_imag * fi, kern_real * fi + kern_imag * fr)
                    for fr, fi in spectra
                ]
            )
    far = forward(leaving)
    intensity = None
    for fr, fi in far:
        power = fr * fr + fi * fi
        intensity = power if intensity is None else intensity + power
    factor = 1.0 - measured_ref[held] / jnp.sqrt(jnp.maximum(intensity, 1.0))
    back = inverse([(fr * factor, fi * factor) for fr, fi in far])
    for layer in reversed(range(slice_count)):
        grad_real = None
        grad_imag = None
        for (wr, wi), (br, bi) in zip(history[layer], back):
            term_real = wr * br + wi * bi
            term_imag = wr * bi - wi * br
            grad_real = term_real if grad_real is None else grad_real + term_real
            grad_imag = term_imag if grad_imag is None else grad_imag + term_imag
        grad_ref[held, layer, 0] = grad_real
        grad_ref[held, layer, 1] = grad_imag
        patch_real = patch_ref[held, layer, 0].astype(jnp.float32)
        patch_imag = patch_ref[held, layer, 1].astype(jnp.float32)
        back = [
            (patch_real * br + patch_imag * bi, patch_real * bi - patch_imag * br)
            for br, bi in back
        ]
        if layer > 0:
            spectra = forward(back)
            back = inverse(
                [
                    (kern_real * fr + kern_imag * fi, kern_real * fi - kern_imag * fr)
                    for fr, fi in spectra
                ]
            )

    for mode, (br, bi) in enumerate(back):
        probe_sum_ref[mode, 0] = probe_sum_ref[mode, 0] + br
        probe_sum_ref[mode, 1] = probe_sum_ref[mode, 1] + bi


def dft_mats(length):
    counter = jnp.arange(length, dtype=jnp.int32)
    product = counter[:, None] * counter[None, :] % length
    angles = product.astype(jnp.float32) * (2.0 * math.pi / length)
    norming = 1.0 / math.sqrt(length)
    cosine = jnp.cos(angles) * norming
    sine = jnp.sin(angles) * norming
    minus = jnp.concatenate(
        [jnp.concatenate([cosine, -sine], axis=1), jnp.concatenate([sine, cosine], axis=1)], axis=0
    )
    plus = jnp.concatenate(
        [jnp.concatenate([cosine, sine], axis=1), jnp.concatenate([-sine, cosine], axis=1)], axis=0
    )

    def parts(value):
        high = lax.reduce_precision(value, exponent_bits=8, mantissa_bits=7)
        return high.astype(jnp.bfloat16), (value - high).astype(jnp.bfloat16)

    def right(value):
        high, low = parts(value)
        return jnp.concatenate([high, high, low], axis=0)

    def left(value):
        high, low = parts(value)
        return jnp.concatenate([high, high, low], axis=1)

    mats_right = jnp.stack([right(minus), right(plus)])
    mats_left = jnp.stack([left(plus), left(minus)])
    return mats_right, mats_left


def propagate(patches, measured, probe_modes, prop_phase, peak):
    count, slice_count = patches.shape[:2]
    modes = probe_modes.shape[0]
    side = patches.shape[-1]
    kern = jnp.stack([jnp.cos(prop_phase), jnp.sin(prop_phase)])
    mats_right, mats_left = dft_mats(side)
    held = math.gcd(count, 8)
    whole = lambda shape: pl.BlockSpec(shape, lambda k: (0,) * len(shape))
    return pl.pallas_call(
        propagate_kernel,
        grid=(count // held,),
        in_specs=[
            pl.BlockSpec((held, slice_count, 2, side, side), lambda k: (k, 0, 0, 0, 0)),
            pl.BlockSpec((held, side, side), lambda k: (k, 0, 0)),
            whole((modes, 2, side, side)),
            whole((2, side, side)),
            whole((2, 6 * side, 2 * side)),
            whole((2, 2 * side, 6 * side)),
            pl.BlockSpec(memory_space=pltpu.SMEM),
        ],
        out_specs=[
            pl.BlockSpec((held, slice_count, 2, side, side), lambda k: (k, 0, 0, 0, 0)),
            whole((modes, 2, side, side)),
        ],
        out_shape=[
            jax.ShapeDtypeStruct((count, slice_count, 2, side, side), jnp.float32),
            jax.ShapeDtypeStruct((modes, 2, side, side), jnp.float32),
        ],
        compiler_params=pltpu.CompilerParams(dimension_semantics=("arbitrary",)),
    )(patches, measured, probe_modes, kern, mats_right, mats_left, peak.reshape(1, 1))


def member_sum(value, members):
    flat = value.reshape(members, -1)
    pieces = lax.all_to_all(flat, "member", split_axis=0, concat_axis=0, tiled=True)
    mine = jnp.sum(pieces, axis=0, keepdims=True)
    spread = jnp.broadcast_to(mine, flat.shape)
    whole = lax.all_to_all(spread, "member", split_axis=0, concat_axis=0, tiled=True)
    return whole.reshape(value.shape)


def on_device(object_field, probe_modes, prop_phase, amplitude, tile_owner, corner):
    members = lax.axis_size("member")
    pos_dev = tile_owner.shape[1]
    capacity = max(2, (2 * pos_dev + members - 1) // members)
    slot_count = members * capacity
    tile_cells = object_field.shape[2]
    patch_side = prop_phase.shape[0]
    power = jnp.max(jnp.sum(probe_modes * probe_modes, axis=(1, 2)))
    peak_power = group_max(power) + 1e-06
    flat_slots = slot_numbers(tile_owner[0, :, 0], members, capacity)
    listed = lax.all_gather(jnp.concatenate([tile_owner[0], corner[0]], axis=1), "member")
    owners, corners = listed[:, :, 0], listed[:, :, 1:]
    ranks = jax.vmap(lambda row: slot_numbers(row, members, capacity) - row * capacity)(owners)
    senders = jnp.arange(members, dtype=jnp.int32)[:, None]
    mine = (owners == lax.axis_index("member")).reshape(-1)
    targets = (senders * capacity + ranks).reshape(-1)
    entries = jnp.concatenate(
        [jnp.ones((members * pos_dev, 1), jnp.int32), corners.reshape(members * pos_dev, 2)], axis=1
    )
    chosen = (
        (targets[:, None] == jnp.arange(slot_count, dtype=jnp.int32)[None, :]) & mine[:, None]
    ).astype(jnp.int32)
    requests = jnp.sum(chosen[:, :, None] * entries[:, None, :], axis=0)
    after_gather = jnp.min(listed).astype(jnp.float32) * 0.0
    sent = jnp.zeros((slot_count, patch_side, patch_side), jnp.float32).at[flat_slots].set(
        amplitude[0] + after_gather
    )
    measured = lax.all_to_all(
        sent.reshape(members, capacity, patch_side, patch_side),
        "member",
        split_axis=0,
        concat_axis=0,
        tiled=True,
    ).reshape(slot_count, patch_side, patch_side)
    patches = cut_windows(object_field, requests, patch_side)
    gradients, adjoint_sum = propagate(patches, measured, probe_modes[0], prop_phase, peak_power)
    probe_grad = member_sum(adjoint_sum / pos_dev, members)[None]
    object_grad = accumulate(gradients, requests, peak_power, tile_cells)
    return (object_grad, probe_grad)


def solution(mesh):
    return jax.shard_map(
        on_device,
        mesh=mesh,
        in_specs=(
            P(None, None, "group", "member"),
            P("group", None, None, None, None),
            P(),
            P("group", "member", None, None),
            P("group", "member", None),
            P("group", "member", None),
        ),
        out_specs=(P(None, None, "group", "member"), P("group", None, None, None, None)),
        check_vma=False,
    )
```

```python
from functools import partial
import math

import jax
import jax.numpy as jnp
from jax import lax
from jax.experimental import pallas as pl
from jax.experimental.pallas import tpu as pltpu
from jax.sharding import PartitionSpec as P

DFT_PRECISION = lax.Precision.HIGH


def fourier_blocks(length, sign):
    counter = jnp.arange(length, dtype=jnp.int32)
    product = counter[:, None] * counter[None, :] % length
    angles = product.astype(jnp.float32) * (2.0 * math.pi / length)
    norming = 1.0 / math.sqrt(length)
    cosine = jnp.cos(angles) * norming
    sine_part = jnp.sin(angles) * (sign * norming)
    return jnp.stack([jnp.stack([cosine, sine_part]), jnp.stack([-sine_part, cosine])])


def transform(field, blocks):
    across = jnp.einsum("...chn,cdnk->...dhk", field, blocks, precision=DFT_PRECISION)
    return jnp.einsum("cdkn,...cnw->...dkw", blocks, across, precision=DFT_PRECISION)


def complex_times(left, right):
    left_re, left_im = (left[..., 0, :, :], left[..., 1, :, :])
    right_re, right_im = (right[..., 0, :, :], right[..., 1, :, :])
    return jnp.stack(
        [left_re * right_re - left_im * right_im, left_re * right_im + left_im * right_re], axis=-3
    )


def conj_times(left, right):
    left_re, left_im = (left[..., 0, :, :], left[..., 1, :, :])
    right_re, right_im = (right[..., 0, :, :], right[..., 1, :, :])
    return jnp.stack(
        [left_re * right_re + left_im * right_im, left_re * right_im - left_im * right_re], axis=-3
    )


def slot_numbers(targets, members, capacity):
    matches = (targets[:, None] == jnp.arange(members, dtype=jnp.int32)[None, :]).astype(jnp.int32)
    before = jnp.cumsum(matches, axis=0) - matches
    return targets * capacity + jnp.sum(before * matches, axis=1)


def selectors(offsets, patch_side, tile_cells, dtype):
    inner = jnp.arange(patch_side, dtype=jnp.int32)
    cells = jnp.arange(tile_cells, dtype=jnp.int32)
    hit = offsets[:, None, None] + inner[None, :, None] == cells[None, None, :]
    return hit.astype(dtype)


def cut_windows(tiles, requests, patch_side):
    tile_cells = tiles.shape[-1]
    valid = requests[:, 0].astype(jnp.bfloat16)
    row_sel = selectors(requests[:, 1], patch_side, tile_cells, jnp.bfloat16) * valid[:, None, None]
    col_sel = selectors(requests[:, 2], patch_side, tile_cells, jnp.bfloat16)
    rows = jnp.einsum("kit,sctu->kscui", row_sel, tiles, preferred_element_type=jnp.float32)
    rows = rows.astype(jnp.bfloat16)
    window = jnp.einsum("kscui,kju->kscij", rows, col_sel, preferred_element_type=jnp.float32)
    return window.astype(jnp.bfloat16)


def place_kernel(requests, peak, terms, out, total):
    step = pl.program_id(0)
    held = terms.shape[0]
    tile_cells = out.shape[-1]

    @pl.when(step == 0)
    def _():
        total[...] = jnp.zeros_like(total)

    for index in range(held):
        place_one(step * held + index, index, requests, terms, total)

    @pl.when(step == pl.num_programs(0) - 1)
    def _():
        out[...] = total[:, :, :tile_cells, :tile_cells] / peak[0, 0]


def place_one(slot, index, requests, terms, total):
    slice_count = terms.shape[1]
    patch_side = terms.shape[-1]
    row = requests[slot, 1]
    col = requests[slot, 2]
    row_base = pl.multiple_of((row // 8) * 8, 8)
    col_base = pl.multiple_of((col // 128) * 128, 128)
    row_rest = row - row_base
    col_rest = col - col_base
    band_rows = patch_side + 8
    band_cols = 2 * patch_side
    row_pick = (
        lax.broadcasted_iota(jnp.int32, (band_rows, patch_side), 0)
        == lax.broadcasted_iota(jnp.int32, (band_rows, patch_side), 1) + row_rest
    ).astype(jnp.bfloat16)
    col_pick = (
        lax.broadcasted_iota(jnp.int32, (patch_side, band_cols), 1)
        == lax.broadcasted_iota(jnp.int32, (patch_side, band_cols), 0) + col_rest
    ).astype(jnp.bfloat16)
    pieces = []
    for layer in range(slice_count):
        for part in range(2):
            term = terms[index, layer, part]
            high = term.astype(jnp.bfloat16)
            low = (term - high.astype(jnp.float32)).astype(jnp.bfloat16)
            pieces += [high, low]
    side_by_side = jnp.concatenate(pieces, axis=1)
    shifted = jnp.dot(row_pick, side_by_side, preferred_element_type=jnp.float32)
    shifted = shifted.astype(jnp.bfloat16)
    stacked = jnp.concatenate(
        [shifted[:, index * patch_side:(index + 1) * patch_side] for index in range(len(pieces))],
        axis=0,
    )
    placed = jnp.dot(stacked, col_pick, preferred_element_type=jnp.float32)
    for layer in range(slice_count):
        for part in range(2):
            index = 2 * (2 * layer + part)
            band = (
                placed[index * band_rows:(index + 1) * band_rows]
                + placed[(index + 1) * band_rows:(index + 2) * band_rows]
            )
            window = total.at[layer, part, pl.ds(row_base, band_rows), pl.ds(col_base, band_cols)]
            window[...] = window[...] + band


def accumulate(terms, requests, peak, tile_cells):
    slot_count, slice_count = terms.shape[:2]
    patch_side = terms.shape[-1]
    held = math.gcd(slot_count, 8)
    grid_spec = pltpu.PrefetchScalarGridSpec(
        num_scalar_prefetch=1,
        grid=(slot_count // held,),
        in_specs=[
            pl.BlockSpec(memory_space=pltpu.SMEM),
            pl.BlockSpec(
                (held, slice_count, 2, patch_side, patch_side), lambda k, req: (k, 0, 0, 0, 0)
            ),
        ],
        out_specs=pl.BlockSpec(
            (slice_count, 2, tile_cells, tile_cells), lambda k, req: (0, 0, 0, 0)
        ),
        scratch_shapes=[
            pltpu.VMEM(
                (slice_count, 2, tile_cells + 8, tile_cells + patch_side), jnp.float32
            )
        ],
    )
    return pl.pallas_call(
        place_kernel,
        grid_spec=grid_spec,
        out_shape=jax.ShapeDtypeStruct((slice_count, 2, tile_cells, tile_cells), jnp.float32),
        compiler_params=pltpu.CompilerParams(dimension_semantics=("arbitrary",)),
    )(requests, peak.reshape(1, 1), terms)


def group_max(value):
    count = lax.axis_size("group")
    if count & (count - 1) == 0:
        step = 1
        while step < count:
            pairs = [(index, index ^ step) for index in range(count)]
            value = jnp.maximum(value, lax.ppermute(value, "group", pairs))
            step *= 2
        return value
    running = value
    pairs = [(index, (index + 1) % count) for index in range(count)]
    for _ in range(count - 1):
        value = lax.ppermute(value, "group", pairs)
        running = jnp.maximum(running, value)
    return running


def split_pair(value):
    high = value.astype(jnp.bfloat16)
    low = (value - high.astype(jnp.float32)).astype(jnp.bfloat16)
    return high, low


def stack_three(value, axis):
    high = value.astype(jnp.bfloat16)
    low = (value - high.astype(jnp.float32)).astype(jnp.bfloat16)
    return jnp.concatenate([high, low, high], axis=axis)


def fourier_2d(fields, right_mat, left_mat):
    side = fields[0][0].shape[0]
    count = len(fields)
    rows = jnp.concatenate([jnp.concatenate([re, im], axis=1) for re, im in fields], axis=0)
    mid = jnp.dot(rows, right_mat, precision=lax.Precision.HIGH, preferred_element_type=jnp.float32)
    parted = jnp.concatenate(
        [
            jnp.concatenate([mid[m * side:(m + 1) * side, :side] for m in range(count)], axis=1),
            jnp.concatenate([mid[m * side:(m + 1) * side, side:] for m in range(count)], axis=1),
        ],
        axis=0,
    )
    out = jnp.dot(left_mat, parted, precision=lax.Precision.HIGH, preferred_element_type=jnp.float32)
    return [
        (out[:side, m * side:(m + 1) * side], out[side:, m * side:(m + 1) * side])
        for m in range(count)
    ]


def propagate_kernel(patch_ref, measured_ref, probe_ref, kern_ref, mats_right, mats_left,
                     peak_ref, grad_ref, probe_sum_ref):
    @pl.when(pl.program_id(0) == 0)
    def _():
        probe_sum_ref[...] = jnp.zeros_like(probe_sum_ref)

    for held in range(patch_ref.shape[0]):
        propagate_one(held, patch_ref, measured_ref, probe_ref, kern_ref, mats_right, mats_left,
                      grad_ref, probe_sum_ref)


def propagate_one(held, patch_ref, measured_ref, probe_ref, kern_ref, mats_right, mats_left,
                  grad_ref, probe_sum_ref):
    slice_count = patch_ref.shape[1]
    modes = probe_ref.shape[0]
    forward = lambda fields: fourier_2d(fields, mats_right[0], mats_left[0])
    inverse = lambda fields: fourier_2d(fields, mats_right[1], mats_left[1])
    kern_real, kern_imag = kern_ref[0], kern_ref[1]
    waves = [(probe_ref[m, 0], probe_ref[m, 1]) for m in range(modes)]
    history = []
    leaving = None
    for layer in range(slice_count):
        history.append(waves)
        patch_real = patch_ref[held, layer, 0].astype(jnp.float32)
        patch_imag = patch_ref[held, layer, 1].astype(jnp.float32)
        leaving = [
            (wr * patch_real - wi * patch_imag, wr * patch_imag + wi * patch_real)
            for wr, wi in waves
        ]
        if layer < slice_count - 1:
            spectra = forward(leaving)
            waves = inverse(
                [
                    (kern_real * fr - kern_imag * fi, kern_real * fi + kern_imag * fr)
                    for fr, fi in spectra
                ]
            )
    far = forward(leaving)
    intensity = None
    for fr, fi in far:
        power = fr * fr + fi * fi
        intensity = power if intensity is None else intensity + power
    factor = 1.0 - measured_ref[held] / jnp.sqrt(jnp.maximum(intensity, 1.0))
    back = inverse([(fr * factor, fi * factor) for fr, fi in far])
    for layer in reversed(range(slice_count)):
        grad_real = None
        grad_imag = None
        for (wr, wi), (br, bi) in zip(history[layer], back):
            term_real = wr * br + wi * bi
            term_imag = wr * bi - wi * br
            grad_real = term_real if grad_real is None else grad_real + term_real
            grad_imag = term_imag if grad_imag is None else grad_imag + term_imag
        grad_ref[held, layer, 0] = grad_real
        grad_ref[held, layer, 1] = grad_imag
        patch_real = patch_ref[held, layer, 0].astype(jnp.float32)
        patch_imag = patch_ref[held, layer, 1].astype(jnp.float32)
        back = [
            (patch_real * br + patch_imag * bi, patch_real * bi - patch_imag * br)
            for br, bi in back
        ]
        if layer > 0:
            spectra = forward(back)
            back = inverse(
                [
                    (kern_real * fr + kern_imag * fi, kern_real * fi - kern_imag * fr)
                    for fr, fi in spectra
                ]
            )

    for mode, (br, bi) in enumerate(back):
        probe_sum_ref[mode, 0] = probe_sum_ref[mode, 0] + br
        probe_sum_ref[mode, 1] = probe_sum_ref[mode, 1] + bi


def dft_mats(length):
    counter = jnp.arange(length, dtype=jnp.int32)
    product = counter[:, None] * counter[None, :] % length
    angles = product.astype(jnp.float32) * (2.0 * math.pi / length)
    norming = 1.0 / math.sqrt(length)
    cosine = jnp.cos(angles) * norming
    sine = jnp.sin(angles) * norming
    minus = jnp.concatenate(
        [jnp.concatenate([cosine, -sine], axis=1), jnp.concatenate([sine, cosine], axis=1)], axis=0
    )
    plus = jnp.concatenate(
        [jnp.concatenate([cosine, sine], axis=1), jnp.concatenate([-sine, cosine], axis=1)], axis=0
    )

    def parts(value):
        high = lax.reduce_precision(value, exponent_bits=8, mantissa_bits=7)
        return high.astype(jnp.bfloat16), (value - high).astype(jnp.bfloat16)

    def right(value):
        high, low = parts(value)
        return jnp.concatenate([high, high, low], axis=0)

    def left(value):
        high, low = parts(value)
        return jnp.concatenate([high, high, low], axis=1)

    mats_right = jnp.stack([minus, plus])
    mats_left = jnp.stack([plus, minus])
    return mats_right, mats_left


def propagate(patches, measured, probe_modes, prop_phase, peak):
    count, slice_count = patches.shape[:2]
    modes = probe_modes.shape[0]
    side = patches.shape[-1]
    kern = jnp.stack([jnp.cos(prop_phase), jnp.sin(prop_phase)])
    mats_right, mats_left = dft_mats(side)
    held = math.gcd(count, 8)
    whole = lambda shape: pl.BlockSpec(shape, lambda k: (0,) * len(shape))
    return pl.pallas_call(
        propagate_kernel,
        grid=(count // held,),
        in_specs=[
            pl.BlockSpec((held, slice_count, 2, side, side), lambda k: (k, 0, 0, 0, 0)),
            pl.BlockSpec((held, side, side), lambda k: (k, 0, 0)),
            whole((modes, 2, side, side)),
            whole((2, side, side)),
            whole((2, 2 * side, 2 * side)),
            whole((2, 2 * side, 2 * side)),
            pl.BlockSpec(memory_space=pltpu.SMEM),
        ],
        out_specs=[
            pl.BlockSpec((held, slice_count, 2, side, side), lambda k: (k, 0, 0, 0, 0)),
            whole((modes, 2, side, side)),
        ],
        out_shape=[
            jax.ShapeDtypeStruct((count, slice_count, 2, side, side), jnp.float32),
            jax.ShapeDtypeStruct((modes, 2, side, side), jnp.float32),
        ],
        compiler_params=pltpu.CompilerParams(dimension_semantics=("arbitrary",)),
    )(patches, measured, probe_modes, kern, mats_right, mats_left, peak.reshape(1, 1))


def member_sum(value, members):
    flat = value.reshape(members, -1)
    pieces = lax.all_to_all(flat, "member", split_axis=0, concat_axis=0, tiled=True)
    mine = jnp.sum(pieces, axis=0, keepdims=True)
    spread = jnp.broadcast_to(mine, flat.shape)
    whole = lax.all_to_all(spread, "member", split_axis=0, concat_axis=0, tiled=True)
    return whole.reshape(value.shape)


def on_device(object_field, probe_modes, prop_phase, amplitude, tile_owner, corner):
    members = lax.axis_size("member")
    pos_dev = tile_owner.shape[1]
    capacity = max(2, (2 * pos_dev + members - 1) // members)
    slot_count = members * capacity
    tile_cells = object_field.shape[2]
    patch_side = prop_phase.shape[0]
    power = jnp.max(jnp.sum(probe_modes * probe_modes, axis=(1, 2)))
    peak_power = group_max(power) + 1e-06
    flat_slots = slot_numbers(tile_owner[0, :, 0], members, capacity)
    entries = jnp.concatenate([jnp.ones((pos_dev, 1), jnp.int32), corner[0]], axis=1)
    chosen = (flat_slots[:, None] == jnp.arange(slot_count, dtype=jnp.int32)[None, :]).astype(
        jnp.int32
    )
    outgoing = jnp.sum(chosen[:, :, None] * entries[:, None, :], axis=0)
    requests = lax.all_to_all(
        outgoing.reshape(members, capacity, 3), "member", split_axis=0, concat_axis=0, tiled=True
    ).reshape(slot_count, 3)
    sent = jnp.zeros((slot_count, patch_side, patch_side), jnp.float32).at[flat_slots].set(
        amplitude[0]
    )
    measured = lax.all_to_all(
        sent.reshape(members, capacity, patch_side, patch_side),
        "member",
        split_axis=0,
        concat_axis=0,
        tiled=True,
    ).reshape(slot_count, patch_side, patch_side)
    patches = cut_windows(object_field, requests, patch_side)
    gradients, adjoint_sum = propagate(patches, measured, probe_modes[0], prop_phase, peak_power)
    probe_grad = member_sum(adjoint_sum / pos_dev, members)[None]
    object_grad = accumulate(gradients, requests, peak_power, tile_cells)
    return (object_grad, probe_grad)


def solution(mesh):
    return jax.shard_map(
        on_device,
        mesh=mesh,
        in_specs=(
            P(None, None, "group", "member"),
            P("group", None, None, None, None),
            P(),
            P("group", "member", None, None),
            P("group", "member", None),
            P("group", "member", None),
        ),
        out_specs=(P(None, None, "group", "member"), P("group", None, None, None, None)),
        check_vma=False,
    )
```

```python
from functools import partial
import math

import jax
import jax.numpy as jnp
from jax import lax
from jax.experimental import pallas as pl
from jax.experimental.pallas import tpu as pltpu
from jax.sharding import PartitionSpec as P

DFT_PRECISION = lax.Precision.HIGH


def fourier_blocks(length, sign):
    counter = jnp.arange(length, dtype=jnp.int32)
    product = counter[:, None] * counter[None, :] % length
    angles = product.astype(jnp.float32) * (2.0 * math.pi / length)
    norming = 1.0 / math.sqrt(length)
    cosine = jnp.cos(angles) * norming
    sine_part = jnp.sin(angles) * (sign * norming)
    return jnp.stack([jnp.stack([cosine, sine_part]), jnp.stack([-sine_part, cosine])])


def transform(field, blocks):
    across = jnp.einsum("...chn,cdnk->...dhk", field, blocks, precision=DFT_PRECISION)
    return jnp.einsum("cdkn,...cnw->...dkw", blocks, across, precision=DFT_PRECISION)


def complex_times(left, right):
    left_re, left_im = (left[..., 0, :, :], left[..., 1, :, :])
    right_re, right_im = (right[..., 0, :, :], right[..., 1, :, :])
    return jnp.stack(
        [left_re * right_re - left_im * right_im, left_re * right_im + left_im * right_re], axis=-3
    )


def conj_times(left, right):
    left_re, left_im = (left[..., 0, :, :], left[..., 1, :, :])
    right_re, right_im = (right[..., 0, :, :], right[..., 1, :, :])
    return jnp.stack(
        [left_re * right_re + left_im * right_im, left_re * right_im - left_im * right_re], axis=-3
    )


def slot_numbers(targets, members, capacity):
    matches = (targets[:, None] == jnp.arange(members, dtype=jnp.int32)[None, :]).astype(jnp.int32)
    before = jnp.cumsum(matches, axis=0) - matches
    return targets * capacity + jnp.sum(before * matches, axis=1)


def selectors(offsets, patch_side, tile_cells, dtype):
    inner = jnp.arange(patch_side, dtype=jnp.int32)
    cells = jnp.arange(tile_cells, dtype=jnp.int32)
    hit = offsets[:, None, None] + inner[None, :, None] == cells[None, None, :]
    return hit.astype(dtype)


def cut_windows(tiles, requests, patch_side):
    tile_cells = tiles.shape[-1]
    valid = requests[:, 0].astype(jnp.bfloat16)
    row_sel = selectors(requests[:, 1], patch_side, tile_cells, jnp.bfloat16) * valid[:, None, None]
    col_sel = selectors(requests[:, 2], patch_side, tile_cells, jnp.bfloat16)
    rows = jnp.einsum("kit,sctu->kscui", row_sel, tiles, preferred_element_type=jnp.float32)
    rows = rows.astype(jnp.bfloat16)
    window = jnp.einsum("kscui,kju->kscij", rows, col_sel, preferred_element_type=jnp.float32)
    return window.astype(jnp.bfloat16)


def place_kernel(requests, peak, terms, out, total):
    step = pl.program_id(0)
    held = terms.shape[0]
    tile_cells = out.shape[-1]

    @pl.when(step == 0)
    def _():
        total[...] = jnp.zeros_like(total)

    for index in range(held):
        place_one(step * held + index, index, requests, terms, total)

    @pl.when(step == pl.num_programs(0) - 1)
    def _():
        out[...] = total[:, :, :tile_cells, :tile_cells] / peak[0, 0]


def place_one(slot, index, requests, terms, total):
    slice_count = terms.shape[1]
    patch_side = terms.shape[-1]
    row = requests[slot, 1]
    col = requests[slot, 2]
    row_base = pl.multiple_of((row // 8) * 8, 8)
    col_base = pl.multiple_of((col // 128) * 128, 128)
    row_rest = row - row_base
    col_rest = col - col_base
    band_rows = patch_side + 8
    band_cols = 2 * patch_side
    row_pick = (
        lax.broadcasted_iota(jnp.int32, (band_rows, patch_side), 0)
        == lax.broadcasted_iota(jnp.int32, (band_rows, patch_side), 1) + row_rest
    ).astype(jnp.bfloat16)
    col_pick = (
        lax.broadcasted_iota(jnp.int32, (patch_side, band_cols), 1)
        == lax.broadcasted_iota(jnp.int32, (patch_side, band_cols), 0) + col_rest
    ).astype(jnp.bfloat16)
    pieces = []
    for layer in range(slice_count):
        for part in range(2):
            term = terms[index, layer, part]
            high = term.astype(jnp.bfloat16)
            low = (term - high.astype(jnp.float32)).astype(jnp.bfloat16)
            pieces += [high, low]
    side_by_side = jnp.concatenate(pieces, axis=1)
    shifted = jnp.dot(row_pick, side_by_side, preferred_element_type=jnp.float32)
    shifted = shifted.astype(jnp.bfloat16)
    stacked = jnp.concatenate(
        [shifted[:, index * patch_side:(index + 1) * patch_side] for index in range(len(pieces))],
        axis=0,
    )
    placed = jnp.dot(stacked, col_pick, preferred_element_type=jnp.float32)
    for layer in range(slice_count):
        for part in range(2):
            index = 2 * (2 * layer + part)
            band = (
                placed[index * band_rows:(index + 1) * band_rows]
                + placed[(index + 1) * band_rows:(index + 2) * band_rows]
            )
            window = total.at[layer, part, pl.ds(row_base, band_rows), pl.ds(col_base, band_cols)]
            window[...] = window[...] + band


def accumulate(terms, requests, peak, tile_cells):
    slot_count, slice_count = terms.shape[:2]
    patch_side = terms.shape[-1]
    held = math.gcd(slot_count, 8)
    grid_spec = pltpu.PrefetchScalarGridSpec(
        num_scalar_prefetch=1,
        grid=(slot_count // held,),
        in_specs=[
            pl.BlockSpec(memory_space=pltpu.SMEM),
            pl.BlockSpec(
                (held, slice_count, 2, patch_side, patch_side), lambda k, req: (k, 0, 0, 0, 0)
            ),
        ],
        out_specs=pl.BlockSpec(
            (slice_count, 2, tile_cells, tile_cells), lambda k, req: (0, 0, 0, 0)
        ),
        scratch_shapes=[
            pltpu.VMEM(
                (slice_count, 2, tile_cells + 8, tile_cells + patch_side), jnp.float32
            )
        ],
    )
    return pl.pallas_call(
        place_kernel,
        grid_spec=grid_spec,
        out_shape=jax.ShapeDtypeStruct((slice_count, 2, tile_cells, tile_cells), jnp.float32),
        compiler_params=pltpu.CompilerParams(dimension_semantics=("arbitrary",)),
    )(requests, peak.reshape(1, 1), terms)


def group_max(value):
    count = lax.axis_size("group")
    if count & (count - 1) == 0:
        step = 1
        while step < count:
            pairs = [(index, index ^ step) for index in range(count)]
            value = jnp.maximum(value, lax.ppermute(value, "group", pairs))
            step *= 2
        return value
    running = value
    pairs = [(index, (index + 1) % count) for index in range(count)]
    for _ in range(count - 1):
        value = lax.ppermute(value, "group", pairs)
        running = jnp.maximum(running, value)
    return running


def split_pair(value):
    high = value.astype(jnp.bfloat16)
    low = (value - high.astype(jnp.float32)).astype(jnp.bfloat16)
    return high, low


def stack_three(value, axis):
    high = value.astype(jnp.bfloat16)
    low = (value - high.astype(jnp.float32)).astype(jnp.bfloat16)
    return jnp.concatenate([high, low, high], axis=axis)


def fourier_2d(fields, right_mat, left_mat):
    side = fields[0][0].shape[0]
    count = len(fields)
    rows = jnp.concatenate([jnp.concatenate([re, im], axis=1) for re, im in fields], axis=0)
    mid = jnp.dot(stack_three(rows, 1), right_mat, preferred_element_type=jnp.float32)
    parted = jnp.concatenate(
        [
            jnp.concatenate([mid[m * side:(m + 1) * side, :side] for m in range(count)], axis=1),
            jnp.concatenate([mid[m * side:(m + 1) * side, side:] for m in range(count)], axis=1),
        ],
        axis=0,
    )
    out = jnp.dot(left_mat, stack_three(parted, 0), preferred_element_type=jnp.float32)
    return [
        (out[:side, m * side:(m + 1) * side], out[side:, m * side:(m + 1) * side])
        for m in range(count)
    ]


def propagate_kernel(patch_ref, measured_ref, probe_ref, kern_ref, mats_right, mats_left,
                     peak_ref, grad_ref, probe_sum_ref):
    @pl.when(pl.program_id(0) == 0)
    def _():
        probe_sum_ref[...] = jnp.zeros_like(probe_sum_ref)

    held = patch_ref.shape[0]
    together = 2 if held % 2 == 0 else 1
    for first in range(0, held, together):
        propagate_group(list(range(first, first + together)), patch_ref, measured_ref, probe_ref,
                        kern_ref, mats_right, mats_left, grad_ref, probe_sum_ref)


def propagate_group(slots, patch_ref, measured_ref, probe_ref, kern_ref, mats_right, mats_left,
                    grad_ref, probe_sum_ref):
    slice_count = patch_ref.shape[1]
    modes = probe_ref.shape[0]
    forward = lambda fields: fourier_2d(fields, mats_right[0], mats_left[0])
    inverse = lambda fields: fourier_2d(fields, mats_right[1], mats_left[1])
    kern_real, kern_imag = kern_ref[0], kern_ref[1]
    owner = [j for j in range(len(slots)) for _ in range(modes)]
    waves = [(probe_ref[m, 0], probe_ref[m, 1]) for _ in slots for m in range(modes)]

    def patch(layer):
        return [
            (patch_ref[s, layer, 0].astype(jnp.float32), patch_ref[s, layer, 1].astype(jnp.float32))
            for s in slots
        ]

    history = []
    leaving = None
    for layer in range(slice_count):
        history.append(waves)
        cells = patch(layer)
        leaving = []
        for (wr, wi), j in zip(waves, owner):
            pr, pi = cells[j]
            leaving.append((wr * pr - wi * pi, wr * pi + wi * pr))
        if layer < slice_count - 1:
            spectra = forward(leaving)
            waves = inverse(
                [
                    (kern_real * fr - kern_imag * fi, kern_real * fi + kern_imag * fr)
                    for fr, fi in spectra
                ]
            )
    far = forward(leaving)
    scaled = []
    for j, s in enumerate(slots):
        intensity = None
        for m in range(modes):
            fr, fi = far[j * modes + m]
            power = fr * fr + fi * fi
            intensity = power if intensity is None else intensity + power
        factor = 1.0 - measured_ref[s] / jnp.sqrt(jnp.maximum(intensity, 1.0))
        for m in range(modes):
            fr, fi = far[j * modes + m]
            scaled.append((fr * factor, fi * factor))
    back = inverse(scaled)
    for layer in reversed(range(slice_count)):
        for j, s in enumerate(slots):
            grad_real = None
            grad_imag = None
            for m in range(modes):
                wr, wi = history[layer][j * modes + m]
                br, bi = back[j * modes + m]
                term_real = wr * br + wi * bi
                term_imag = wr * bi - wi * br
                grad_real = term_real if grad_real is None else grad_real + term_real
                grad_imag = term_imag if grad_imag is None else grad_imag + term_imag
            grad_ref[s, layer, 0] = grad_real
            grad_ref[s, layer, 1] = grad_imag
        cells = patch(layer)
        moved = []
        for (br, bi), j in zip(back, owner):
            pr, pi = cells[j]
            moved.append((pr * br + pi * bi, pr * bi - pi * br))
        back = moved
        if layer > 0:
            spectra = forward(back)
            back = inverse(
                [
                    (kern_real * fr + kern_imag * fi, kern_real * fi - kern_imag * fr)
                    for fr, fi in spectra
                ]
            )
    for j in range(len(slots)):
        for m in range(modes):
            br, bi = back[j * modes + m]
            probe_sum_ref[m, 0] = probe_sum_ref[m, 0] + br
            probe_sum_ref[m, 1] = probe_sum_ref[m, 1] + bi


def dft_mats(length):
    counter = jnp.arange(length, dtype=jnp.int32)
    product = counter[:, None] * counter[None, :] % length
    angles = product.astype(jnp.float32) * (2.0 * math.pi / length)
    norming = 1.0 / math.sqrt(length)
    cosine = jnp.cos(angles) * norming
    sine = jnp.sin(angles) * norming
    minus = jnp.concatenate(
        [jnp.concatenate([cosine, -sine], axis=1), jnp.concatenate([sine, cosine], axis=1)], axis=0
    )
    plus = jnp.concatenate(
        [jnp.concatenate([cosine, sine], axis=1), jnp.concatenate([-sine, cosine], axis=1)], axis=0
    )

    def parts(value):
        high = lax.reduce_precision(value, exponent_bits=8, mantissa_bits=7)
        return high.astype(jnp.bfloat16), (value - high).astype(jnp.bfloat16)

    def right(value):
        high, low = parts(value)
        return jnp.concatenate([high, high, low], axis=0)

    def left(value):
        high, low = parts(value)
        return jnp.concatenate([high, high, low], axis=1)

    mats_right = jnp.stack([right(minus), right(plus)])
    mats_left = jnp.stack([left(plus), left(minus)])
    return mats_right, mats_left


def propagate(patches, measured, probe_modes, prop_phase, peak):
    count, slice_count = patches.shape[:2]
    modes = probe_modes.shape[0]
    side = patches.shape[-1]
    kern = jnp.stack([jnp.cos(prop_phase), jnp.sin(prop_phase)])
    mats_right, mats_left = dft_mats(side)
    held = math.gcd(count, 8)
    whole = lambda shape: pl.BlockSpec(shape, lambda k: (0,) * len(shape))
    return pl.pallas_call(
        propagate_kernel,
        grid=(count // held,),
        in_specs=[
            pl.BlockSpec((held, slice_count, 2, side, side), lambda k: (k, 0, 0, 0, 0)),
            pl.BlockSpec((held, side, side), lambda k: (k, 0, 0)),
            whole((modes, 2, side, side)),
            whole((2, side, side)),
            whole((2, 6 * side, 2 * side)),
            whole((2, 2 * side, 6 * side)),
            pl.BlockSpec(memory_space=pltpu.SMEM),
        ],
        out_specs=[
            pl.BlockSpec((held, slice_count, 2, side, side), lambda k: (k, 0, 0, 0, 0)),
            whole((modes, 2, side, side)),
        ],
        out_shape=[
            jax.ShapeDtypeStruct((count, slice_count, 2, side, side), jnp.float32),
            jax.ShapeDtypeStruct((modes, 2, side, side), jnp.float32),
        ],
        compiler_params=pltpu.CompilerParams(dimension_semantics=("arbitrary",)),
    )(patches, measured, probe_modes, kern, mats_right, mats_left, peak.reshape(1, 1))


def member_sum(value, members):
    flat = value.reshape(members, -1)
    pieces = lax.all_to_all(flat, "member", split_axis=0, concat_axis=0, tiled=True)
    mine = jnp.sum(pieces, axis=0, keepdims=True)
    spread = jnp.broadcast_to(mine, flat.shape)
    whole = lax.all_to_all(spread, "member", split_axis=0, concat_axis=0, tiled=True)
    return whole.reshape(value.shape)


def on_device(object_field, probe_modes, prop_phase, amplitude, tile_owner, corner):
    members = lax.axis_size("member")
    pos_dev = tile_owner.shape[1]
    capacity = max(2, (2 * pos_dev + members - 1) // members)
    slot_count = members * capacity
    tile_cells = object_field.shape[2]
    patch_side = prop_phase.shape[0]
    power = jnp.max(jnp.sum(probe_modes * probe_modes, axis=(1, 2)))
    peak_power = group_max(power) + 1e-06
    flat_slots = slot_numbers(tile_owner[0, :, 0], members, capacity)
    entries = jnp.concatenate([jnp.ones((pos_dev, 1), jnp.int32), corner[0]], axis=1)
    chosen = (flat_slots[:, None] == jnp.arange(slot_count, dtype=jnp.int32)[None, :]).astype(
        jnp.int32
    )
    outgoing = jnp.sum(chosen[:, :, None] * entries[:, None, :], axis=0)
    requests = lax.all_to_all(
        outgoing.reshape(members, capacity, 3), "member", split_axis=0, concat_axis=0, tiled=True
    ).reshape(slot_count, 3)
    sent = jnp.zeros((slot_count, patch_side, patch_side), jnp.float32).at[flat_slots].set(
        amplitude[0]
    )
    measured = lax.all_to_all(
        sent.reshape(members, capacity, patch_side, patch_side),
        "member",
        split_axis=0,
        concat_axis=0,
        tiled=True,
    ).reshape(slot_count, patch_side, patch_side)
    patches = cut_windows(object_field, requests, patch_side)
    gradients, adjoint_sum = propagate(patches, measured, probe_modes[0], prop_phase, peak_power)
    probe_grad = member_sum(adjoint_sum / pos_dev, members)[None]
    object_grad = accumulate(gradients, requests, peak_power, tile_cells)
    return (object_grad, probe_grad)


def solution(mesh):
    return jax.shard_map(
        on_device,
        mesh=mesh,
        in_specs=(
            P(None, None, "group", "member"),
            P("group", None, None, None, None),
            P(),
            P("group", "member", None, None),
            P("group", "member", None),
            P("group", "member", None),
        ),
        out_specs=(P(None, None, "group", "member"), P("group", None, None, None, None)),
        check_vma=False,
    )
```

```python
from functools import partial
import math

import jax
import jax.numpy as jnp
from jax import lax
from jax.experimental import pallas as pl
from jax.experimental.pallas import tpu as pltpu
from jax.sharding import PartitionSpec as P

DFT_PRECISION = lax.Precision.HIGH


def fourier_blocks(length, sign):
    counter = jnp.arange(length, dtype=jnp.int32)
    product = counter[:, None] * counter[None, :] % length
    angles = product.astype(jnp.float32) * (2.0 * math.pi / length)
    norming = 1.0 / math.sqrt(length)
    cosine = jnp.cos(angles) * norming
    sine_part = jnp.sin(angles) * (sign * norming)
    return jnp.stack([jnp.stack([cosine, sine_part]), jnp.stack([-sine_part, cosine])])


def transform(field, blocks):
    across = jnp.einsum("...chn,cdnk->...dhk", field, blocks, precision=DFT_PRECISION)
    return jnp.einsum("cdkn,...cnw->...dkw", blocks, across, precision=DFT_PRECISION)


def complex_times(left, right):
    left_re, left_im = (left[..., 0, :, :], left[..., 1, :, :])
    right_re, right_im = (right[..., 0, :, :], right[..., 1, :, :])
    return jnp.stack(
        [left_re * right_re - left_im * right_im, left_re * right_im + left_im * right_re], axis=-3
    )


def conj_times(left, right):
    left_re, left_im = (left[..., 0, :, :], left[..., 1, :, :])
    right_re, right_im = (right[..., 0, :, :], right[..., 1, :, :])
    return jnp.stack(
        [left_re * right_re + left_im * right_im, left_re * right_im - left_im * right_re], axis=-3
    )


def slot_numbers(targets, members, capacity):
    matches = (targets[:, None] == jnp.arange(members, dtype=jnp.int32)[None, :]).astype(jnp.int32)
    before = jnp.cumsum(matches, axis=0) - matches
    return targets * capacity + jnp.sum(before * matches, axis=1)


def selectors(offsets, patch_side, tile_cells, dtype):
    inner = jnp.arange(patch_side, dtype=jnp.int32)
    cells = jnp.arange(tile_cells, dtype=jnp.int32)
    hit = offsets[:, None, None] + inner[None, :, None] == cells[None, None, :]
    return hit.astype(dtype)


def cut_windows(tiles, requests, patch_side):
    tile_cells = tiles.shape[-1]
    valid = requests[:, 0].astype(jnp.bfloat16)
    row_sel = selectors(requests[:, 1], patch_side, tile_cells, jnp.bfloat16) * valid[:, None, None]
    col_sel = selectors(requests[:, 2], patch_side, tile_cells, jnp.bfloat16)
    rows = jnp.einsum("kit,sctu->kscui", row_sel, tiles, preferred_element_type=jnp.float32)
    rows = rows.astype(jnp.bfloat16)
    window = jnp.einsum("kscui,kju->kscij", rows, col_sel, preferred_element_type=jnp.float32)
    return window.astype(jnp.bfloat16)


def place_kernel(requests, peak, terms, out, total):
    step = pl.program_id(0)
    held = terms.shape[0]
    tile_cells = out.shape[-1]

    @pl.when(step == 0)
    def _():
        total[...] = jnp.zeros_like(total)

    for index in range(held):
        place_one(step * held + index, index, requests, terms, total)

    @pl.when(step == pl.num_programs(0) - 1)
    def _():
        out[...] = total[:, :, :tile_cells, :tile_cells] / peak[0, 0]


def place_one(slot, index, requests, terms, total):
    slice_count = terms.shape[1]
    patch_side = terms.shape[-1]
    row = requests[slot, 1]
    col = requests[slot, 2]
    row_base = pl.multiple_of((row // 8) * 8, 8)
    col_base = pl.multiple_of((col // 128) * 128, 128)
    row_rest = row - row_base
    col_rest = col - col_base
    band_rows = patch_side + 8
    band_cols = 2 * patch_side
    row_pick = (
        lax.broadcasted_iota(jnp.int32, (band_rows, patch_side), 0)
        == lax.broadcasted_iota(jnp.int32, (band_rows, patch_side), 1) + row_rest
    ).astype(jnp.bfloat16)
    col_pick = (
        lax.broadcasted_iota(jnp.int32, (patch_side, band_cols), 1)
        == lax.broadcasted_iota(jnp.int32, (patch_side, band_cols), 0) + col_rest
    ).astype(jnp.bfloat16)
    pieces = []
    for layer in range(slice_count):
        for part in range(2):
            term = terms[index, layer, part]
            high = term.astype(jnp.bfloat16)
            low = (term - high.astype(jnp.float32)).astype(jnp.bfloat16)
            pieces += [high, low]
    side_by_side = jnp.concatenate(pieces, axis=1)
    shifted = jnp.dot(row_pick, side_by_side, preferred_element_type=jnp.float32)
    shifted = shifted.astype(jnp.bfloat16)
    stacked = jnp.concatenate(
        [shifted[:, index * patch_side:(index + 1) * patch_side] for index in range(len(pieces))],
        axis=0,
    )
    placed = jnp.dot(stacked, col_pick, preferred_element_type=jnp.float32)
    for layer in range(slice_count):
        for part in range(2):
            index = 2 * (2 * layer + part)
            band = (
                placed[index * band_rows:(index + 1) * band_rows]
                + placed[(index + 1) * band_rows:(index + 2) * band_rows]
            )
            window = total.at[layer, part, pl.ds(row_base, band_rows), pl.ds(col_base, band_cols)]
            window[...] = window[...] + band


def accumulate(terms, requests, peak, tile_cells):
    slot_count, slice_count = terms.shape[:2]
    patch_side = terms.shape[-1]
    held = math.gcd(slot_count, 8)
    grid_spec = pltpu.PrefetchScalarGridSpec(
        num_scalar_prefetch=1,
        grid=(slot_count // held,),
        in_specs=[
            pl.BlockSpec(memory_space=pltpu.SMEM),
            pl.BlockSpec(
                (held, slice_count, 2, patch_side, patch_side), lambda k, req: (k, 0, 0, 0, 0)
            ),
        ],
        out_specs=pl.BlockSpec(
            (slice_count, 2, tile_cells, tile_cells), lambda k, req: (0, 0, 0, 0)
        ),
        scratch_shapes=[
            pltpu.VMEM(
                (slice_count, 2, tile_cells + 8, tile_cells + patch_side), jnp.float32
            )
        ],
    )
    return pl.pallas_call(
        place_kernel,
        grid_spec=grid_spec,
        out_shape=jax.ShapeDtypeStruct((slice_count, 2, tile_cells, tile_cells), jnp.float32),
        compiler_params=pltpu.CompilerParams(dimension_semantics=("arbitrary",)),
    )(requests, peak.reshape(1, 1), terms)


def group_max(value):
    count = lax.axis_size("group")
    if count & (count - 1) == 0:
        step = 1
        while step < count:
            pairs = [(index, index ^ step) for index in range(count)]
            value = jnp.maximum(value, lax.ppermute(value, "group", pairs))
            step *= 2
        return value
    running = value
    pairs = [(index, (index + 1) % count) for index in range(count)]
    for _ in range(count - 1):
        value = lax.ppermute(value, "group", pairs)
        running = jnp.maximum(running, value)
    return running


def split_pair(value):
    high = value.astype(jnp.bfloat16)
    low = (value - high.astype(jnp.float32)).astype(jnp.bfloat16)
    return high, low


def stack_three(value, axis):
    high = value.astype(jnp.bfloat16)
    low = (value - high.astype(jnp.float32)).astype(jnp.bfloat16)
    return jnp.concatenate([high, low, high], axis=axis)


def fourier_2d(fields, right_mat, left_mat):
    side = fields[0][0].shape[0]
    count = len(fields)
    rows = jnp.concatenate([jnp.concatenate([re, im], axis=1) for re, im in fields], axis=0)
    mid = jnp.dot(stack_three(rows, 1), right_mat, preferred_element_type=jnp.float32)
    parted = jnp.concatenate(
        [
            jnp.concatenate([mid[m * side:(m + 1) * side, :side] for m in range(count)], axis=1),
            jnp.concatenate([mid[m * side:(m + 1) * side, side:] for m in range(count)], axis=1),
        ],
        axis=0,
    )
    out = jnp.dot(left_mat, stack_three(parted, 0), preferred_element_type=jnp.float32)
    return [
        (out[:side, m * side:(m + 1) * side], out[side:, m * side:(m + 1) * side])
        for m in range(count)
    ]


def propagate_kernel(patch_ref, measured_ref, probe_ref, kern_ref, mats_right, mats_left,
                     peak_ref, grad_ref, probe_sum_ref):
    @pl.when(pl.program_id(0) == 0)
    def _():
        probe_sum_ref[...] = jnp.zeros_like(probe_sum_ref)

    held = patch_ref.shape[0]
    together = math.gcd(held, 4)
    for first in range(0, held, together):
        propagate_group(list(range(first, first + together)), patch_ref, measured_ref, probe_ref,
                        kern_ref, mats_right, mats_left, grad_ref, probe_sum_ref)


def propagate_group(slots, patch_ref, measured_ref, probe_ref, kern_ref, mats_right, mats_left,
                    grad_ref, probe_sum_ref):
    slice_count = patch_ref.shape[1]
    modes = probe_ref.shape[0]
    forward = lambda fields: fourier_2d(fields, mats_right[0], mats_left[0])
    inverse = lambda fields: fourier_2d(fields, mats_right[1], mats_left[1])
    kern_real, kern_imag = kern_ref[0], kern_ref[1]
    owner = [j for j in range(len(slots)) for _ in range(modes)]
    waves = [(probe_ref[m, 0], probe_ref[m, 1]) for _ in slots for m in range(modes)]

    def patch(layer):
        return [
            (patch_ref[s, layer, 0].astype(jnp.float32), patch_ref[s, layer, 1].astype(jnp.float32))
            for s in slots
        ]

    history = []
    leaving = None
    for layer in range(slice_count):
        history.append(waves)
        cells = patch(layer)
        leaving = []
        for (wr, wi), j in zip(waves, owner):
            pr, pi = cells[j]
            leaving.append((wr * pr - wi * pi, wr * pi + wi * pr))
        if layer < slice_count - 1:
            spectra = forward(leaving)
            waves = inverse(
                [
                    (kern_real * fr - kern_imag * fi, kern_real * fi + kern_imag * fr)
                    for fr, fi in spectra
                ]
            )
    far = forward(leaving)
    scaled = []
    for j, s in enumerate(slots):
        intensity = None
        for m in range(modes):
            fr, fi = far[j * modes + m]
            power = fr * fr + fi * fi
            intensity = power if intensity is None else intensity + power
        factor = 1.0 - measured_ref[s] / jnp.sqrt(jnp.maximum(intensity, 1.0))
        for m in range(modes):
            fr, fi = far[j * modes + m]
            scaled.append((fr * factor, fi * factor))
    back = inverse(scaled)
    for layer in reversed(range(slice_count)):
        for j, s in enumerate(slots):
            grad_real = None
            grad_imag = None
            for m in range(modes):
                wr, wi = history[layer][j * modes + m]
                br, bi = back[j * modes + m]
                term_real = wr * br + wi * bi
                term_imag = wr * bi - wi * br
                grad_real = term_real if grad_real is None else grad_real + term_real
                grad_imag = term_imag if grad_imag is None else grad_imag + term_imag
            grad_ref[s, layer, 0] = grad_real
            grad_ref[s, layer, 1] = grad_imag
        cells = patch(layer)
        moved = []
        for (br, bi), j in zip(back, owner):
            pr, pi = cells[j]
            moved.append((pr * br + pi * bi, pr * bi - pi * br))
        back = moved
        if layer > 0:
            spectra = forward(back)
            back = inverse(
                [
                    (kern_real * fr + kern_imag * fi, kern_real * fi - kern_imag * fr)
                    for fr, fi in spectra
                ]
            )
    for j in range(len(slots)):
        for m in range(modes):
            br, bi = back[j * modes + m]
            probe_sum_ref[m, 0] = probe_sum_ref[m, 0] + br
            probe_sum_ref[m, 1] = probe_sum_ref[m, 1] + bi


def dft_mats(length):
    counter = jnp.arange(length, dtype=jnp.int32)
    product = counter[:, None] * counter[None, :] % length
    angles = product.astype(jnp.float32) * (2.0 * math.pi / length)
    norming = 1.0 / math.sqrt(length)
    cosine = jnp.cos(angles) * norming
    sine = jnp.sin(angles) * norming
    minus = jnp.concatenate(
        [jnp.concatenate([cosine, -sine], axis=1), jnp.concatenate([sine, cosine], axis=1)], axis=0
    )
    plus = jnp.concatenate(
        [jnp.concatenate([cosine, sine], axis=1), jnp.concatenate([-sine, cosine], axis=1)], axis=0
    )

    def parts(value):
        high = lax.reduce_precision(value, exponent_bits=8, mantissa_bits=7)
        return high.astype(jnp.bfloat16), (value - high).astype(jnp.bfloat16)

    def right(value):
        high, low = parts(value)
        return jnp.concatenate([high, high, low], axis=0)

    def left(value):
        high, low = parts(value)
        return jnp.concatenate([high, high, low], axis=1)

    mats_right = jnp.stack([right(minus), right(plus)])
    mats_left = jnp.stack([left(plus), left(minus)])
    return mats_right, mats_left


def propagate(patches, measured, probe_modes, prop_phase, peak):
    count, slice_count = patches.shape[:2]
    modes = probe_modes.shape[0]
    side = patches.shape[-1]
    kern = jnp.stack([jnp.cos(prop_phase), jnp.sin(prop_phase)])
    mats_right, mats_left = dft_mats(side)
    held = math.gcd(count, 8)
    whole = lambda shape: pl.BlockSpec(shape, lambda k: (0,) * len(shape))
    return pl.pallas_call(
        propagate_kernel,
        grid=(count // held,),
        in_specs=[
            pl.BlockSpec((held, slice_count, 2, side, side), lambda k: (k, 0, 0, 0, 0)),
            pl.BlockSpec((held, side, side), lambda k: (k, 0, 0)),
            whole((modes, 2, side, side)),
            whole((2, side, side)),
            whole((2, 6 * side, 2 * side)),
            whole((2, 2 * side, 6 * side)),
            pl.BlockSpec(memory_space=pltpu.SMEM),
        ],
        out_specs=[
            pl.BlockSpec((held, slice_count, 2, side, side), lambda k: (k, 0, 0, 0, 0)),
            whole((modes, 2, side, side)),
        ],
        out_shape=[
            jax.ShapeDtypeStruct((count, slice_count, 2, side, side), jnp.float32),
            jax.ShapeDtypeStruct((modes, 2, side, side), jnp.float32),
        ],
        compiler_params=pltpu.CompilerParams(dimension_semantics=("arbitrary",)),
    )(patches, measured, probe_modes, kern, mats_right, mats_left, peak.reshape(1, 1))


def member_sum(value, members):
    flat = value.reshape(members, -1)
    pieces = lax.all_to_all(flat, "member", split_axis=0, concat_axis=0, tiled=True)
    mine = jnp.sum(pieces, axis=0, keepdims=True)
    spread = jnp.broadcast_to(mine, flat.shape)
    whole = lax.all_to_all(spread, "member", split_axis=0, concat_axis=0, tiled=True)
    return whole.reshape(value.shape)


def on_device(object_field, probe_modes, prop_phase, amplitude, tile_owner, corner):
    members = lax.axis_size("member")
    pos_dev = tile_owner.shape[1]
    capacity = max(2, (2 * pos_dev + members - 1) // members)
    slot_count = members * capacity
    tile_cells = object_field.shape[2]
    patch_side = prop_phase.shape[0]
    power = jnp.max(jnp.sum(probe_modes * probe_modes, axis=(1, 2)))
    peak_power = group_max(power) + 1e-06
    flat_slots = slot_numbers(tile_owner[0, :, 0], members, capacity)
    entries = jnp.concatenate([jnp.ones((pos_dev, 1), jnp.int32), corner[0]], axis=1)
    chosen = (flat_slots[:, None] == jnp.arange(slot_count, dtype=jnp.int32)[None, :]).astype(
        jnp.int32
    )
    outgoing = jnp.sum(chosen[:, :, None] * entries[:, None, :], axis=0)
    requests = lax.all_to_all(
        outgoing.reshape(members, capacity, 3), "member", split_axis=0, concat_axis=0, tiled=True
    ).reshape(slot_count, 3)
    sent = jnp.zeros((slot_count, patch_side, patch_side), jnp.float32).at[flat_slots].set(
        amplitude[0]
    )
    measured = lax.all_to_all(
        sent.reshape(members, capacity, patch_side, patch_side),
        "member",
        split_axis=0,
        concat_axis=0,
        tiled=True,
    ).reshape(slot_count, patch_side, patch_side)
    patches = cut_windows(object_field, requests, patch_side)
    gradients, adjoint_sum = propagate(patches, measured, probe_modes[0], prop_phase, peak_power)
    probe_grad = member_sum(adjoint_sum / pos_dev, members)[None]
    object_grad = accumulate(gradients, requests, peak_power, tile_cells)
    return (object_grad, probe_grad)


def solution(mesh):
    return jax.shard_map(
        on_device,
        mesh=mesh,
        in_specs=(
            P(None, None, "group", "member"),
            P("group", None, None, None, None),
            P(),
            P("group", "member", None, None),
            P("group", "member", None),
            P("group", "member", None),
        ),
        out_specs=(P(None, None, "group", "member"), P("group", None, None, None, None)),
        check_vma=False,
    )
```

```python
from functools import partial
import math

import jax
import jax.numpy as jnp
from jax import lax
from jax.experimental import pallas as pl
from jax.experimental.pallas import tpu as pltpu
from jax.sharding import PartitionSpec as P

DFT_PRECISION = lax.Precision.HIGH


def fourier_blocks(length, sign):
    counter = jnp.arange(length, dtype=jnp.int32)
    product = counter[:, None] * counter[None, :] % length
    angles = product.astype(jnp.float32) * (2.0 * math.pi / length)
    norming = 1.0 / math.sqrt(length)
    cosine = jnp.cos(angles) * norming
    sine_part = jnp.sin(angles) * (sign * norming)
    return jnp.stack([jnp.stack([cosine, sine_part]), jnp.stack([-sine_part, cosine])])


def transform(field, blocks):
    across = jnp.einsum("...chn,cdnk->...dhk", field, blocks, precision=DFT_PRECISION)
    return jnp.einsum("cdkn,...cnw->...dkw", blocks, across, precision=DFT_PRECISION)


def complex_times(left, right):
    left_re, left_im = (left[..., 0, :, :], left[..., 1, :, :])
    right_re, right_im = (right[..., 0, :, :], right[..., 1, :, :])
    return jnp.stack(
        [left_re * right_re - left_im * right_im, left_re * right_im + left_im * right_re], axis=-3
    )


def conj_times(left, right):
    left_re, left_im = (left[..., 0, :, :], left[..., 1, :, :])
    right_re, right_im = (right[..., 0, :, :], right[..., 1, :, :])
    return jnp.stack(
        [left_re * right_re + left_im * right_im, left_re * right_im - left_im * right_re], axis=-3
    )


def slot_numbers(targets, members, capacity):
    matches = (targets[:, None] == jnp.arange(members, dtype=jnp.int32)[None, :]).astype(jnp.int32)
    before = jnp.cumsum(matches, axis=0) - matches
    return targets * capacity + jnp.sum(before * matches, axis=1)


def selectors(offsets, patch_side, tile_cells, dtype):
    inner = jnp.arange(patch_side, dtype=jnp.int32)
    cells = jnp.arange(tile_cells, dtype=jnp.int32)
    hit = offsets[:, None, None] + inner[None, :, None] == cells[None, None, :]
    return hit.astype(dtype)


def cut_windows(tiles, requests, patch_side):
    tile_cells = tiles.shape[-1]
    valid = requests[:, 0].astype(jnp.bfloat16)
    row_sel = selectors(requests[:, 1], patch_side, tile_cells, jnp.bfloat16) * valid[:, None, None]
    col_sel = selectors(requests[:, 2], patch_side, tile_cells, jnp.bfloat16)
    rows = jnp.einsum("kit,sctu->kscui", row_sel, tiles, preferred_element_type=jnp.float32)
    rows = rows.astype(jnp.bfloat16)
    window = jnp.einsum("kscui,kju->kscij", rows, col_sel, preferred_element_type=jnp.float32)
    return window.astype(jnp.bfloat16)


def place_kernel(requests, peak, terms, out, total):
    step = pl.program_id(0)
    held = terms.shape[0]
    tile_cells = out.shape[-1]

    @pl.when(step == 0)
    def _():
        total[...] = jnp.zeros_like(total)

    for index in range(held):
        place_one(step * held + index, index, requests, terms, total)

    @pl.when(step == pl.num_programs(0) - 1)
    def _():
        out[...] = total[:, :, :tile_cells, :tile_cells] / peak[0, 0]


def place_one(slot, index, requests, terms, total):
    slice_count = terms.shape[1]
    patch_side = terms.shape[-1]
    row = requests[slot, 1]
    col = requests[slot, 2]
    row_base = pl.multiple_of((row // 8) * 8, 8)
    col_base = pl.multiple_of((col // 128) * 128, 128)
    row_rest = row - row_base
    col_rest = col - col_base
    band_rows = patch_side + 8
    band_cols = 2 * patch_side
    row_pick = (
        lax.broadcasted_iota(jnp.int32, (band_rows, patch_side), 0)
        == lax.broadcasted_iota(jnp.int32, (band_rows, patch_side), 1) + row_rest
    ).astype(jnp.bfloat16)
    col_pick = (
        lax.broadcasted_iota(jnp.int32, (patch_side, band_cols), 1)
        == lax.broadcasted_iota(jnp.int32, (patch_side, band_cols), 0) + col_rest
    ).astype(jnp.bfloat16)
    pieces = []
    for layer in range(slice_count):
        for part in range(2):
            term = terms[index, layer, part]
            high = term.astype(jnp.bfloat16)
            low = (term - high.astype(jnp.float32)).astype(jnp.bfloat16)
            pieces += [high, low]
    side_by_side = jnp.concatenate(pieces, axis=1)
    shifted = jnp.dot(row_pick, side_by_side, preferred_element_type=jnp.float32)
    shifted = shifted.astype(jnp.bfloat16)
    stacked = jnp.concatenate(
        [shifted[:, index * patch_side:(index + 1) * patch_side] for index in range(len(pieces))],
        axis=0,
    )
    placed = jnp.dot(stacked, col_pick, preferred_element_type=jnp.float32)
    for layer in range(slice_count):
        for part in range(2):
            index = 2 * (2 * layer + part)
            band = (
                placed[index * band_rows:(index + 1) * band_rows]
                + placed[(index + 1) * band_rows:(index + 2) * band_rows]
            )
            window = total.at[layer, part, pl.ds(row_base, band_rows), pl.ds(col_base, band_cols)]
            window[...] = window[...] + band


def accumulate(terms, requests, peak, tile_cells):
    slot_count, slice_count = terms.shape[:2]
    patch_side = terms.shape[-1]
    held = math.gcd(slot_count, 8)
    grid_spec = pltpu.PrefetchScalarGridSpec(
        num_scalar_prefetch=1,
        grid=(slot_count // held,),
        in_specs=[
            pl.BlockSpec(memory_space=pltpu.SMEM),
            pl.BlockSpec(
                (held, slice_count, 2, patch_side, patch_side), lambda k, req: (k, 0, 0, 0, 0)
            ),
        ],
        out_specs=pl.BlockSpec(
            (slice_count, 2, tile_cells, tile_cells), lambda k, req: (0, 0, 0, 0)
        ),
        scratch_shapes=[
            pltpu.VMEM(
                (slice_count, 2, tile_cells + 8, tile_cells + patch_side), jnp.float32
            )
        ],
    )
    return pl.pallas_call(
        place_kernel,
        grid_spec=grid_spec,
        out_shape=jax.ShapeDtypeStruct((slice_count, 2, tile_cells, tile_cells), jnp.float32),
        compiler_params=pltpu.CompilerParams(dimension_semantics=("arbitrary",)),
    )(requests, peak.reshape(1, 1), terms)


def group_max(value):
    count = lax.axis_size("group")
    if count & (count - 1) == 0:
        step = 1
        while step < count:
            pairs = [(index, index ^ step) for index in range(count)]
            value = jnp.maximum(value, lax.ppermute(value, "group", pairs))
            step *= 2
        return value
    running = value
    pairs = [(index, (index + 1) % count) for index in range(count)]
    for _ in range(count - 1):
        value = lax.ppermute(value, "group", pairs)
        running = jnp.maximum(running, value)
    return running


def split_pair(value):
    high = value.astype(jnp.bfloat16)
    low = (value - high.astype(jnp.float32)).astype(jnp.bfloat16)
    return high, low


def stack_three(value, axis):
    high = value.astype(jnp.bfloat16)
    low = (value - high.astype(jnp.float32)).astype(jnp.bfloat16)
    return jnp.concatenate([high, low, high], axis=axis)


def fourier_2d(fields, right_mat, left_mat):
    side = fields[0][0].shape[0]
    count = len(fields)
    rows = jnp.concatenate([jnp.concatenate([re, im], axis=1) for re, im in fields], axis=0)
    mid = jnp.dot(stack_three(rows, 1), right_mat, preferred_element_type=jnp.float32)
    parted = jnp.concatenate(
        [
            jnp.concatenate([mid[m * side:(m + 1) * side, :side] for m in range(count)], axis=1),
            jnp.concatenate([mid[m * side:(m + 1) * side, side:] for m in range(count)], axis=1),
        ],
        axis=0,
    )
    out = jnp.dot(left_mat, stack_three(parted, 0), preferred_element_type=jnp.float32)
    return [
        (out[:side, m * side:(m + 1) * side], out[side:, m * side:(m + 1) * side])
        for m in range(count)
    ]


def propagate_kernel(patch_ref, measured_ref, probe_ref, kern_ref, mats_right, mats_left,
                     peak_ref, grad_ref, probe_sum_ref):
    @pl.when(pl.program_id(0) == 0)
    def _():
        probe_sum_ref[...] = jnp.zeros_like(probe_sum_ref)

    held = patch_ref.shape[0]
    together = held
    for first in range(0, held, together):
        propagate_group(list(range(first, first + together)), patch_ref, measured_ref, probe_ref,
                        kern_ref, mats_right, mats_left, grad_ref, probe_sum_ref)


def propagate_group(slots, patch_ref, measured_ref, probe_ref, kern_ref, mats_right, mats_left,
                    grad_ref, probe_sum_ref):
    slice_count = patch_ref.shape[1]
    modes = probe_ref.shape[0]
    forward = lambda fields: fourier_2d(fields, mats_right[0], mats_left[0])
    inverse = lambda fields: fourier_2d(fields, mats_right[1], mats_left[1])
    kern_real, kern_imag = kern_ref[0], kern_ref[1]
    owner = [j for j in range(len(slots)) for _ in range(modes)]
    waves = [(probe_ref[m, 0], probe_ref[m, 1]) for _ in slots for m in range(modes)]

    def patch(layer):
        return [
            (patch_ref[s, layer, 0].astype(jnp.float32), patch_ref[s, layer, 1].astype(jnp.float32))
            for s in slots
        ]

    history = []
    leaving = None
    for layer in range(slice_count):
        history.append(waves)
        cells = patch(layer)
        leaving = []
        for (wr, wi), j in zip(waves, owner):
            pr, pi = cells[j]
            leaving.append((wr * pr - wi * pi, wr * pi + wi * pr))
        if layer < slice_count - 1:
            spectra = forward(leaving)
            waves = inverse(
                [
                    (kern_real * fr - kern_imag * fi, kern_real * fi + kern_imag * fr)
                    for fr, fi in spectra
                ]
            )
    far = forward(leaving)
    scaled = []
    for j, s in enumerate(slots):
        intensity = None
        for m in range(modes):
            fr, fi = far[j * modes + m]
            power = fr * fr + fi * fi
            intensity = power if intensity is None else intensity + power
        factor = 1.0 - measured_ref[s] / jnp.sqrt(jnp.maximum(intensity, 1.0))
        for m in range(modes):
            fr, fi = far[j * modes + m]
            scaled.append((fr * factor, fi * factor))
    back = inverse(scaled)
    for layer in reversed(range(slice_count)):
        for j, s in enumerate(slots):
            grad_real = None
            grad_imag = None
            for m in range(modes):
                wr, wi = history[layer][j * modes + m]
                br, bi = back[j * modes + m]
                term_real = wr * br + wi * bi
                term_imag = wr * bi - wi * br
                grad_real = term_real if grad_real is None else grad_real + term_real
                grad_imag = term_imag if grad_imag is None else grad_imag + term_imag
            grad_ref[s, layer, 0] = grad_real
            grad_ref[s, layer, 1] = grad_imag
        cells = patch(layer)
        moved = []
        for (br, bi), j in zip(back, owner):
            pr, pi = cells[j]
            moved.append((pr * br + pi * bi, pr * bi - pi * br))
        back = moved
        if layer > 0:
            spectra = forward(back)
            back = inverse(
                [
                    (kern_real * fr + kern_imag * fi, kern_real * fi - kern_imag * fr)
                    for fr, fi in spectra
                ]
            )
    for j in range(len(slots)):
        for m in range(modes):
            br, bi = back[j * modes + m]
            probe_sum_ref[m, 0] = probe_sum_ref[m, 0] + br
            probe_sum_ref[m, 1] = probe_sum_ref[m, 1] + bi


def dft_mats(length):
    counter = jnp.arange(length, dtype=jnp.int32)
    product = counter[:, None] * counter[None, :] % length
    angles = product.astype(jnp.float32) * (2.0 * math.pi / length)
    norming = 1.0 / math.sqrt(length)
    cosine = jnp.cos(angles) * norming
    sine = jnp.sin(angles) * norming
    minus = jnp.concatenate(
        [jnp.concatenate([cosine, -sine], axis=1), jnp.concatenate([sine, cosine], axis=1)], axis=0
    )
    plus = jnp.concatenate(
        [jnp.concatenate([cosine, sine], axis=1), jnp.concatenate([-sine, cosine], axis=1)], axis=0
    )

    def parts(value):
        high = lax.reduce_precision(value, exponent_bits=8, mantissa_bits=7)
        return high.astype(jnp.bfloat16), (value - high).astype(jnp.bfloat16)

    def right(value):
        high, low = parts(value)
        return jnp.concatenate([high, high, low], axis=0)

    def left(value):
        high, low = parts(value)
        return jnp.concatenate([high, high, low], axis=1)

    mats_right = jnp.stack([right(minus), right(plus)])
    mats_left = jnp.stack([left(plus), left(minus)])
    return mats_right, mats_left


def propagate(patches, measured, probe_modes, prop_phase, peak):
    count, slice_count = patches.shape[:2]
    modes = probe_modes.shape[0]
    side = patches.shape[-1]
    kern = jnp.stack([jnp.cos(prop_phase), jnp.sin(prop_phase)])
    mats_right, mats_left = dft_mats(side)
    held = math.gcd(count, 8)
    whole = lambda shape: pl.BlockSpec(shape, lambda k: (0,) * len(shape))
    return pl.pallas_call(
        propagate_kernel,
        grid=(count // held,),
        in_specs=[
            pl.BlockSpec((held, slice_count, 2, side, side), lambda k: (k, 0, 0, 0, 0)),
            pl.BlockSpec((held, side, side), lambda k: (k, 0, 0)),
            whole((modes, 2, side, side)),
            whole((2, side, side)),
            whole((2, 6 * side, 2 * side)),
            whole((2, 2 * side, 6 * side)),
            pl.BlockSpec(memory_space=pltpu.SMEM),
        ],
        out_specs=[
            pl.BlockSpec((held, slice_count, 2, side, side), lambda k: (k, 0, 0, 0, 0)),
            whole((modes, 2, side, side)),
        ],
        out_shape=[
            jax.ShapeDtypeStruct((count, slice_count, 2, side, side), jnp.float32),
            jax.ShapeDtypeStruct((modes, 2, side, side), jnp.float32),
        ],
        compiler_params=pltpu.CompilerParams(dimension_semantics=("arbitrary",)),
    )(patches, measured, probe_modes, kern, mats_right, mats_left, peak.reshape(1, 1))


def member_sum(value, members):
    flat = value.reshape(members, -1)
    pieces = lax.all_to_all(flat, "member", split_axis=0, concat_axis=0, tiled=True)
    mine = jnp.sum(pieces, axis=0, keepdims=True)
    spread = jnp.broadcast_to(mine, flat.shape)
    whole = lax.all_to_all(spread, "member", split_axis=0, concat_axis=0, tiled=True)
    return whole.reshape(value.shape)


def on_device(object_field, probe_modes, prop_phase, amplitude, tile_owner, corner):
    members = lax.axis_size("member")
    pos_dev = tile_owner.shape[1]
    capacity = max(2, (2 * pos_dev + members - 1) // members)
    slot_count = members * capacity
    tile_cells = object_field.shape[2]
    patch_side = prop_phase.shape[0]
    power = jnp.max(jnp.sum(probe_modes * probe_modes, axis=(1, 2)))
    peak_power = group_max(power) + 1e-06
    flat_slots = slot_numbers(tile_owner[0, :, 0], members, capacity)
    entries = jnp.concatenate([jnp.ones((pos_dev, 1), jnp.int32), corner[0]], axis=1)
    chosen = (flat_slots[:, None] == jnp.arange(slot_count, dtype=jnp.int32)[None, :]).astype(
        jnp.int32
    )
    outgoing = jnp.sum(chosen[:, :, None] * entries[:, None, :], axis=0)
    requests = lax.all_to_all(
        outgoing.reshape(members, capacity, 3), "member", split_axis=0, concat_axis=0, tiled=True
    ).reshape(slot_count, 3)
    sent = jnp.zeros((slot_count, patch_side, patch_side), jnp.float32).at[flat_slots].set(
        amplitude[0]
    )
    measured = lax.all_to_all(
        sent.reshape(members, capacity, patch_side, patch_side),
        "member",
        split_axis=0,
        concat_axis=0,
        tiled=True,
    ).reshape(slot_count, patch_side, patch_side)
    patches = cut_windows(object_field, requests, patch_side)
    gradients, adjoint_sum = propagate(patches, measured, probe_modes[0], prop_phase, peak_power)
    probe_grad = member_sum(adjoint_sum / pos_dev, members)[None]
    object_grad = accumulate(gradients, requests, peak_power, tile_cells)
    return (object_grad, probe_grad)


def solution(mesh):
    return jax.shard_map(
        on_device,
        mesh=mesh,
        in_specs=(
            P(None, None, "group", "member"),
            P("group", None, None, None, None),
            P(),
            P("group", "member", None, None),
            P("group", "member", None),
            P("group", "member", None),
        ),
        out_specs=(P(None, None, "group", "member"), P("group", None, None, None, None)),
        check_vma=False,
    )
```

```python
from functools import partial
import math

import jax
import jax.numpy as jnp
from jax import lax
from jax.experimental import pallas as pl
from jax.experimental.pallas import tpu as pltpu
from jax.sharding import PartitionSpec as P

DFT_PRECISION = lax.Precision.HIGH


def fourier_blocks(length, sign):
    counter = jnp.arange(length, dtype=jnp.int32)
    product = counter[:, None] * counter[None, :] % length
    angles = product.astype(jnp.float32) * (2.0 * math.pi / length)
    norming = 1.0 / math.sqrt(length)
    cosine = jnp.cos(angles) * norming
    sine_part = jnp.sin(angles) * (sign * norming)
    return jnp.stack([jnp.stack([cosine, sine_part]), jnp.stack([-sine_part, cosine])])


def transform(field, blocks):
    across = jnp.einsum("...chn,cdnk->...dhk", field, blocks, precision=DFT_PRECISION)
    return jnp.einsum("cdkn,...cnw->...dkw", blocks, across, precision=DFT_PRECISION)


def complex_times(left, right):
    left_re, left_im = (left[..., 0, :, :], left[..., 1, :, :])
    right_re, right_im = (right[..., 0, :, :], right[..., 1, :, :])
    return jnp.stack(
        [left_re * right_re - left_im * right_im, left_re * right_im + left_im * right_re], axis=-3
    )


def conj_times(left, right):
    left_re, left_im = (left[..., 0, :, :], left[..., 1, :, :])
    right_re, right_im = (right[..., 0, :, :], right[..., 1, :, :])
    return jnp.stack(
        [left_re * right_re + left_im * right_im, left_re * right_im - left_im * right_re], axis=-3
    )


def slot_numbers(targets, members, capacity):
    matches = (targets[:, None] == jnp.arange(members, dtype=jnp.int32)[None, :]).astype(jnp.int32)
    before = jnp.cumsum(matches, axis=0) - matches
    return targets * capacity + jnp.sum(before * matches, axis=1)


def selectors(offsets, patch_side, tile_cells, dtype):
    inner = jnp.arange(patch_side, dtype=jnp.int32)
    cells = jnp.arange(tile_cells, dtype=jnp.int32)
    hit = offsets[:, None, None] + inner[None, :, None] == cells[None, None, :]
    return hit.astype(dtype)


def cut_windows(tiles, requests, patch_side):
    tile_cells = tiles.shape[-1]
    valid = requests[:, 0].astype(jnp.bfloat16)
    row_sel = selectors(requests[:, 1], patch_side, tile_cells, jnp.bfloat16) * valid[:, None, None]
    col_sel = selectors(requests[:, 2], patch_side, tile_cells, jnp.bfloat16)
    rows = jnp.einsum("kit,sctu->kscui", row_sel, tiles, preferred_element_type=jnp.float32)
    rows = rows.astype(jnp.bfloat16)
    window = jnp.einsum("kscui,kju->kscij", rows, col_sel, preferred_element_type=jnp.float32)
    return window.astype(jnp.bfloat16)


def place_kernel(requests, peak, terms, out, total):
    step = pl.program_id(0)
    held = terms.shape[0]
    tile_cells = out.shape[-1]

    @pl.when(step == 0)
    def _():
        total[...] = jnp.zeros_like(total)

    for index in range(held):
        place_one(step * held + index, index, requests, terms, total)

    @pl.when(step == pl.num_programs(0) - 1)
    def _():
        out[...] = total[:, :, :tile_cells, :tile_cells] / peak[0, 0]


def place_one(slot, index, requests, terms, total):
    slice_count = terms.shape[1]
    patch_side = terms.shape[-1]
    row = requests[slot, 1]
    col = requests[slot, 2]
    row_base = pl.multiple_of((row // 8) * 8, 8)
    col_base = pl.multiple_of((col // 128) * 128, 128)
    row_rest = row - row_base
    col_rest = col - col_base
    band_rows = patch_side + 8
    band_cols = 2 * patch_side
    row_pick = (
        lax.broadcasted_iota(jnp.int32, (band_rows, patch_side), 0)
        == lax.broadcasted_iota(jnp.int32, (band_rows, patch_side), 1) + row_rest
    ).astype(jnp.bfloat16)
    col_pick = (
        lax.broadcasted_iota(jnp.int32, (patch_side, band_cols), 1)
        == lax.broadcasted_iota(jnp.int32, (patch_side, band_cols), 0) + col_rest
    ).astype(jnp.bfloat16)
    pieces = []
    for layer in range(slice_count):
        for part in range(2):
            term = terms[index, layer, part]
            high = term.astype(jnp.bfloat16)
            low = (term - high.astype(jnp.float32)).astype(jnp.bfloat16)
            pieces += [high, low]
    side_by_side = jnp.concatenate(pieces, axis=1)
    shifted = jnp.dot(row_pick, side_by_side, preferred_element_type=jnp.float32)
    shifted = shifted.astype(jnp.bfloat16)
    stacked = jnp.concatenate(
        [shifted[:, index * patch_side:(index + 1) * patch_side] for index in range(len(pieces))],
        axis=0,
    )
    placed = jnp.dot(stacked, col_pick, preferred_element_type=jnp.float32)
    for layer in range(slice_count):
        for part in range(2):
            index = 2 * (2 * layer + part)
            band = (
                placed[index * band_rows:(index + 1) * band_rows]
                + placed[(index + 1) * band_rows:(index + 2) * band_rows]
            )
            window = total.at[layer, part, pl.ds(row_base, band_rows), pl.ds(col_base, band_cols)]
            window[...] = window[...] + band


def accumulate(terms, requests, peak, tile_cells):
    slot_count, slice_count = terms.shape[:2]
    patch_side = terms.shape[-1]
    held = math.gcd(slot_count, 16)
    grid_spec = pltpu.PrefetchScalarGridSpec(
        num_scalar_prefetch=1,
        grid=(slot_count // held,),
        in_specs=[
            pl.BlockSpec(memory_space=pltpu.SMEM),
            pl.BlockSpec(
                (held, slice_count, 2, patch_side, patch_side), lambda k, req: (k, 0, 0, 0, 0)
            ),
        ],
        out_specs=pl.BlockSpec(
            (slice_count, 2, tile_cells, tile_cells), lambda k, req: (0, 0, 0, 0)
        ),
        scratch_shapes=[
            pltpu.VMEM(
                (slice_count, 2, tile_cells + 8, tile_cells + patch_side), jnp.float32
            )
        ],
    )
    return pl.pallas_call(
        place_kernel,
        grid_spec=grid_spec,
        out_shape=jax.ShapeDtypeStruct((slice_count, 2, tile_cells, tile_cells), jnp.float32),
        compiler_params=pltpu.CompilerParams(dimension_semantics=("arbitrary",)),
    )(requests, peak.reshape(1, 1), terms)


def group_max(value):
    count = lax.axis_size("group")
    if count & (count - 1) == 0:
        step = 1
        while step < count:
            pairs = [(index, index ^ step) for index in range(count)]
            value = jnp.maximum(value, lax.ppermute(value, "group", pairs))
            step *= 2
        return value
    running = value
    pairs = [(index, (index + 1) % count) for index in range(count)]
    for _ in range(count - 1):
        value = lax.ppermute(value, "group", pairs)
        running = jnp.maximum(running, value)
    return running


def split_pair(value):
    high = value.astype(jnp.bfloat16)
    low = (value - high.astype(jnp.float32)).astype(jnp.bfloat16)
    return high, low


def stack_three(value, axis):
    high = value.astype(jnp.bfloat16)
    low = (value - high.astype(jnp.float32)).astype(jnp.bfloat16)
    return jnp.concatenate([high, low, high], axis=axis)


def fourier_2d(fields, right_mat, left_mat):
    side = fields[0][0].shape[0]
    count = len(fields)
    rows = jnp.concatenate([jnp.concatenate([re, im], axis=1) for re, im in fields], axis=0)
    mid = jnp.dot(stack_three(rows, 1), right_mat, preferred_element_type=jnp.float32)
    parted = jnp.concatenate(
        [
            jnp.concatenate([mid[m * side:(m + 1) * side, :side] for m in range(count)], axis=1),
            jnp.concatenate([mid[m * side:(m + 1) * side, side:] for m in range(count)], axis=1),
        ],
        axis=0,
    )
    out = jnp.dot(left_mat, stack_three(parted, 0), preferred_element_type=jnp.float32)
    return [
        (out[:side, m * side:(m + 1) * side], out[side:, m * side:(m + 1) * side])
        for m in range(count)
    ]


def propagate_kernel(patch_ref, measured_ref, probe_ref, kern_ref, mats_right, mats_left,
                     peak_ref, grad_ref, probe_sum_ref):
    @pl.when(pl.program_id(0) == 0)
    def _():
        probe_sum_ref[...] = jnp.zeros_like(probe_sum_ref)

    held = patch_ref.shape[0]
    together = held
    for first in range(0, held, together):
        propagate_group(list(range(first, first + together)), patch_ref, measured_ref, probe_ref,
                        kern_ref, mats_right, mats_left, grad_ref, probe_sum_ref)


def propagate_group(slots, patch_ref, measured_ref, probe_ref, kern_ref, mats_right, mats_left,
                    grad_ref, probe_sum_ref):
    slice_count = patch_ref.shape[1]
    modes = probe_ref.shape[0]
    forward = lambda fields: fourier_2d(fields, mats_right[0], mats_left[0])
    inverse = lambda fields: fourier_2d(fields, mats_right[1], mats_left[1])
    kern_real, kern_imag = kern_ref[0], kern_ref[1]
    owner = [j for j in range(len(slots)) for _ in range(modes)]
    waves = [(probe_ref[m, 0], probe_ref[m, 1]) for _ in slots for m in range(modes)]

    def patch(layer):
        return [
            (patch_ref[s, layer, 0].astype(jnp.float32), patch_ref[s, layer, 1].astype(jnp.float32))
            for s in slots
        ]

    history = []
    leaving = None
    for layer in range(slice_count):
        history.append(waves)
        cells = patch(layer)
        leaving = []
        for (wr, wi), j in zip(waves, owner):
            pr, pi = cells[j]
            leaving.append((wr * pr - wi * pi, wr * pi + wi * pr))
        if layer < slice_count - 1:
            spectra = forward(leaving)
            waves = inverse(
                [
                    (kern_real * fr - kern_imag * fi, kern_real * fi + kern_imag * fr)
                    for fr, fi in spectra
                ]
            )
    far = forward(leaving)
    scaled = []
    for j, s in enumerate(slots):
        intensity = None
        for m in range(modes):
            fr, fi = far[j * modes + m]
            power = fr * fr + fi * fi
            intensity = power if intensity is None else intensity + power
        factor = 1.0 - measured_ref[s] / jnp.sqrt(jnp.maximum(intensity, 1.0))
        for m in range(modes):
            fr, fi = far[j * modes + m]
            scaled.append((fr * factor, fi * factor))
    back = inverse(scaled)
    for layer in reversed(range(slice_count)):
        for j, s in enumerate(slots):
            grad_real = None
            grad_imag = None
            for m in range(modes):
                wr, wi = history[layer][j * modes + m]
                br, bi = back[j * modes + m]
                term_real = wr * br + wi * bi
                term_imag = wr * bi - wi * br
                grad_real = term_real if grad_real is None else grad_real + term_real
                grad_imag = term_imag if grad_imag is None else grad_imag + term_imag
            grad_ref[s, layer, 0] = grad_real
            grad_ref[s, layer, 1] = grad_imag
        cells = patch(layer)
        moved = []
        for (br, bi), j in zip(back, owner):
            pr, pi = cells[j]
            moved.append((pr * br + pi * bi, pr * bi - pi * br))
        back = moved
        if layer > 0:
            spectra = forward(back)
            back = inverse(
                [
                    (kern_real * fr + kern_imag * fi, kern_real * fi - kern_imag * fr)
                    for fr, fi in spectra
                ]
            )
    for j in range(len(slots)):
        for m in range(modes):
            br, bi = back[j * modes + m]
            probe_sum_ref[m, 0] = probe_sum_ref[m, 0] + br
            probe_sum_ref[m, 1] = probe_sum_ref[m, 1] + bi


def dft_mats(length):
    counter = jnp.arange(length, dtype=jnp.int32)
    product = counter[:, None] * counter[None, :] % length
    angles = product.astype(jnp.float32) * (2.0 * math.pi / length)
    norming = 1.0 / math.sqrt(length)
    cosine = jnp.cos(angles) * norming
    sine = jnp.sin(angles) * norming
    minus = jnp.concatenate(
        [jnp.concatenate([cosine, -sine], axis=1), jnp.concatenate([sine, cosine], axis=1)], axis=0
    )
    plus = jnp.concatenate(
        [jnp.concatenate([cosine, sine], axis=1), jnp.concatenate([-sine, cosine], axis=1)], axis=0
    )

    def parts(value):
        high = lax.reduce_precision(value, exponent_bits=8, mantissa_bits=7)
        return high.astype(jnp.bfloat16), (value - high).astype(jnp.bfloat16)

    def right(value):
        high, low = parts(value)
        return jnp.concatenate([high, high, low], axis=0)

    def left(value):
        high, low = parts(value)
        return jnp.concatenate([high, high, low], axis=1)

    mats_right = jnp.stack([right(minus), right(plus)])
    mats_left = jnp.stack([left(plus), left(minus)])
    return mats_right, mats_left


def propagate(patches, measured, probe_modes, prop_phase, peak):
    count, slice_count = patches.shape[:2]
    modes = probe_modes.shape[0]
    side = patches.shape[-1]
    kern = jnp.stack([jnp.cos(prop_phase), jnp.sin(prop_phase)])
    mats_right, mats_left = dft_mats(side)
    held = math.gcd(count, 8)
    whole = lambda shape: pl.BlockSpec(shape, lambda k: (0,) * len(shape))
    return pl.pallas_call(
        propagate_kernel,
        grid=(count // held,),
        in_specs=[
            pl.BlockSpec((held, slice_count, 2, side, side), lambda k: (k, 0, 0, 0, 0)),
            pl.BlockSpec((held, side, side), lambda k: (k, 0, 0)),
            whole((modes, 2, side, side)),
            whole((2, side, side)),
            whole((2, 6 * side, 2 * side)),
            whole((2, 2 * side, 6 * side)),
            pl.BlockSpec(memory_space=pltpu.SMEM),
        ],
        out_specs=[
            pl.BlockSpec((held, slice_count, 2, side, side), lambda k: (k, 0, 0, 0, 0)),
            whole((modes, 2, side, side)),
        ],
        out_shape=[
            jax.ShapeDtypeStruct((count, slice_count, 2, side, side), jnp.float32),
            jax.ShapeDtypeStruct((modes, 2, side, side), jnp.float32),
        ],
        compiler_params=pltpu.CompilerParams(dimension_semantics=("arbitrary",)),
    )(patches, measured, probe_modes, kern, mats_right, mats_left, peak.reshape(1, 1))


def member_sum(value, members):
    flat = value.reshape(members, -1)
    pieces = lax.all_to_all(flat, "member", split_axis=0, concat_axis=0, tiled=True)
    mine = jnp.sum(pieces, axis=0, keepdims=True)
    spread = jnp.broadcast_to(mine, flat.shape)
    whole = lax.all_to_all(spread, "member", split_axis=0, concat_axis=0, tiled=True)
    return whole.reshape(value.shape)


def on_device(object_field, probe_modes, prop_phase, amplitude, tile_owner, corner):
    members = lax.axis_size("member")
    pos_dev = tile_owner.shape[1]
    capacity = max(2, (2 * pos_dev + members - 1) // members)
    slot_count = members * capacity
    tile_cells = object_field.shape[2]
    patch_side = prop_phase.shape[0]
    power = jnp.max(jnp.sum(probe_modes * probe_modes, axis=(1, 2)))
    peak_power = group_max(power) + 1e-06
    flat_slots = slot_numbers(tile_owner[0, :, 0], members, capacity)
    entries = jnp.concatenate([jnp.ones((pos_dev, 1), jnp.int32), corner[0]], axis=1)
    chosen = (flat_slots[:, None] == jnp.arange(slot_count, dtype=jnp.int32)[None, :]).astype(
        jnp.int32
    )
    outgoing = jnp.sum(chosen[:, :, None] * entries[:, None, :], axis=0)
    requests = lax.all_to_all(
        outgoing.reshape(members, capacity, 3), "member", split_axis=0, concat_axis=0, tiled=True
    ).reshape(slot_count, 3)
    sent = jnp.zeros((slot_count, patch_side, patch_side), jnp.float32).at[flat_slots].set(
        amplitude[0]
    )
    measured = lax.all_to_all(
        sent.reshape(members, capacity, patch_side, patch_side),
        "member",
        split_axis=0,
        concat_axis=0,
        tiled=True,
    ).reshape(slot_count, patch_side, patch_side)
    patches = cut_windows(object_field, requests, patch_side)
    gradients, adjoint_sum = propagate(patches, measured, probe_modes[0], prop_phase, peak_power)
    probe_grad = member_sum(adjoint_sum / pos_dev, members)[None]
    object_grad = accumulate(gradients, requests, peak_power, tile_cells)
    return (object_grad, probe_grad)


def solution(mesh):
    return jax.shard_map(
        on_device,
        mesh=mesh,
        in_specs=(
            P(None, None, "group", "member"),
            P("group", None, None, None, None),
            P(),
            P("group", "member", None, None),
            P("group", "member", None),
            P("group", "member", None),
        ),
        out_specs=(P(None, None, "group", "member"), P("group", None, None, None, None)),
        check_vma=False,
    )
```
